32 devices in a mesh: seq: 8 (over y, x, core), head: 4 (over z).
Axes of the slice: x: 2, y: 2, z: 4, core: 2. Of those that a mesh axis runs over, the one named last changes fastest.
Arguments:
- queries: bfloat16 [2048, 4096], P('seq', 'head'), may hold values from -24 to 24
- keys: bfloat16 [2048, 4096], P('seq', 'head'), may hold values from -24 to 24
- values: bfloat16 [2048, 4096], P('seq', 'head'), may hold values from -6 to 6
- out_weight: bfloat16 [4096, 4096], P('head'), may hold values from -0.75 to 0.75
- global_blocks: int32 [2], replicated, may hold values from 0 to 31, as said below
- random_blocks: int32 [32, 3], replicated, may hold values from 0 to 31, as said below
- window_blocks: int32 [32], P('head'), may hold values from 1 to 2, as said below
- yarn_scale: int32 [1], replicated, may hold values from 2 to 64
- yarn_context: int32 [1], replicated, may hold values from 1024 to 4096
Outputs:
- mixed: bfloat16 [2048, 4096], P('seq', 'head')
The draws below stay inside these ranges and needn't reach their ends.
Inputs may be any that keep to these rules, and one draw needn't show every extreme that they name: `global_blocks`: 2 different block numbers. `random_blocks`: of the 12 random blocks named by the query blocks of one index of seq, at most 2 lie among the blocks of any one index of seq, and some index of seq holds exactly 2 of them. `window_blocks`: some head has reach 2.
All inputs are finite; a program needn't handle non-finite values.
Results may differ from the reference program's by a relative error of at most 0.013.
Values may be sent and summed in bfloat16 or wider, within the bound.
No kernel may reach another device: no remote copies, remote signals or barrier semaphores. Data moves between devices by JAX's collectives and lax.ppermute only.
A program may use at most 128 MiB of HBM per device.

```python
import math
import jax
import jax.numpy as jnp
from jax import lax

D = 4096
HEADS = 32
HEAD_DIM = 128
BLOCK = 64
GLOB = 2
RAND = 3
WMAX = 2
NT = 2048
NB = 32
BLK_DEV = 4


def draw_queries(key, part):
    noise_key = jax.random.fold_in(key, 11)
    grid_shape = (NT // BLOCK, BLOCK, HEADS, HEAD_DIM)
    noise = jax.random.truncated_normal(noise_key, -4.0, 4.0, grid_shape, jnp.float32)
    return noise.reshape(NT, HEADS * HEAD_DIM).astype(jnp.bfloat16)


def draw_keys(key, part):
    noise_key = jax.random.fold_in(key, 13)
    grid_shape = (NT // BLOCK, BLOCK, HEADS, HEAD_DIM)
    noise = jax.random.truncated_normal(noise_key, -4.0, 4.0, grid_shape, jnp.float32)
    return noise.reshape(NT, HEADS * HEAD_DIM).astype(jnp.bfloat16)


def draw_values(key, part):
    noise_key, mean_key, level_key = jax.random.split(jax.random.fold_in(key, 17), 3)
    block_count = NT // BLOCK
    grid_shape = (block_count, BLOCK, HEADS * HEAD_DIM)
    region = jnp.arange(block_count) * 8 // block_count
    high_region = jax.random.permutation(level_key, 8) < 4
    region_level = jnp.where(high_region, 1.8, 0.2).astype(jnp.float32)[region]
    noise = jax.random.truncated_normal(noise_key, -4.0, 4.0, grid_shape, jnp.float32)
    column_mean = 0.3 * jax.random.truncated_normal(mean_key, -3.0, 3.0, (HEADS * HEAD_DIM,), jnp.float32)
    field = noise + region_level[:, None, None] * column_mean[None, None, :]
    return field.reshape(NT, HEADS * HEAD_DIM).astype(jnp.bfloat16)


def draw_global_blocks(key, part):
    return jax.random.permutation(jax.random.fold_in(key, 21), NT // BLOCK)[:GLOB].astype(jnp.int32)


def draw_random_blocks(key, part):
    block_count = NT // BLOCK
    device_count = block_count // BLK_DEV
    slot_total = BLK_DEV * RAND
    order_key, shift_key, local_key = jax.random.split(jax.random.fold_in(key, 31), 3)
    orders = jax.vmap(lambda single: jax.random.permutation(single, slot_total))(jax.random.split(order_key, device_count))
    shifts = jax.random.randint(shift_key, (device_count, 1), 0, device_count)
    owners = (orders + shifts) % device_count
    local_pick = jax.random.randint(local_key, (device_count, slot_total), 0, BLK_DEV)
    return (owners * BLK_DEV + local_pick).reshape(block_count, RAND).astype(jnp.int32)


def draw_window_blocks(key, part):
    width_key, head_key = jax.random.split(jax.random.fold_in(key, 41))
    widths = jax.random.randint(width_key, (HEADS,), 1, WMAX + 1)
    chosen = jax.random.randint(head_key, (), 0, HEADS)
    return jnp.where(jnp.arange(HEADS) == chosen, WMAX, widths).astype(jnp.int32)


def steps_of(rng, shape, cuts, least, high):
    def one(dim, shards_of):
        heights = jax.random.uniform(jax.random.fold_in(jax.random.fold_in(rng, 6), dim), (shards_of,), jnp.float32, least / len(cuts), high / len(cuts))
        return jnp.repeat(jnp.exp(heights), shape[dim] // shards_of).reshape((-1,) + (1,) * (len(shape) - dim - 1))

    level = one(*cuts[0])
    for cut in cuts[1:]:
        level = level * one(*cut)
    return level


def gaussian(rng, extent, spread, most, pieces=(), kind=jnp.bfloat16):
    entries = jax.random.normal(rng, extent, jnp.float32) * spread
    if len(pieces) > 0:
        entries = steps_of(rng, extent, pieces, -0.22, 0.18) * entries
    return jnp.clip(entries, min=-most, max=most).astype(kind)


def setup_inputs(seed: int = 0) -> dict:
    arg_keys = jax.random.split(jax.random.key(seed), 10)
    return {
        "queries": draw_queries(jax.random.fold_in(arg_keys[9], 71), 0),
        "keys": draw_keys(jax.random.fold_in(arg_keys[9], 71), 0),
        "values": draw_values(jax.random.fold_in(arg_keys[9], 71), 0),
        "out_weight": gaussian(arg_keys[3], (HEADS * HEAD_DIM, D), (HEADS * HEAD_DIM // 64) ** -0.5, 0.75, ((0, 4),)),
        "global_blocks": draw_global_blocks(jax.random.fold_in(arg_keys[9], 71), 0),
        "random_blocks": draw_random_blocks(jax.random.fold_in(arg_keys[9], 71), 0),
        "window_blocks": draw_window_blocks(jax.random.fold_in(arg_keys[9], 71), 0),
        "yarn_scale": jax.random.randint(arg_keys[7], (1,), 2, 65).astype(jnp.int32),
        "yarn_context": jax.random.randint(arg_keys[8], (1,), 1024, 4097).astype(jnp.int32),
    }


masked_score = -1e+30

def yarn_tables(yarn_scale, yarn_context):
    half_dim = HEAD_DIM // 2
    pair_index = jnp.arange(half_dim).astype(jnp.float32)
    base_rate = 10000.0 ** (-2.0 * pair_index / HEAD_DIM)
    factor = yarn_scale[0].astype(jnp.float32)
    context = yarn_context[0].astype(jnp.float32)
    turn_ratio = context * base_rate / (2.0 * math.pi)
    ramp_weight = jnp.clip((turn_ratio - 1.0) / 31.0, 0.0, 1.0)
    frequency = base_rate * ((1.0 - ramp_weight) / factor + ramp_weight)
    mscale = 0.1 * jnp.log(factor) + 1.0
    return (frequency, mscale)

def rotate(source, first_row, frequency, mscale):
    row_count, row_width = source.shape
    half_dim = HEAD_DIM // 2
    position = (first_row + jnp.arange(row_count)).astype(jnp.float32)
    angle_table = position[:, None] * frequency[None, :]
    cosine = jnp.cos(angle_table)[:, None, :] * mscale
    sine_part = jnp.sin(angle_table)[:, None, :] * mscale
    halves_view = source.astype(jnp.float32).reshape(row_count, row_width // HEAD_DIM, 2, half_dim)
    lower_half = halves_view[:, :, 0]
    upper_half = halves_view[:, :, 1]
    turned = jnp.stack([lower_half * cosine - upper_half * sine_part, upper_half * cosine + lower_half * sine_part], axis=2)
    return turned.reshape(row_count, row_width).astype(jnp.bfloat16)

def block_attend(query_blocks, key_blocks, value_blocks, valid_slots):
    count_q, slot_count = (key_blocks.shape[0], key_blocks.shape[1])
    heads_here = query_blocks.shape[-1] // HEAD_DIM
    query_grid = query_blocks.reshape(count_q, BLOCK, heads_here, HEAD_DIM).astype(jnp.float32)
    key_grid = key_blocks.reshape(count_q, slot_count * BLOCK, heads_here, HEAD_DIM).astype(jnp.float32)
    value_grid = value_blocks.reshape(count_q, slot_count * BLOCK, heads_here, HEAD_DIM).astype(jnp.float32)
    scores = jnp.einsum('bqhd,bshd->bhqs', query_grid, key_grid) * (1.0 / math.sqrt(HEAD_DIM))
    present = jnp.repeat(jnp.transpose(valid_slots, (0, 2, 1)), BLOCK, axis=2)[:, :, None, :]
    scores = jnp.where(present, scores, masked_score)
    peak = lax.optimization_barrier(jnp.max(scores, axis=3, keepdims=True))
    expo = jnp.exp(scores - peak)
    total = lax.optimization_barrier(jnp.sum(expo, axis=3))
    weights = expo.astype(jnp.bfloat16).astype(jnp.float32)
    mixture = jnp.einsum('bhqs,bshd->bqhd', weights, value_grid)
    mixture = mixture / jnp.transpose(total, (0, 2, 1))[..., None]
    return mixture.reshape(count_q, BLOCK, heads_here * HEAD_DIM)

def reference(queries, keys, values, out_weight, global_blocks, random_blocks, window_blocks, yarn_scale, yarn_context):
    frequency, mscale = yarn_tables(yarn_scale, yarn_context)
    query_rot = rotate(queries, 0, frequency, mscale)
    key_rot = rotate(keys, 0, frequency, mscale)
    full_width = HEADS * HEAD_DIM
    query_view = query_rot.reshape(NB, BLOCK, full_width)
    key_view = key_rot.reshape(NB, BLOCK, full_width)
    value_view = values.reshape(NB, BLOCK, full_width)
    offsets = jnp.arange(-WMAX, WMAX + 1)
    block_ids = jnp.arange(NB)
    window_ids = block_ids[:, None] + offsets[None, :]
    inside = (window_ids >= 0) & (window_ids < NB)
    reach = jnp.abs(offsets)[None, :, None] <= window_blocks[None, None, :]
    window_valid = inside[:, :, None] & reach
    all_ids = jnp.concatenate([jnp.clip(window_ids, 0, NB - 1).astype(jnp.int32), jnp.broadcast_to(global_blocks[None, :], (NB, GLOB)).astype(jnp.int32), random_blocks.astype(jnp.int32)], axis=1)
    all_valid = jnp.concatenate([window_valid, jnp.ones((NB, GLOB + RAND, HEADS), dtype=bool)], axis=1)

    def one_block(items):
        block_index, slot_ids, slot_valid = items
        return block_attend(query_view[block_index][None], key_view[slot_ids][None], value_view[slot_ids][None], slot_valid[None])[0]
    attended = lax.map(one_block, (block_ids, all_ids, all_valid)).astype(jnp.bfloat16)
    head_keys = key_rot.reshape(NT, HEADS, HEAD_DIM).transpose(1, 0, 2)
    head_values = values.reshape(NT, HEADS, HEAD_DIM).transpose(1, 0, 2)

    def one_head(items):
        query_head, key_head, value_head = items
        scores = jnp.dot(query_head, key_head.T, preferred_element_type=jnp.float32) * (1.0 / math.sqrt(HEAD_DIM))
        peak = lax.optimization_barrier(jnp.max(scores, axis=1, keepdims=True))
        expo = jnp.exp(scores - peak)
        total = lax.optimization_barrier(jnp.sum(expo, axis=1))
        mixture = jnp.dot(expo.astype(jnp.bfloat16), value_head, preferred_element_type=jnp.float32)
        return mixture / total[:, None]
    zero_index = jnp.zeros((), jnp.int32)
    for global_slot in range(GLOB):
        global_id = global_blocks[global_slot].astype(jnp.int32)
        query_rows = lax.dynamic_slice_in_dim(query_rot, global_id * BLOCK, BLOCK, 0)
        query_heads = query_rows.reshape(BLOCK, HEADS, HEAD_DIM).transpose(1, 0, 2)
        dense = lax.map(one_head, (query_heads, head_keys, head_values))
        dense_block = dense.transpose(1, 0, 2).reshape(BLOCK, full_width).astype(jnp.bfloat16)
        attended = lax.dynamic_update_slice(attended, dense_block[None], (global_id, zero_index, zero_index))
    attention_out = attended.reshape(NT, full_width)
    return jnp.dot(attention_out, out_weight, preferred_element_type=jnp.float32).astype(jnp.bfloat16)
```

```python
import math

import jax
import jax.numpy as jnp
from jax import lax
from jax.sharding import PartitionSpec as P

HEAD_DIM = 128
BLOCK = 64
GLOB = 2
RAND = 3
WMAX = 2


masked_score = -1e30


def padded_2(cells, sides, width):
    for axis, dim in sides:
        count = lax.axis_size(axis)
        ends = count - 1
        head = lax.slice_in_dim(cells, 0, width, axis=dim)
        tail = lax.slice_in_dim(cells, cells.shape[dim] - width, cells.shape[dim], axis=dim)
        cells = jnp.concatenate(
            [
                lax.ppermute(tail, axis, [(i, (i + 1) % count) for i in range(ends)]),
                cells,
                lax.ppermute(head, axis, [((i + 1) % count, i) for i in range(ends)]),
            ],
            axis=dim,
        )
    return cells


def yarn_tables(yarn_scale, yarn_context):
    half_dim = HEAD_DIM // 2
    pair_index = jnp.arange(half_dim).astype(jnp.float32)
    base_rate = 10000.0 ** (-2.0 * pair_index / HEAD_DIM)
    factor = yarn_scale[0].astype(jnp.float32)
    context = yarn_context[0].astype(jnp.float32)
    turn_ratio = context * base_rate / (2.0 * math.pi)
    ramp_weight = jnp.clip((turn_ratio - 1.0) / 31.0, 0.0, 1.0)
    frequency = base_rate * ((1.0 - ramp_weight) / factor + ramp_weight)
    mscale = 0.1 * jnp.log(factor) + 1.0
    return (frequency, mscale)


def rotate(source, first_row, frequency, mscale):
    row_count, row_width = source.shape
    half_dim = HEAD_DIM // 2
    position = (first_row + jnp.arange(row_count)).astype(jnp.float32)
    angle_table = position[:, None] * frequency[None, :]
    cosine = jnp.cos(angle_table)[:, None, :] * mscale
    sine_part = jnp.sin(angle_table)[:, None, :] * mscale
    halves_view = source.astype(jnp.float32).reshape(row_count, row_width // HEAD_DIM, 2, half_dim)
    lower_half = halves_view[:, :, 0]
    upper_half = halves_view[:, :, 1]
    turned = jnp.stack(
        [
            lower_half * cosine - upper_half * sine_part,
            upper_half * cosine + lower_half * sine_part,
        ],
        axis=2,
    )
    return turned.reshape(row_count, row_width).astype(jnp.bfloat16)


def block_attend(query_blocks, key_blocks, value_blocks, valid_slots):
    count_q, slot_count = (key_blocks.shape[0], key_blocks.shape[1])
    heads_here = query_blocks.shape[-1] // HEAD_DIM
    query_grid = query_blocks.reshape(count_q, BLOCK, heads_here, HEAD_DIM)
    key_grid = key_blocks.reshape(count_q, slot_count * BLOCK, heads_here, HEAD_DIM)
    value_grid = value_blocks.reshape(count_q, slot_count * BLOCK, heads_here, HEAD_DIM)
    scores = jnp.einsum(
        "bqhd,bshd->bhqs", query_grid, key_grid, preferred_element_type=jnp.float32
    ) * (1.0 / math.sqrt(HEAD_DIM))
    present = jnp.repeat(jnp.transpose(valid_slots, (0, 2, 1)), BLOCK, axis=2)[:, :, None, :]
    scores = jnp.where(present, scores, masked_score)
    peak = jnp.max(scores, axis=3, keepdims=True)
    expo = jnp.exp(scores - peak)
    total = jnp.sum(expo, axis=3)
    weights = expo.astype(jnp.bfloat16)
    mixture = jnp.einsum("bhqs,bshd->bqhd", weights, value_grid, preferred_element_type=jnp.float32)
    mixture = mixture / jnp.transpose(total, (0, 2, 1))[..., None]
    return mixture.reshape(count_q, BLOCK, heads_here * HEAD_DIM).astype(jnp.bfloat16)


def xor_perm(count, bit):
    return [(i, i ^ bit) for i in range(count)]


def tree_reduce(parts, merge, axis):
    count = lax.axis_size(axis)
    place = lax.axis_index(axis)
    bits = []
    bit = 1
    while bit < count:
        bits.append(bit)
        bit *= 2
    for bit in bits:
        upper = (place // bit) % 2
        halves = jax.tree.map(lambda x: x.reshape((2, x.shape[0] // 2) + x.shape[1:]), parts)
        keep = jax.tree.map(lambda h: lax.dynamic_index_in_dim(h, upper, 0, keepdims=False), halves)
        send = jax.tree.map(lambda h: lax.dynamic_index_in_dim(h, 1 - upper, 0, keepdims=False), halves)
        got = lax.ppermute(send, axis, xor_perm(count, bit))
        parts = merge(keep, got)
    for bit in reversed(bits):
        upper = (place // bit) % 2
        got = lax.ppermute(parts, axis, xor_perm(count, bit))

        def join(mine, theirs):
            pair = jnp.stack([mine, theirs])
            first = lax.dynamic_index_in_dim(pair, upper, 0, keepdims=False)
            second = lax.dynamic_index_in_dim(pair, 1 - upper, 0, keepdims=False)
            return jnp.concatenate([first, second], axis=0)

        parts = jax.tree.map(join, parts, got)
    return parts


def add_merge(a, b):
    return jax.tree.map(jnp.add, a, b)


def softmax_merge(a, b):
    mix_a, total_a, peak_a = a
    mix_b, total_b, peak_b = b
    peak = jnp.maximum(peak_a, peak_b)
    scale_a = jnp.exp(peak_a - peak)
    scale_b = jnp.exp(peak_b - peak)
    mix = mix_a * scale_a[..., None] + mix_b * scale_b[..., None]
    total = total_a * scale_a + total_b * scale_b
    return (mix, total, peak)


def project_over_head(rows, out_weight):
    head_count = lax.axis_size("head")
    row_count, width_here = rows.shape
    weight_view = out_weight.reshape(width_here, head_count, out_weight.shape[1] // head_count)
    partial = jnp.einsum("td,dhc->htc", rows, weight_view, preferred_element_type=jnp.float32)
    gathered = lax.all_to_all(partial.astype(jnp.bfloat16), "head", 0, 0, tiled=True)
    return jnp.sum(gathered.astype(jnp.float32), axis=0)


def on_device(
    queries,
    keys,
    values,
    out_weight,
    global_blocks,
    random_blocks,
    window_blocks,
    yarn_scale,
    yarn_context,
):
    tok_here, width_here = queries.shape
    heads_here = width_here // HEAD_DIM
    blocks_here = tok_here // BLOCK
    seq_count = lax.axis_size("seq")
    seq_place = lax.axis_index("seq")
    block_total = seq_count * blocks_here
    frequency, mscale = yarn_tables(yarn_scale, yarn_context)
    first_row = seq_place * tok_here
    query_rot = rotate(queries, first_row, frequency, mscale)
    key_rot = rotate(keys, first_row, frequency, mscale)
    pair_kv = jnp.stack([key_rot, values])
    padded = padded_2(pair_kv, (("seq", 1),), WMAX * BLOCK)
    padded_blocks = padded.reshape(2, blocks_here + 2 * WMAX, BLOCK, width_here)
    offsets = jnp.arange(-WMAX, WMAX + 1)
    window_ids = seq_place * blocks_here + jnp.arange(blocks_here)[:, None] + offsets[None, :]
    inside = (window_ids >= 0) & (window_ids < block_total)
    reach = jnp.abs(offsets)[None, :, None] <= window_blocks[None, None, :]
    window_valid = inside[:, :, None] & reach
    owner_global = global_blocks // blocks_here
    local_global = jnp.clip(global_blocks - seq_place * blocks_here, 0, blocks_here - 1)
    mine_global = owner_global == seq_place
    query_view = query_rot.reshape(blocks_here, BLOCK, width_here)
    key_view = key_rot.reshape(blocks_here, BLOCK, width_here)
    value_view = values.reshape(blocks_here, BLOCK, width_here)
    picked = jnp.stack([query_view[local_global], key_view[local_global], value_view[local_global]])
    masked = jnp.where(mine_global[None, :, None, None], picked, jnp.zeros_like(picked))
    shared = tree_reduce(masked.reshape(3 * GLOB * BLOCK, width_here), add_merge, "seq")
    shared = shared.reshape(3, GLOB, BLOCK, width_here)
    slot_total = blocks_here * RAND
    capacity = (slot_total + seq_count - 1) // seq_count
    flat_ids = random_blocks.reshape(seq_count, slot_total)
    owners = flat_ids // blocks_here
    slot_order = jnp.arange(slot_total)
    same_owner = (owners[:, :, None] == owners[:, None, :]) & (
        slot_order[None, None, :] < slot_order[None, :, None]
    )
    ranks = jnp.sum(same_owner.astype(jnp.int32), axis=2)
    local_ids = flat_ids - owners * blocks_here
    wanted = (owners[:, None, :] == seq_place) & (
        ranks[:, None, :] == jnp.arange(capacity)[None, :, None]
    )
    send_local = jnp.sum(jnp.where(wanted, local_ids[:, None, :], 0), axis=2)
    kv_blocks = pair_kv.reshape(2, blocks_here, BLOCK, width_here)
    outgoing = kv_blocks[:, send_local]
    incoming = lax.all_to_all(outgoing, "seq", split_axis=1, concat_axis=1, tiled=True)
    my_owners = owners[seq_place]
    my_ranks = ranks[seq_place]
    random_kv = incoming[:, my_owners, my_ranks].reshape(2, blocks_here, RAND, BLOCK, width_here)
    slot_parts = [
        padded_blocks[:, offset_slot : offset_slot + blocks_here][:, :, None]
        for offset_slot in range(2 * WMAX + 1)
    ]
    slot_parts.append(
        jnp.broadcast_to(shared[1:3][:, None], (2, blocks_here, GLOB, BLOCK, width_here))
    )
    slot_parts.append(random_kv)
    all_kv = jnp.concatenate(slot_parts, axis=2)
    all_valid = jnp.concatenate(
        [window_valid, jnp.ones((blocks_here, GLOB + RAND, heads_here), dtype=bool)], axis=1
    )
    attended = block_attend(query_view, all_kv[0], all_kv[1], all_valid)
    mixed = project_over_head(attended.reshape(tok_here, width_here), out_weight)
    global_query = shared[0].reshape(GLOB, BLOCK, heads_here, HEAD_DIM)
    key_grid = key_rot.reshape(tok_here, heads_here, HEAD_DIM)
    value_grid = values.reshape(tok_here, heads_here, HEAD_DIM)
    global_scores = jnp.einsum(
        "gqhd,khd->gqhk", global_query, key_grid, preferred_element_type=jnp.float32
    ) * (1.0 / math.sqrt(HEAD_DIM))
    local_peak = jnp.max(global_scores, axis=3)
    expo = jnp.exp(global_scores - local_peak[..., None])
    partial_total = jnp.sum(expo, axis=3)
    partial_mix = jnp.einsum(
        "gqhk,khd->gqhd", expo.astype(jnp.bfloat16), value_grid, preferred_element_type=jnp.float32
    )
    row_total = GLOB * BLOCK
    mix_sum, total_sum, _ = tree_reduce(
        (
            partial_mix.reshape(row_total, heads_here, HEAD_DIM),
            partial_total.reshape(row_total, heads_here),
            local_peak.reshape(row_total, heads_here),
        ),
        softmax_merge,
        "seq",
    )
    global_out = (mix_sum / total_sum[..., None]).reshape(row_total, width_here).astype(jnp.bfloat16)
    global_mixed = project_over_head(global_out, out_weight).reshape(GLOB, BLOCK, -1)
    mixed = mixed.reshape(blocks_here, BLOCK, -1)
    block_index = jnp.arange(blocks_here)
    for global_slot in range(GLOB):
        hit = mine_global[global_slot] & (block_index == local_global[global_slot])
        mixed = jnp.where(hit[:, None, None], global_mixed[global_slot][None], mixed)
    return mixed.reshape(tok_here, -1).astype(jnp.bfloat16)


def solution(mesh):
    in_specs = (
        P("seq", "head"),
        P("seq", "head"),
        P("seq", "head"),
        P("head", None),
        P(),
        P(),
        P("head"),
        P(),
        P(),
    )
    out_specs = P("seq", "head")
    return jax.shard_map(
        on_device, mesh=mesh, in_specs=in_specs, out_specs=out_specs, check_vma=False
    )
```

```python
import math

import jax
import jax.numpy as jnp
from jax import lax
from jax.sharding import PartitionSpec as P

HEAD_DIM = 128
BLOCK = 64
GLOB = 2
RAND = 3
WMAX = 2


masked_score = -1e30


def padded_2(cells, sides, width):
    for axis, dim in sides:
        count = lax.axis_size(axis)
        ends = count - 1
        head = lax.slice_in_dim(cells, 0, width, axis=dim)
        tail = lax.slice_in_dim(cells, cells.shape[dim] - width, cells.shape[dim], axis=dim)
        cells = jnp.concatenate(
            [
                lax.ppermute(tail, axis, [(i, (i + 1) % count) for i in range(ends)]),
                cells,
                lax.ppermute(head, axis, [((i + 1) % count, i) for i in range(ends)]),
            ],
            axis=dim,
        )
    return cells


def yarn_tables(yarn_scale, yarn_context):
    half_dim = HEAD_DIM // 2
    pair_index = jnp.arange(half_dim).astype(jnp.float32)
    base_rate = 10000.0 ** (-2.0 * pair_index / HEAD_DIM)
    factor = yarn_scale[0].astype(jnp.float32)
    context = yarn_context[0].astype(jnp.float32)
    turn_ratio = context * base_rate / (2.0 * math.pi)
    ramp_weight = jnp.clip((turn_ratio - 1.0) / 31.0, 0.0, 1.0)
    frequency = base_rate * ((1.0 - ramp_weight) / factor + ramp_weight)
    mscale = 0.1 * jnp.log(factor) + 1.0
    return (frequency, mscale)


def rotate(source, first_row, frequency, mscale):
    row_count, row_width = source.shape
    half_dim = HEAD_DIM // 2
    position = (first_row + jnp.arange(row_count)).astype(jnp.float32)
    angle_table = position[:, None] * frequency[None, :]
    cosine = jnp.cos(angle_table)[:, None, :] * mscale
    sine_part = jnp.sin(angle_table)[:, None, :] * mscale
    halves_view = source.astype(jnp.float32).reshape(row_count, row_width // HEAD_DIM, 2, half_dim)
    lower_half = halves_view[:, :, 0]
    upper_half = halves_view[:, :, 1]
    turned = jnp.stack(
        [
            lower_half * cosine - upper_half * sine_part,
            upper_half * cosine + lower_half * sine_part,
        ],
        axis=2,
    )
    return turned.reshape(row_count, row_width).astype(jnp.bfloat16)


def block_attend(query_blocks, key_blocks, value_blocks, valid_slots):
    count_q, slot_count = (key_blocks.shape[0], key_blocks.shape[1])
    heads_here = query_blocks.shape[-1] // HEAD_DIM
    query_grid = query_blocks.reshape(count_q, BLOCK, heads_here, HEAD_DIM)
    key_grid = key_blocks.reshape(count_q, slot_count * BLOCK, heads_here, HEAD_DIM)
    value_grid = value_blocks.reshape(count_q, slot_count * BLOCK, heads_here, HEAD_DIM)
    scores = jnp.einsum(
        "bqhd,bshd->bhqs", query_grid, key_grid, preferred_element_type=jnp.float32
    ) * (1.0 / math.sqrt(HEAD_DIM))
    present = jnp.repeat(jnp.transpose(valid_slots, (0, 2, 1)), BLOCK, axis=2)[:, :, None, :]
    scores = jnp.where(present, scores, masked_score)
    peak = jnp.max(scores, axis=3, keepdims=True)
    expo = jnp.exp(scores - peak)
    total = jnp.sum(expo, axis=3)
    weights = expo.astype(jnp.bfloat16)
    mixture = jnp.einsum("bhqs,bshd->bqhd", weights, value_grid, preferred_element_type=jnp.float32)
    mixture = mixture / jnp.transpose(total, (0, 2, 1))[..., None]
    return mixture.reshape(count_q, BLOCK, heads_here * HEAD_DIM).astype(jnp.bfloat16)


def xor_perm(count, bit):
    return [(i, i ^ bit) for i in range(count)]


def tree_reduce(parts, merge, axis):
    count = lax.axis_size(axis)
    place = lax.axis_index(axis)
    bits = []
    bit = 1
    while bit < count:
        bits.append(bit)
        bit *= 2
    for bit in bits:
        upper = (place // bit) % 2
        halves = jax.tree.map(lambda x: x.reshape((2, x.shape[0] // 2) + x.shape[1:]), parts)
        keep = jax.tree.map(lambda h: lax.dynamic_index_in_dim(h, upper, 0, keepdims=False), halves)
        send = jax.tree.map(lambda h: lax.dynamic_index_in_dim(h, 1 - upper, 0, keepdims=False), halves)
        got = lax.ppermute(send, axis, xor_perm(count, bit))
        parts = merge(keep, got)
    for bit in reversed(bits):
        upper = (place // bit) % 2
        got = lax.ppermute(parts, axis, xor_perm(count, bit))

        def join(mine, theirs):
            pair = jnp.stack([mine, theirs])
            first = lax.dynamic_index_in_dim(pair, upper, 0, keepdims=False)
            second = lax.dynamic_index_in_dim(pair, 1 - upper, 0, keepdims=False)
            return jnp.concatenate([first, second], axis=0)

        parts = jax.tree.map(join, parts, got)
    return parts


def add_merge(a, b):
    return jax.tree.map(jnp.add, a, b)


def softmax_merge(a, b):
    peak = jnp.maximum(a[..., -1], b[..., -1])
    scale_a = jnp.exp(a[..., -1] - peak)
    scale_b = jnp.exp(b[..., -1] - peak)
    merged = a[..., :-1] * scale_a[..., None] + b[..., :-1] * scale_b[..., None]
    return jnp.concatenate([merged, peak[..., None]], axis=-1)


def project_over_head(rows, out_weight):
    head_count = lax.axis_size("head")
    row_count = rows.shape[0]
    partial = lax.dot_general(
        out_weight, rows, (((0,), (1,)), ((), ())), preferred_element_type=jnp.float32
    ).astype(jnp.bfloat16)
    partial = partial.reshape(head_count, out_weight.shape[1] // head_count, row_count)
    gathered = lax.all_to_all(partial, "head", 0, 0, tiled=True)
    return jnp.sum(gathered.astype(jnp.float32), axis=0).T


def sparse_attend(query_view, window_kv, global_kv, random_kv, window_valid):
    blocks_here, _, width_here = query_view.shape
    heads_here = width_here // HEAD_DIM
    q = query_view.reshape(blocks_here, BLOCK, heads_here, HEAD_DIM)
    win = window_kv.reshape(2, blocks_here + 2 * WMAX, BLOCK, heads_here, HEAD_DIM)
    glo = global_kv.reshape(2, GLOB, BLOCK, heads_here, HEAD_DIM)
    ran = random_kv.reshape(blocks_here, RAND, 2, BLOCK, heads_here, HEAD_DIM)
    scale = 1.0 / math.sqrt(HEAD_DIM)
    parts = []
    for offset_slot in range(2 * WMAX + 1):
        keys_o = win[0, offset_slot : offset_slot + blocks_here]
        s = jnp.einsum("bqhd,bkhd->bhqk", q, keys_o, preferred_element_type=jnp.float32) * scale
        valid = window_valid[:, offset_slot, :]
        parts.append(jnp.where(valid[:, :, None, None], s, masked_score))
    s = jnp.einsum("bqhd,gkhd->bhqgk", q, glo[0], preferred_element_type=jnp.float32) * scale
    parts.append(s.reshape(blocks_here, heads_here, BLOCK, GLOB * BLOCK))
    s = jnp.einsum("bqhd,brkhd->bhqrk", q, ran[:, :, 0], preferred_element_type=jnp.float32) * scale
    parts.append(s.reshape(blocks_here, heads_here, BLOCK, RAND * BLOCK))
    scores = jnp.concatenate(parts, axis=3)
    peak = jnp.max(scores, axis=3, keepdims=True)
    expo = jnp.exp(scores - peak)
    total = jnp.sum(expo, axis=3)
    weights = expo.astype(jnp.bfloat16)
    window_count = (2 * WMAX + 1) * BLOCK
    mixture = None
    for offset_slot in range(2 * WMAX + 1):
        w = weights[..., offset_slot * BLOCK : (offset_slot + 1) * BLOCK]
        vals_o = win[1, offset_slot : offset_slot + blocks_here]
        m = jnp.einsum("bhqk,bkhd->bqhd", w, vals_o, preferred_element_type=jnp.float32)
        mixture = m if mixture is None else mixture + m
    w = weights[..., window_count : window_count + GLOB * BLOCK].reshape(blocks_here, heads_here, BLOCK, GLOB, BLOCK)
    mixture = mixture + jnp.einsum("bhqgk,gkhd->bqhd", w, glo[1], preferred_element_type=jnp.float32)
    w = weights[..., window_count + GLOB * BLOCK :].reshape(blocks_here, heads_here, BLOCK, RAND, BLOCK)
    mixture = mixture + jnp.einsum("bhqrk,brkhd->bqhd", w, ran[:, :, 1], preferred_element_type=jnp.float32)
    mixture = mixture / jnp.transpose(total, (0, 2, 1))[..., None]
    return mixture.reshape(blocks_here, BLOCK, width_here).astype(jnp.bfloat16)


def on_device(
    queries,
    keys,
    values,
    out_weight,
    global_blocks,
    random_blocks,
    window_blocks,
    yarn_scale,
    yarn_context,
):
    tok_here, width_here = queries.shape
    heads_here = width_here // HEAD_DIM
    blocks_here = tok_here // BLOCK
    seq_count = lax.axis_size("seq")
    seq_place = lax.axis_index("seq")
    block_total = seq_count * blocks_here
    frequency, mscale = yarn_tables(yarn_scale, yarn_context)
    first_row = seq_place * tok_here
    query_rot = rotate(queries, first_row, frequency, mscale)
    key_rot = rotate(keys, first_row, frequency, mscale)
    pair_kv = jnp.stack([key_rot, values])
    padded = padded_2(pair_kv, (("seq", 1),), WMAX * BLOCK)
    padded_blocks = padded.reshape(2, blocks_here + 2 * WMAX, BLOCK, width_here)
    offsets = jnp.arange(-WMAX, WMAX + 1)
    window_ids = seq_place * blocks_here + jnp.arange(blocks_here)[:, None] + offsets[None, :]
    inside = (window_ids >= 0) & (window_ids < block_total)
    reach = jnp.abs(offsets)[None, :, None] <= window_blocks[None, None, :]
    window_valid = inside[:, :, None] & reach
    owner_global = global_blocks // blocks_here
    local_global = jnp.clip(global_blocks - seq_place * blocks_here, 0, blocks_here - 1)
    mine_global = owner_global == seq_place
    query_view = query_rot.reshape(blocks_here, BLOCK, width_here)
    key_view = key_rot.reshape(blocks_here, BLOCK, width_here)
    value_view = values.reshape(blocks_here, BLOCK, width_here)
    picked = jnp.stack([query_view[local_global], key_view[local_global], value_view[local_global]])
    masked = jnp.where(mine_global[None, :, None, None], picked, jnp.zeros_like(picked))
    shared = tree_reduce(masked.reshape(3 * GLOB * BLOCK, width_here), add_merge, "seq")
    shared = shared.reshape(3, GLOB, BLOCK, width_here)
    slot_total = blocks_here * RAND
    capacity = (slot_total + seq_count - 1) // seq_count
    flat_ids = random_blocks.reshape(seq_count, slot_total)
    owners = flat_ids // blocks_here
    slot_order = jnp.arange(slot_total)
    same_owner = (owners[:, :, None] == owners[:, None, :]) & (
        slot_order[None, None, :] < slot_order[None, :, None]
    )
    ranks = jnp.sum(same_owner.astype(jnp.int32), axis=2)
    local_ids = flat_ids - owners * blocks_here
    wanted = (owners[:, None, :] == seq_place) & (
        ranks[:, None, :] == jnp.arange(capacity)[None, :, None]
    )
    send_local = jnp.sum(jnp.where(wanted, local_ids[:, None, :], 0), axis=2)
    kv_blocks = jnp.stack(
        [key_rot.reshape(blocks_here, BLOCK, width_here), value_view], axis=1
    )
    outgoing = kv_blocks[send_local]
    incoming = lax.all_to_all(outgoing, "seq", split_axis=0, concat_axis=0, tiled=True)
    my_owners = owners[seq_place]
    my_ranks = ranks[seq_place]
    random_kv = incoming[my_owners, my_ranks].reshape(blocks_here, RAND, 2, BLOCK, width_here)
    attended = sparse_attend(query_view, padded_blocks, shared[1:3], random_kv, window_valid)
    mixed = project_over_head(attended.reshape(tok_here, width_here), out_weight)
    global_query = shared[0].reshape(GLOB, BLOCK, heads_here, HEAD_DIM)
    key_grid = key_rot.reshape(tok_here, heads_here, HEAD_DIM)
    value_grid = values.reshape(tok_here, heads_here, HEAD_DIM)
    global_scores = jnp.einsum(
        "gqhd,khd->gqhk", global_query, key_grid, preferred_element_type=jnp.float32
    ) * (1.0 / math.sqrt(HEAD_DIM))
    local_peak = jnp.max(global_scores, axis=3)
    expo = jnp.exp(global_scores - local_peak[..., None])
    partial_total = jnp.sum(expo, axis=3)
    partial_mix = jnp.einsum(
        "gqhk,khd->gqhd", expo.astype(jnp.bfloat16), value_grid, preferred_element_type=jnp.float32
    )
    row_total = GLOB * BLOCK
    packed = jnp.concatenate(
        [
            partial_mix.reshape(row_total, heads_here, HEAD_DIM),
            partial_total.reshape(row_total, heads_here, 1),
            local_peak.reshape(row_total, heads_here, 1),
        ],
        axis=2,
    )
    reduced = tree_reduce(packed, softmax_merge, "seq")
    global_out = (
        (reduced[..., :HEAD_DIM] / reduced[..., HEAD_DIM : HEAD_DIM + 1])
        .reshape(row_total, width_here)
        .astype(jnp.bfloat16)
    )
    global_mixed = project_over_head(global_out, out_weight).reshape(GLOB, BLOCK, -1)
    mixed = mixed.reshape(blocks_here, BLOCK, -1)
    block_index = jnp.arange(blocks_here)
    for global_slot in range(GLOB):
        hit = mine_global[global_slot] & (block_index == local_global[global_slot])
        mixed = jnp.where(hit[:, None, None], global_mixed[global_slot][None], mixed)
    return mixed.reshape(tok_here, -1).astype(jnp.bfloat16)


def solution(mesh):
    in_specs = (
        P("seq", "head"),
        P("seq", "head"),
        P("seq", "head"),
        P("head", None),
        P(),
        P(),
        P("head"),
        P(),
        P(),
    )
    out_specs = P("seq", "head")
    return jax.shard_map(
        on_device, mesh=mesh, in_specs=in_specs, out_specs=out_specs, check_vma=False
    )
```

```python
import math

import jax
import jax.numpy as jnp
from jax import lax
from jax.sharding import PartitionSpec as P

HEAD_DIM = 128
BLOCK = 64
GLOB = 2
RAND = 3
WMAX = 2


masked_score = -1e30


def padded_2(cells, sides, width):
    for axis, dim in sides:
        count = lax.axis_size(axis)
        ends = count - 1
        head = lax.slice_in_dim(cells, 0, width, axis=dim)
        tail = lax.slice_in_dim(cells, cells.shape[dim] - width, cells.shape[dim], axis=dim)
        cells = jnp.concatenate(
            [
                lax.ppermute(tail, axis, [(i, (i + 1) % count) for i in range(ends)]),
                cells,
                lax.ppermute(head, axis, [((i + 1) % count, i) for i in range(ends)]),
            ],
            axis=dim,
        )
    return cells


def yarn_tables(yarn_scale, yarn_context):
    half_dim = HEAD_DIM // 2
    pair_index = jnp.arange(half_dim).astype(jnp.float32)
    base_rate = 10000.0 ** (-2.0 * pair_index / HEAD_DIM)
    factor = yarn_scale[0].astype(jnp.float32)
    context = yarn_context[0].astype(jnp.float32)
    turn_ratio = context * base_rate / (2.0 * math.pi)
    ramp_weight = jnp.clip((turn_ratio - 1.0) / 31.0, 0.0, 1.0)
    frequency = base_rate * ((1.0 - ramp_weight) / factor + ramp_weight)
    mscale = 0.1 * jnp.log(factor) + 1.0
    return (frequency, mscale)


def rotate(source, first_row, frequency, mscale):
    row_count, row_width = source.shape
    half_dim = HEAD_DIM // 2
    position = (first_row + jnp.arange(row_count)).astype(jnp.float32)
    angle_table = position[:, None] * frequency[None, :]
    cosine = jnp.cos(angle_table)[:, None, :] * mscale
    sine_part = jnp.sin(angle_table)[:, None, :] * mscale
    halves_view = source.astype(jnp.float32).reshape(row_count, row_width // HEAD_DIM, 2, half_dim)
    lower_half = halves_view[:, :, 0]
    upper_half = halves_view[:, :, 1]
    turned = jnp.stack(
        [
            lower_half * cosine - upper_half * sine_part,
            upper_half * cosine + lower_half * sine_part,
        ],
        axis=2,
    )
    return turned.reshape(row_count, row_width).astype(jnp.bfloat16)


def block_attend(query_blocks, key_blocks, value_blocks, valid_slots):
    count_q, slot_count = (key_blocks.shape[0], key_blocks.shape[1])
    heads_here = query_blocks.shape[-1] // HEAD_DIM
    query_grid = query_blocks.reshape(count_q, BLOCK, heads_here, HEAD_DIM)
    key_grid = key_blocks.reshape(count_q, slot_count * BLOCK, heads_here, HEAD_DIM)
    value_grid = value_blocks.reshape(count_q, slot_count * BLOCK, heads_here, HEAD_DIM)
    scores = jnp.einsum(
        "bqhd,bshd->bhqs", query_grid, key_grid, preferred_element_type=jnp.float32
    ) * (1.0 / math.sqrt(HEAD_DIM))
    present = jnp.repeat(jnp.transpose(valid_slots, (0, 2, 1)), BLOCK, axis=2)[:, :, None, :]
    scores = jnp.where(present, scores, masked_score)
    peak = jnp.max(scores, axis=3, keepdims=True)
    expo = jnp.exp(scores - peak)
    total = jnp.sum(expo, axis=3)
    weights = expo.astype(jnp.bfloat16)
    mixture = jnp.einsum("bhqs,bshd->bqhd", weights, value_grid, preferred_element_type=jnp.float32)
    mixture = mixture / jnp.transpose(total, (0, 2, 1))[..., None]
    return mixture.reshape(count_q, BLOCK, heads_here * HEAD_DIM).astype(jnp.bfloat16)


def xor_perm(count, bit):
    return [(i, i ^ bit) for i in range(count)]


def tree_reduce(parts, merge, axis):
    count = lax.axis_size(axis)
    place = lax.axis_index(axis)
    bits = []
    bit = 1
    while bit < count:
        bits.append(bit)
        bit *= 2
    for bit in bits:
        upper = (place // bit) % 2
        halves = jax.tree.map(lambda x: x.reshape((2, x.shape[0] // 2) + x.shape[1:]), parts)
        keep = jax.tree.map(lambda h: lax.dynamic_index_in_dim(h, upper, 0, keepdims=False), halves)
        send = jax.tree.map(lambda h: lax.dynamic_index_in_dim(h, 1 - upper, 0, keepdims=False), halves)
        got = lax.ppermute(send, axis, xor_perm(count, bit))
        parts = merge(keep, got)
    for bit in reversed(bits):
        upper = (place // bit) % 2
        got = lax.ppermute(parts, axis, xor_perm(count, bit))

        def join(mine, theirs):
            pair = jnp.stack([mine, theirs])
            first = lax.dynamic_index_in_dim(pair, upper, 0, keepdims=False)
            second = lax.dynamic_index_in_dim(pair, 1 - upper, 0, keepdims=False)
            return jnp.concatenate([first, second], axis=0)

        parts = jax.tree.map(join, parts, got)
    return parts


def add_merge(a, b):
    return jax.tree.map(jnp.add, a, b)


def softmax_merge(a, b):
    width = a.shape[1] - 128
    heads = width // HEAD_DIM
    peak_a = a[:, width + heads : width + 2 * heads]
    peak_b = b[:, width + heads : width + 2 * heads]
    peak = jnp.maximum(peak_a, peak_b)
    scale_a = jnp.exp(peak_a - peak)
    scale_b = jnp.exp(peak_b - peak)
    rows = a.shape[0]
    mix = (
        a[:, :width].reshape(rows, heads, HEAD_DIM) * scale_a[..., None]
        + b[:, :width].reshape(rows, heads, HEAD_DIM) * scale_b[..., None]
    ).reshape(rows, width)
    total = a[:, width : width + heads] * scale_a + b[:, width : width + heads] * scale_b
    pad = jnp.zeros((rows, 128 - 2 * heads), a.dtype)
    return jnp.concatenate([mix, total, peak, pad], axis=1)


def head_partials(rows, out_weight):
    head_count = lax.axis_size("head")
    partial = lax.dot_general(
        out_weight, rows, (((0,), (1,)), ((), ())), preferred_element_type=jnp.float32
    ).astype(jnp.bfloat16)
    return partial.reshape(head_count, out_weight.shape[1] // head_count, rows.shape[0])


def sum_over_head(partial):
    gathered = lax.all_to_all(partial, "head", 0, 0, tiled=True)
    return jnp.sum(gathered.astype(jnp.float32), axis=0).T


def on_device(
    queries,
    keys,
    values,
    out_weight,
    global_blocks,
    random_blocks,
    window_blocks,
    yarn_scale,
    yarn_context,
):
    tok_here, width_here = queries.shape
    heads_here = width_here // HEAD_DIM
    blocks_here = tok_here // BLOCK
    seq_count = lax.axis_size("seq")
    seq_place = lax.axis_index("seq")
    block_total = seq_count * blocks_here
    frequency, mscale = yarn_tables(yarn_scale, yarn_context)
    first_row = seq_place * tok_here
    query_rot = rotate(queries, first_row, frequency, mscale)
    key_rot = rotate(keys, first_row, frequency, mscale)
    pair_kv = jnp.stack([key_rot, values])
    padded = padded_2(pair_kv, (("seq", 1),), WMAX * BLOCK)
    padded_blocks = padded.reshape(2, blocks_here + 2 * WMAX, BLOCK, width_here)
    offsets = jnp.arange(-WMAX, WMAX + 1)
    window_ids = seq_place * blocks_here + jnp.arange(blocks_here)[:, None] + offsets[None, :]
    inside = (window_ids >= 0) & (window_ids < block_total)
    reach = jnp.abs(offsets)[None, :, None] <= window_blocks[None, None, :]
    window_valid = inside[:, :, None] & reach
    owner_global = global_blocks // blocks_here
    local_global = jnp.clip(global_blocks - seq_place * blocks_here, 0, blocks_here - 1)
    mine_global = owner_global == seq_place
    query_view = query_rot.reshape(blocks_here, BLOCK, width_here)
    key_view = key_rot.reshape(blocks_here, BLOCK, width_here)
    value_view = values.reshape(blocks_here, BLOCK, width_here)
    picked = jnp.stack([query_view[local_global], key_view[local_global], value_view[local_global]])
    masked = jnp.where(mine_global[None, :, None, None], picked, jnp.zeros_like(picked))
    shared = tree_reduce(masked.reshape(3 * GLOB * BLOCK, width_here), add_merge, "seq")
    shared = shared.reshape(3, GLOB, BLOCK, width_here)
    slot_total = blocks_here * RAND
    capacity = (slot_total + seq_count - 1) // seq_count
    flat_ids = random_blocks.reshape(seq_count, slot_total)
    owners = flat_ids // blocks_here
    slot_order = jnp.arange(slot_total)
    same_owner = (owners[:, :, None] == owners[:, None, :]) & (
        slot_order[None, None, :] < slot_order[None, :, None]
    )
    ranks = jnp.sum(same_owner.astype(jnp.int32), axis=2)
    local_ids = flat_ids - owners * blocks_here
    wanted = (owners[:, None, :] == seq_place) & (
        ranks[:, None, :] == jnp.arange(capacity)[None, :, None]
    )
    send_local = jnp.sum(jnp.where(wanted, local_ids[:, None, :], 0), axis=2)
    kv_blocks = pair_kv.reshape(2, blocks_here, BLOCK, width_here)
    outgoing = kv_blocks[:, send_local]
    incoming = lax.all_to_all(outgoing, "seq", split_axis=1, concat_axis=1, tiled=True)
    my_owners = owners[seq_place]
    my_ranks = ranks[seq_place]
    random_kv = incoming[:, my_owners, my_ranks].reshape(2, blocks_here, RAND, BLOCK, width_here)
    slot_parts = [
        padded_blocks[:, offset_slot : offset_slot + blocks_here][:, :, None]
        for offset_slot in range(2 * WMAX + 1)
    ]
    slot_parts.append(
        jnp.broadcast_to(shared[1:3][:, None], (2, blocks_here, GLOB, BLOCK, width_here))
    )
    slot_parts.append(random_kv)
    all_kv = jnp.concatenate(slot_parts, axis=2)
    all_valid = jnp.concatenate(
        [window_valid, jnp.ones((blocks_here, GLOB + RAND, heads_here), dtype=bool)], axis=1
    )
    attended = block_attend(query_view, all_kv[0], all_kv[1], all_valid)
    global_query = shared[0]
    key_later = key_rot
    value_later = values
    global_query = global_query.reshape(GLOB, BLOCK, heads_here, HEAD_DIM)
    key_grid = key_later.reshape(tok_here, heads_here, HEAD_DIM)
    value_grid = value_later.reshape(tok_here, heads_here, HEAD_DIM)
    global_scores = jnp.einsum(
        "gqhd,khd->gqhk", global_query, key_grid, preferred_element_type=jnp.float32
    ) * (1.0 / math.sqrt(HEAD_DIM))
    local_peak = jnp.max(global_scores, axis=3)
    expo = jnp.exp(global_scores - local_peak[..., None])
    partial_total = jnp.sum(expo, axis=3)
    partial_mix = jnp.einsum(
        "gqhk,khd->gqhd", expo.astype(jnp.bfloat16), value_grid, preferred_element_type=jnp.float32
    )
    row_total = GLOB * BLOCK
    packed = jnp.concatenate(
        [
            partial_mix.reshape(row_total, width_here),
            partial_total.reshape(row_total, heads_here),
            local_peak.reshape(row_total, heads_here),
            jnp.zeros((row_total, 128 - 2 * heads_here), jnp.float32),
        ],
        axis=1,
    )
    reduced = tree_reduce(packed, softmax_merge, "seq")
    mix_sum = reduced[:, :width_here].reshape(row_total, heads_here, HEAD_DIM)
    total_sum = reduced[:, width_here : width_here + heads_here]
    global_out = (mix_sum / total_sum[..., None]).reshape(row_total, width_here).astype(jnp.bfloat16)
    global_out = global_out.reshape(GLOB, BLOCK, width_here)
    block_index = jnp.arange(blocks_here)
    for global_slot in range(GLOB):
        hit = mine_global[global_slot] & (block_index == local_global[global_slot])
        attended = jnp.where(hit[:, None, None], global_out[global_slot][None], attended)
    mixed = sum_over_head(head_partials(attended.reshape(tok_here, width_here), out_weight))
    return mixed.astype(jnp.bfloat16)


def solution(mesh):
    in_specs = (
        P("seq", "head"),
        P("seq", "head"),
        P("seq", "head"),
        P("head", None),
        P(),
        P(),
        P("head"),
        P(),
        P(),
    )
    out_specs = P("seq", "head")
    return jax.shard_map(
        on_device, mesh=mesh, in_specs=in_specs, out_specs=out_specs, check_vma=False
    )
```

```python
import math

import jax
import jax.numpy as jnp
from jax import lax
from jax.sharding import PartitionSpec as P

HEAD_DIM = 128
BLOCK = 64
GLOB = 2
RAND = 3
WMAX = 2


masked_score = -1e30


def padded_2(cells, sides, width):
    for axis, dim in sides:
        count = lax.axis_size(axis)
        ends = count - 1
        head = lax.slice_in_dim(cells, 0, width, axis=dim)
        tail = lax.slice_in_dim(cells, cells.shape[dim] - width, cells.shape[dim], axis=dim)
        cells = jnp.concatenate(
            [
                lax.ppermute(tail, axis, [(i, (i + 1) % count) for i in range(ends)]),
                cells,
                lax.ppermute(head, axis, [((i + 1) % count, i) for i in range(ends)]),
            ],
            axis=dim,
        )
    return cells


def yarn_tables(yarn_scale, yarn_context):
    half_dim = HEAD_DIM // 2
    pair_index = jnp.arange(half_dim).astype(jnp.float32)
    base_rate = 10000.0 ** (-2.0 * pair_index / HEAD_DIM)
    factor = yarn_scale[0].astype(jnp.float32)
    context = yarn_context[0].astype(jnp.float32)
    turn_ratio = context * base_rate / (2.0 * math.pi)
    ramp_weight = jnp.clip((turn_ratio - 1.0) / 31.0, 0.0, 1.0)
    frequency = base_rate * ((1.0 - ramp_weight) / factor + ramp_weight)
    mscale = 0.1 * jnp.log(factor) + 1.0
    return (frequency, mscale)


def rotate(source, first_row, frequency, mscale):
    row_count, row_width = source.shape
    half_dim = HEAD_DIM // 2
    position = (first_row + jnp.arange(row_count)).astype(jnp.float32)
    angle_table = position[:, None] * frequency[None, :]
    cosine = jnp.cos(angle_table)[:, None, :] * mscale
    sine_part = jnp.sin(angle_table)[:, None, :] * mscale
    halves_view = source.astype(jnp.float32).reshape(row_count, row_width // HEAD_DIM, 2, half_dim)
    lower_half = halves_view[:, :, 0]
    upper_half = halves_view[:, :, 1]
    turned = jnp.stack(
        [
            lower_half * cosine - upper_half * sine_part,
            upper_half * cosine + lower_half * sine_part,
        ],
        axis=2,
    )
    return turned.reshape(row_count, row_width).astype(jnp.bfloat16)


def block_attend(query_blocks, key_blocks, value_blocks, valid_slots):
    count_q, slot_count = (key_blocks.shape[0], key_blocks.shape[1])
    heads_here = query_blocks.shape[-1] // HEAD_DIM
    query_grid = query_blocks.reshape(count_q, BLOCK, heads_here, HEAD_DIM)
    key_grid = key_blocks.reshape(count_q, slot_count * BLOCK, heads_here, HEAD_DIM)
    value_grid = value_blocks.reshape(count_q, slot_count * BLOCK, heads_here, HEAD_DIM)
    scores = jnp.einsum(
        "bqhd,bshd->bhqs", query_grid, key_grid, preferred_element_type=jnp.float32
    ) * (1.0 / math.sqrt(HEAD_DIM))
    present = jnp.repeat(jnp.transpose(valid_slots, (0, 2, 1)), BLOCK, axis=2)[:, :, None, :]
    scores = jnp.where(present, scores, masked_score)
    peak = jnp.max(scores, axis=3, keepdims=True)
    expo = jnp.exp(scores - peak)
    total = jnp.sum(expo, axis=3)
    weights = expo.astype(jnp.bfloat16)
    mixture = jnp.einsum("bhqs,bshd->bqhd", weights, value_grid, preferred_element_type=jnp.float32)
    mixture = mixture / jnp.transpose(total, (0, 2, 1))[..., None]
    return mixture.reshape(count_q, BLOCK, heads_here * HEAD_DIM).astype(jnp.bfloat16)


def xor_perm(count, bit):
    return [(i, i ^ bit) for i in range(count)]


def tree_reduce(parts, merge, axis):
    count = lax.axis_size(axis)
    place = lax.axis_index(axis)
    bits = []
    bit = 1
    while bit < count:
        bits.append(bit)
        bit *= 2
    for bit in bits:
        upper = (place // bit) % 2
        halves = jax.tree.map(lambda x: x.reshape((2, x.shape[0] // 2) + x.shape[1:]), parts)
        keep = jax.tree.map(lambda h: lax.dynamic_index_in_dim(h, upper, 0, keepdims=False), halves)
        send = jax.tree.map(lambda h: lax.dynamic_index_in_dim(h, 1 - upper, 0, keepdims=False), halves)
        got = lax.ppermute(send, axis, xor_perm(count, bit))
        parts = merge(keep, got)
    for bit in reversed(bits):
        upper = (place // bit) % 2
        got = lax.ppermute(parts, axis, xor_perm(count, bit))

        def join(mine, theirs):
            pair = jnp.stack([mine, theirs])
            first = lax.dynamic_index_in_dim(pair, upper, 0, keepdims=False)
            second = lax.dynamic_index_in_dim(pair, 1 - upper, 0, keepdims=False)
            return jnp.concatenate([first, second], axis=0)

        parts = jax.tree.map(join, parts, got)
    return parts


def add_merge(a, b):
    return jax.tree.map(jnp.add, a, b)


def softmax_merge(a, b):
    width = a.shape[1] - 128
    heads = width // HEAD_DIM
    peak_a = a[:, width + heads : width + 2 * heads]
    peak_b = b[:, width + heads : width + 2 * heads]
    peak = jnp.maximum(peak_a, peak_b)
    scale_a = jnp.exp(peak_a - peak)
    scale_b = jnp.exp(peak_b - peak)
    rows = a.shape[0]
    mix = (
        a[:, :width].reshape(rows, heads, HEAD_DIM) * scale_a[..., None]
        + b[:, :width].reshape(rows, heads, HEAD_DIM) * scale_b[..., None]
    ).reshape(rows, width)
    total = a[:, width : width + heads] * scale_a + b[:, width : width + heads] * scale_b
    pad = jnp.zeros((rows, 128 - 2 * heads), a.dtype)
    return jnp.concatenate([mix, total, peak, pad], axis=1)


def head_partials(rows, out_weight):
    head_count = lax.axis_size("head")
    partial = lax.dot_general(
        out_weight, rows, (((0,), (1,)), ((), ())), preferred_element_type=jnp.float32
    ).astype(jnp.bfloat16)
    return partial.reshape(head_count, out_weight.shape[1] // head_count, rows.shape[0])


def sum_over_head(partial):
    gathered = lax.all_to_all(partial, "head", 0, 0, tiled=True)
    return jnp.sum(gathered.astype(jnp.float32), axis=0).T


def partial_attend(query_blocks, key_blocks, value_blocks, valid_slots):
    count_q, slot_count = (key_blocks.shape[0], key_blocks.shape[1])
    heads_here = query_blocks.shape[-1] // HEAD_DIM
    query_grid = query_blocks.reshape(count_q, BLOCK, heads_here, HEAD_DIM)
    key_grid = key_blocks.reshape(count_q, slot_count * BLOCK, heads_here, HEAD_DIM)
    value_grid = value_blocks.reshape(count_q, slot_count * BLOCK, heads_here, HEAD_DIM)
    scores = jnp.einsum(
        "bqhd,bshd->bhqs", query_grid, key_grid, preferred_element_type=jnp.float32
    ) * (1.0 / math.sqrt(HEAD_DIM))
    present = jnp.repeat(jnp.transpose(valid_slots, (0, 2, 1)), BLOCK, axis=2)[:, :, None, :]
    scores = jnp.where(present, scores, masked_score)
    peak = jnp.max(scores, axis=3)
    expo = jnp.exp(scores - peak[..., None])
    total = jnp.sum(expo, axis=3)
    mixture = jnp.einsum(
        "bhqs,bshd->bqhd", expo.astype(jnp.bfloat16), value_grid, preferred_element_type=jnp.float32
    )
    return mixture, total, peak


def merge_attend(first, second):
    mix_a, total_a, peak_a = first
    mix_b, total_b, peak_b = second
    peak = jnp.maximum(peak_a, peak_b)
    scale_a = jnp.exp(peak_a - peak)
    scale_b = jnp.exp(peak_b - peak)
    total = total_a * scale_a + total_b * scale_b
    mix = mix_a * jnp.transpose(scale_a, (0, 2, 1))[..., None] + mix_b * jnp.transpose(scale_b, (0, 2, 1))[..., None]
    mix = mix / jnp.transpose(total, (0, 2, 1))[..., None]
    count_q = mix.shape[0]
    return mix.reshape(count_q, BLOCK, -1).astype(jnp.bfloat16)


def on_device(
    queries,
    keys,
    values,
    out_weight,
    global_blocks,
    random_blocks,
    window_blocks,
    yarn_scale,
    yarn_context,
):
    tok_here, width_here = queries.shape
    heads_here = width_here // HEAD_DIM
    blocks_here = tok_here // BLOCK
    seq_count = lax.axis_size("seq")
    seq_place = lax.axis_index("seq")
    block_total = seq_count * blocks_here
    frequency, mscale = yarn_tables(yarn_scale, yarn_context)
    first_row = seq_place * tok_here
    query_rot = rotate(queries, first_row, frequency, mscale)
    key_rot = rotate(keys, first_row, frequency, mscale)
    pair_kv = jnp.stack([key_rot, values])
    padded = padded_2(pair_kv, (("seq", 1),), WMAX * BLOCK)
    padded_blocks = padded.reshape(2, blocks_here + 2 * WMAX, BLOCK, width_here)
    offsets = jnp.arange(-WMAX, WMAX + 1)
    window_ids = seq_place * blocks_here + jnp.arange(blocks_here)[:, None] + offsets[None, :]
    inside = (window_ids >= 0) & (window_ids < block_total)
    reach = jnp.abs(offsets)[None, :, None] <= window_blocks[None, None, :]
    window_valid = inside[:, :, None] & reach
    owner_global = global_blocks // blocks_here
    local_global = jnp.clip(global_blocks - seq_place * blocks_here, 0, blocks_here - 1)
    mine_global = owner_global == seq_place
    query_view = query_rot.reshape(blocks_here, BLOCK, width_here)
    key_view = key_rot.reshape(blocks_here, BLOCK, width_here)
    value_view = values.reshape(blocks_here, BLOCK, width_here)
    picked = jnp.stack([query_view[local_global], key_view[local_global], value_view[local_global]])
    masked = jnp.where(mine_global[None, :, None, None], picked, jnp.zeros_like(picked))
    shared = tree_reduce(masked.reshape(3 * GLOB * BLOCK, width_here), add_merge, "seq")
    shared = shared.reshape(3, GLOB, BLOCK, width_here)
    slot_parts = [
        padded_blocks[:, offset_slot : offset_slot + blocks_here][:, :, None]
        for offset_slot in range(2 * WMAX + 1)
    ]
    slot_parts.append(
        jnp.broadcast_to(shared[1:3][:, None], (2, blocks_here, GLOB, BLOCK, width_here))
    )
    near_kv = jnp.concatenate(slot_parts, axis=2)
    near_valid = jnp.concatenate(
        [window_valid, jnp.ones((blocks_here, GLOB, heads_here), dtype=bool)], axis=1
    )
    global_query = shared[0]
    key_later = key_rot
    value_later = values
    global_query = global_query.reshape(GLOB, BLOCK, heads_here, HEAD_DIM)
    key_grid = key_later.reshape(tok_here, heads_here, HEAD_DIM)
    value_grid = value_later.reshape(tok_here, heads_here, HEAD_DIM)
    global_scores = jnp.einsum(
        "gqhd,khd->gqhk", global_query, key_grid, preferred_element_type=jnp.float32
    ) * (1.0 / math.sqrt(HEAD_DIM))
    local_peak = jnp.max(global_scores, axis=3)
    expo = jnp.exp(global_scores - local_peak[..., None])
    partial_total = jnp.sum(expo, axis=3)
    partial_mix = jnp.einsum(
        "gqhk,khd->gqhd", expo.astype(jnp.bfloat16), value_grid, preferred_element_type=jnp.float32
    )
    row_total = GLOB * BLOCK
    packed = jnp.concatenate(
        [
            partial_mix.reshape(row_total, width_here),
            partial_total.reshape(row_total, heads_here),
            local_peak.reshape(row_total, heads_here),
            jnp.zeros((row_total, 128 - 2 * heads_here), jnp.float32),
        ],
        axis=1,
    )
    reduced = tree_reduce(packed, softmax_merge, "seq")
    slot_total = blocks_here * RAND
    capacity = (slot_total + seq_count - 1) // seq_count
    flat_ids = random_blocks.reshape(seq_count, slot_total)
    owners = flat_ids // blocks_here
    slot_order = jnp.arange(slot_total)
    same_owner = (owners[:, :, None] == owners[:, None, :]) & (
        slot_order[None, None, :] < slot_order[None, :, None]
    )
    ranks = jnp.sum(same_owner.astype(jnp.int32), axis=2)
    local_ids = flat_ids - owners * blocks_here
    wanted = (owners[:, None, :] == seq_place) & (
        ranks[:, None, :] == jnp.arange(capacity)[None, :, None]
    )
    send_local = jnp.sum(jnp.where(wanted, local_ids[:, None, :], 0), axis=2)
    kv_blocks = pair_kv.reshape(2, blocks_here, BLOCK, width_here)
    outgoing = kv_blocks[:, send_local]
    outgoing, reduced = lax.optimization_barrier((outgoing, reduced))
    incoming = lax.all_to_all(outgoing, "seq", split_axis=1, concat_axis=1, tiled=True)
    my_owners = owners[seq_place]
    my_ranks = ranks[seq_place]
    random_kv = incoming[:, my_owners, my_ranks].reshape(2, blocks_here, RAND, BLOCK, width_here)
    near_part = partial_attend(query_view, near_kv[0], near_kv[1], near_valid)
    far_part = partial_attend(
        query_view, random_kv[0], random_kv[1], jnp.ones((blocks_here, RAND, heads_here), dtype=bool)
    )
    attended = merge_attend(near_part, far_part)
    mix_sum = reduced[:, :width_here].reshape(row_total, heads_here, HEAD_DIM)
    total_sum = reduced[:, width_here : width_here + heads_here]
    global_out = (mix_sum / total_sum[..., None]).reshape(row_total, width_here).astype(jnp.bfloat16)
    global_out = global_out.reshape(GLOB, BLOCK, width_here)
    block_index = jnp.arange(blocks_here)
    for global_slot in range(GLOB):
        hit = mine_global[global_slot] & (block_index == local_global[global_slot])
        attended = jnp.where(hit[:, None, None], global_out[global_slot][None], attended)
    mixed = sum_over_head(head_partials(attended.reshape(tok_here, width_here), out_weight))
    return mixed.astype(jnp.bfloat16)


def solution(mesh):
    in_specs = (
        P("seq", "head"),
        P("seq", "head"),
        P("seq", "head"),
        P("head", None),
        P(),
        P(),
        P("head"),
        P(),
        P(),
    )
    out_specs = P("seq", "head")
    return jax.shard_map(
        on_device, mesh=mesh, in_specs=in_specs, out_specs=out_specs, check_vma=False
    )
```

```python
import math

import jax
import jax.numpy as jnp
from jax import lax
from jax.sharding import PartitionSpec as P

HEAD_DIM = 128
BLOCK = 64
GLOB = 2
RAND = 3
WMAX = 2


masked_score = -1e30


def padded_2(cells, sides, width):
    for axis, dim in sides:
        count = lax.axis_size(axis)
        ends = count - 1
        head = lax.slice_in_dim(cells, 0, width, axis=dim)
        tail = lax.slice_in_dim(cells, cells.shape[dim] - width, cells.shape[dim], axis=dim)
        cells = jnp.concatenate(
            [
                lax.ppermute(tail, axis, [(i, (i + 1) % count) for i in range(ends)]),
                cells,
                lax.ppermute(head, axis, [((i + 1) % count, i) for i in range(ends)]),
            ],
            axis=dim,
        )
    return cells


def yarn_tables(yarn_scale, yarn_context):
    half_dim = HEAD_DIM // 2
    pair_index = jnp.arange(half_dim).astype(jnp.float32)
    base_rate = 10000.0 ** (-2.0 * pair_index / HEAD_DIM)
    factor = yarn_scale[0].astype(jnp.float32)
    context = yarn_context[0].astype(jnp.float32)
    turn_ratio = context * base_rate / (2.0 * math.pi)
    ramp_weight = jnp.clip((turn_ratio - 1.0) / 31.0, 0.0, 1.0)
    frequency = base_rate * ((1.0 - ramp_weight) / factor + ramp_weight)
    mscale = 0.1 * jnp.log(factor) + 1.0
    return (frequency, mscale)


def rotate(source, first_row, frequency, mscale):
    row_count, row_width = source.shape
    half_dim = HEAD_DIM // 2
    position = (first_row + jnp.arange(row_count)).astype(jnp.float32)
    angle_table = position[:, None] * frequency[None, :]
    cosine = jnp.cos(angle_table)[:, None, :] * mscale
    sine_part = jnp.sin(angle_table)[:, None, :] * mscale
    halves_view = source.astype(jnp.float32).reshape(row_count, row_width // HEAD_DIM, 2, half_dim)
    lower_half = halves_view[:, :, 0]
    upper_half = halves_view[:, :, 1]
    turned = jnp.stack(
        [
            lower_half * cosine - upper_half * sine_part,
            upper_half * cosine + lower_half * sine_part,
        ],
        axis=2,
    )
    return turned.reshape(row_count, row_width).astype(jnp.bfloat16)


def block_attend(query_blocks, key_blocks, value_blocks, valid_slots):
    count_q, slot_count = (key_blocks.shape[0], key_blocks.shape[1])
    heads_here = query_blocks.shape[-1] // HEAD_DIM
    query_grid = query_blocks.reshape(count_q, BLOCK, heads_here, HEAD_DIM)
    key_grid = key_blocks.reshape(count_q, slot_count * BLOCK, heads_here, HEAD_DIM)
    value_grid = value_blocks.reshape(count_q, slot_count * BLOCK, heads_here, HEAD_DIM)
    scores = jnp.einsum(
        "bqhd,bshd->bhqs", query_grid, key_grid, preferred_element_type=jnp.float32
    ) * (1.0 / math.sqrt(HEAD_DIM))
    present = jnp.repeat(jnp.transpose(valid_slots, (0, 2, 1)), BLOCK, axis=2)[:, :, None, :]
    scores = jnp.where(present, scores, masked_score)
    peak = jnp.max(scores, axis=3, keepdims=True)
    expo = jnp.exp(scores - peak)
    total = jnp.sum(expo, axis=3)
    weights = expo.astype(jnp.bfloat16)
    mixture = jnp.einsum("bhqs,bshd->bqhd", weights, value_grid, preferred_element_type=jnp.float32)
    mixture = mixture / jnp.transpose(total, (0, 2, 1))[..., None]
    return mixture.reshape(count_q, BLOCK, heads_here * HEAD_DIM).astype(jnp.bfloat16)


def xor_perm(count, bit):
    return [(i, i ^ bit) for i in range(count)]


def tree_reduce(parts, merge, axis):
    count = lax.axis_size(axis)
    place = lax.axis_index(axis)
    bits = []
    bit = 1
    while bit < count:
        bits.append(bit)
        bit *= 2
    for bit in bits:
        upper = (place // bit) % 2
        halves = jax.tree.map(lambda x: x.reshape((2, x.shape[0] // 2) + x.shape[1:]), parts)
        keep = jax.tree.map(lambda h: lax.dynamic_index_in_dim(h, upper, 0, keepdims=False), halves)
        send = jax.tree.map(lambda h: lax.dynamic_index_in_dim(h, 1 - upper, 0, keepdims=False), halves)
        got = lax.ppermute(send, axis, xor_perm(count, bit))
        parts = merge(keep, got)
    for bit in reversed(bits):
        upper = (place // bit) % 2
        got = lax.ppermute(parts, axis, xor_perm(count, bit))

        def join(mine, theirs):
            pair = jnp.stack([mine, theirs])
            first = lax.dynamic_index_in_dim(pair, upper, 0, keepdims=False)
            second = lax.dynamic_index_in_dim(pair, 1 - upper, 0, keepdims=False)
            return jnp.concatenate([first, second], axis=0)

        parts = jax.tree.map(join, parts, got)
    return parts


def add_merge(a, b):
    return jax.tree.map(jnp.add, a, b)


def softmax_merge(a, b):
    width = a.shape[1] - 128
    heads = width // HEAD_DIM
    peak_a = a[:, width + heads : width + 2 * heads]
    peak_b = b[:, width + heads : width + 2 * heads]
    peak = jnp.maximum(peak_a, peak_b)
    scale_a = jnp.exp(peak_a - peak)
    scale_b = jnp.exp(peak_b - peak)
    rows = a.shape[0]
    mix = (
        a[:, :width].reshape(rows, heads, HEAD_DIM) * scale_a[..., None]
        + b[:, :width].reshape(rows, heads, HEAD_DIM) * scale_b[..., None]
    ).reshape(rows, width)
    total = a[:, width : width + heads] * scale_a + b[:, width : width + heads] * scale_b
    pad = jnp.zeros((rows, 128 - 2 * heads), a.dtype)
    return jnp.concatenate([mix, total, peak, pad], axis=1)


def head_partials(rows, out_weight):
    head_count = lax.axis_size("head")
    partial = lax.dot_general(
        out_weight, rows, (((0,), (1,)), ((), ())), preferred_element_type=jnp.float32
    ).astype(jnp.bfloat16)
    return partial.reshape(head_count, out_weight.shape[1] // head_count, rows.shape[0])


def sum_over_head(partial):
    gathered = lax.all_to_all(partial, "head", 0, 0, tiled=True)
    return jnp.sum(gathered.astype(jnp.float32), axis=0).T


def partial_attend(query_blocks, key_blocks, value_blocks, valid_slots):
    count_q, slot_count = (key_blocks.shape[0], key_blocks.shape[1])
    heads_here = query_blocks.shape[-1] // HEAD_DIM
    query_grid = query_blocks.reshape(count_q, BLOCK, heads_here, HEAD_DIM)
    key_grid = key_blocks.reshape(count_q, slot_count * BLOCK, heads_here, HEAD_DIM)
    value_grid = value_blocks.reshape(count_q, slot_count * BLOCK, heads_here, HEAD_DIM)
    scores = jnp.einsum(
        "bqhd,bshd->bhqs", query_grid, key_grid, preferred_element_type=jnp.float32
    ) * (1.0 / math.sqrt(HEAD_DIM))
    present = jnp.repeat(jnp.transpose(valid_slots, (0, 2, 1)), BLOCK, axis=2)[:, :, None, :]
    scores = jnp.where(present, scores, masked_score)
    peak = jnp.max(scores, axis=3)
    expo = jnp.exp(scores - peak[..., None])
    total = jnp.sum(expo, axis=3)
    mixture = jnp.einsum(
        "bhqs,bshd->bqhd", expo.astype(jnp.bfloat16), value_grid, preferred_element_type=jnp.float32
    )
    return mixture, total, peak


def merge_attend(first, second):
    mix_a, total_a, peak_a = first
    mix_b, total_b, peak_b = second
    peak = jnp.maximum(peak_a, peak_b)
    scale_a = jnp.exp(peak_a - peak)
    scale_b = jnp.exp(peak_b - peak)
    total = total_a * scale_a + total_b * scale_b
    mix = mix_a * jnp.transpose(scale_a, (0, 2, 1))[..., None] + mix_b * jnp.transpose(scale_b, (0, 2, 1))[..., None]
    mix = mix / jnp.transpose(total, (0, 2, 1))[..., None]
    count_q = mix.shape[0]
    return mix.reshape(count_q, BLOCK, -1).astype(jnp.bfloat16)


def on_device(
    queries,
    keys,
    values,
    out_weight,
    global_blocks,
    random_blocks,
    window_blocks,
    yarn_scale,
    yarn_context,
):
    tok_here, width_here = queries.shape
    heads_here = width_here // HEAD_DIM
    blocks_here = tok_here // BLOCK
    seq_count = lax.axis_size("seq")
    seq_place = lax.axis_index("seq")
    block_total = seq_count * blocks_here
    frequency, mscale = yarn_tables(yarn_scale, yarn_context)
    first_row = seq_place * tok_here
    query_rot = rotate(queries, first_row, frequency, mscale)
    key_rot = rotate(keys, first_row, frequency, mscale)
    pair_kv = jnp.stack([key_rot, values])
    padded = padded_2(pair_kv, (("seq", 1),), WMAX * BLOCK)
    padded_blocks = padded.reshape(2, blocks_here + 2 * WMAX, BLOCK, width_here)
    offsets = jnp.arange(-WMAX, WMAX + 1)
    window_ids = seq_place * blocks_here + jnp.arange(blocks_here)[:, None] + offsets[None, :]
    inside = (window_ids >= 0) & (window_ids < block_total)
    reach = jnp.abs(offsets)[None, :, None] <= window_blocks[None, None, :]
    window_valid = inside[:, :, None] & reach
    owner_global = global_blocks // blocks_here
    local_global = jnp.clip(global_blocks - seq_place * blocks_here, 0, blocks_here - 1)
    mine_global = owner_global == seq_place
    query_view = query_rot.reshape(blocks_here, BLOCK, width_here)
    key_view = key_rot.reshape(blocks_here, BLOCK, width_here)
    value_view = values.reshape(blocks_here, BLOCK, width_here)
    picked = jnp.stack([query_view[local_global], key_view[local_global], value_view[local_global]])
    masked = jnp.where(mine_global[None, :, None, None], picked, jnp.zeros_like(picked))
    shared = tree_reduce(masked.reshape(3 * GLOB * BLOCK, width_here), add_merge, "seq")
    shared = shared.reshape(3, GLOB, BLOCK, width_here)
    slot_parts = [
        padded_blocks[:, offset_slot : offset_slot + blocks_here][:, :, None]
        for offset_slot in range(2 * WMAX + 1)
    ]
    slot_parts.append(
        jnp.broadcast_to(shared[1:3][:, None], (2, blocks_here, GLOB, BLOCK, width_here))
    )
    near_kv = jnp.concatenate(slot_parts, axis=2)
    near_valid = jnp.concatenate(
        [window_valid, jnp.ones((blocks_here, GLOB, heads_here), dtype=bool)], axis=1
    )
    global_query = shared[0]
    key_later = key_rot
    value_later = values
    global_query = global_query.reshape(GLOB, BLOCK, heads_here, HEAD_DIM)
    key_grid = key_later.reshape(tok_here, heads_here, HEAD_DIM)
    value_grid = value_later.reshape(tok_here, heads_here, HEAD_DIM)
    global_scores = jnp.einsum(
        "gqhd,khd->gqhk", global_query, key_grid, preferred_element_type=jnp.float32
    ) * (1.0 / math.sqrt(HEAD_DIM))
    peak = lax.pmax(jnp.max(global_scores, axis=3), "seq")
    expo = jnp.exp(global_scores - peak[..., None])
    partial_total = jnp.sum(expo, axis=3)
    partial_mix = jnp.einsum(
        "gqhk,khd->gqhd", expo.astype(jnp.bfloat16), value_grid, preferred_element_type=jnp.float32
    )
    row_total = GLOB * BLOCK
    packed = jnp.concatenate(
        [
            partial_mix.reshape(row_total, width_here),
            partial_total.reshape(row_total, heads_here),
            jnp.zeros((row_total, 128 - heads_here), jnp.float32),
        ],
        axis=1,
    )
    reduced = lax.psum(packed, "seq")
    slot_total = blocks_here * RAND
    capacity = (slot_total + seq_count - 1) // seq_count
    flat_ids = random_blocks.reshape(seq_count, slot_total)
    owners = flat_ids // blocks_here
    slot_order = jnp.arange(slot_total)
    same_owner = (owners[:, :, None] == owners[:, None, :]) & (
        slot_order[None, None, :] < slot_order[None, :, None]
    )
    ranks = jnp.sum(same_owner.astype(jnp.int32), axis=2)
    local_ids = flat_ids - owners * blocks_here
    wanted = (owners[:, None, :] == seq_place) & (
        ranks[:, None, :] == jnp.arange(capacity)[None, :, None]
    )
    send_local = jnp.sum(jnp.where(wanted, local_ids[:, None, :], 0), axis=2)
    kv_blocks = pair_kv.reshape(2, blocks_here, BLOCK, width_here)
    outgoing = kv_blocks[:, send_local]
    outgoing, shared = lax.optimization_barrier((outgoing, shared))
    incoming = lax.all_to_all(outgoing, "seq", split_axis=1, concat_axis=1, tiled=True)
    my_owners = owners[seq_place]
    my_ranks = ranks[seq_place]
    random_kv = incoming[:, my_owners, my_ranks].reshape(2, blocks_here, RAND, BLOCK, width_here)
    near_part = partial_attend(query_view, near_kv[0], near_kv[1], near_valid)
    far_part = partial_attend(
        query_view, random_kv[0], random_kv[1], jnp.ones((blocks_here, RAND, heads_here), dtype=bool)
    )
    attended = merge_attend(near_part, far_part)
    mix_sum = reduced[:, :width_here].reshape(row_total, heads_here, HEAD_DIM)
    total_sum = reduced[:, width_here : width_here + heads_here]
    global_out = (mix_sum / total_sum[..., None]).reshape(row_total, width_here).astype(jnp.bfloat16)
    mixed = sum_over_head(head_partials(attended.reshape(tok_here, width_here), out_weight))
    global_mixed = sum_over_head(head_partials(global_out, out_weight)).reshape(GLOB, BLOCK, -1)
    mixed = mixed.reshape(blocks_here, BLOCK, -1)
    block_index = jnp.arange(blocks_here)
    for global_slot in range(GLOB):
        hit = mine_global[global_slot] & (block_index == local_global[global_slot])
        mixed = jnp.where(hit[:, None, None], global_mixed[global_slot][None], mixed)
    return mixed.reshape(tok_here, -1).astype(jnp.bfloat16)


def solution(mesh):
    in_specs = (
        P("seq", "head"),
        P("seq", "head"),
        P("seq", "head"),
        P("head", None),
        P(),
        P(),
        P("head"),
        P(),
        P(),
    )
    out_specs = P("seq", "head")
    return jax.shard_map(
        on_device, mesh=mesh, in_specs=in_specs, out_specs=out_specs, check_vma=False
    )
```

```python
import math

import jax
import jax.numpy as jnp
from jax import lax
from jax.sharding import PartitionSpec as P

HEAD_DIM = 128
BLOCK = 64
GLOB = 2
RAND = 3
WMAX = 2


masked_score = -1e30


def padded_2(cells, sides, width):
    for axis, dim in sides:
        count = lax.axis_size(axis)
        ends = count - 1
        head = lax.slice_in_dim(cells, 0, width, axis=dim)
        tail = lax.slice_in_dim(cells, cells.shape[dim] - width, cells.shape[dim], axis=dim)
        cells = jnp.concatenate(
            [
                lax.ppermute(tail, axis, [(i, (i + 1) % count) for i in range(ends)]),
                cells,
                lax.ppermute(head, axis, [((i + 1) % count, i) for i in range(ends)]),
            ],
            axis=dim,
        )
    return cells


def yarn_tables(yarn_scale, yarn_context):
    half_dim = HEAD_DIM // 2
    pair_index = jnp.arange(half_dim).astype(jnp.float32)
    base_rate = 10000.0 ** (-2.0 * pair_index / HEAD_DIM)
    factor = yarn_scale[0].astype(jnp.float32)
    context = yarn_context[0].astype(jnp.float32)
    turn_ratio = context * base_rate / (2.0 * math.pi)
    ramp_weight = jnp.clip((turn_ratio - 1.0) / 31.0, 0.0, 1.0)
    frequency = base_rate * ((1.0 - ramp_weight) / factor + ramp_weight)
    mscale = 0.1 * jnp.log(factor) + 1.0
    return (frequency, mscale)


def rotate(source, first_row, frequency, mscale):
    row_count, row_width = source.shape
    half_dim = HEAD_DIM // 2
    position = (first_row + jnp.arange(row_count)).astype(jnp.float32)
    angle_table = position[:, None] * frequency[None, :]
    cosine = jnp.cos(angle_table)[:, None, :] * mscale
    sine_part = jnp.sin(angle_table)[:, None, :] * mscale
    halves_view = source.astype(jnp.float32).reshape(row_count, row_width // HEAD_DIM, 2, half_dim)
    lower_half = halves_view[:, :, 0]
    upper_half = halves_view[:, :, 1]
    turned = jnp.stack(
        [
            lower_half * cosine - upper_half * sine_part,
            upper_half * cosine + lower_half * sine_part,
        ],
        axis=2,
    )
    return turned.reshape(row_count, row_width).astype(jnp.bfloat16)


def block_attend(query_blocks, key_blocks, value_blocks, valid_slots):
    count_q, slot_count = (key_blocks.shape[0], key_blocks.shape[1])
    heads_here = query_blocks.shape[-1] // HEAD_DIM
    query_grid = query_blocks.reshape(count_q, BLOCK, heads_here, HEAD_DIM)
    key_grid = key_blocks.reshape(count_q, slot_count * BLOCK, heads_here, HEAD_DIM)
    value_grid = value_blocks.reshape(count_q, slot_count * BLOCK, heads_here, HEAD_DIM)
    scores = jnp.einsum(
        "bqhd,bshd->bhqs", query_grid, key_grid, preferred_element_type=jnp.float32
    ) * (1.0 / math.sqrt(HEAD_DIM))
    present = jnp.repeat(jnp.transpose(valid_slots, (0, 2, 1)), BLOCK, axis=2)[:, :, None, :]
    scores = jnp.where(present, scores, masked_score)
    peak = jnp.max(scores, axis=3, keepdims=True)
    expo = jnp.exp(scores - peak)
    total = jnp.sum(expo, axis=3)
    weights = expo.astype(jnp.bfloat16)
    mixture = jnp.einsum("bhqs,bshd->bqhd", weights, value_grid, preferred_element_type=jnp.float32)
    mixture = mixture / jnp.transpose(total, (0, 2, 1))[..., None]
    return mixture.reshape(count_q, BLOCK, heads_here * HEAD_DIM).astype(jnp.bfloat16)


def xor_perm(count, bit):
    return [(i, i ^ bit) for i in range(count)]


def tree_reduce(parts, merge, axis):
    count = lax.axis_size(axis)
    place = lax.axis_index(axis)
    bits = []
    bit = 1
    while bit < count:
        bits.append(bit)
        bit *= 2
    for bit in bits:
        upper = (place // bit) % 2
        halves = jax.tree.map(lambda x: x.reshape((2, x.shape[0] // 2) + x.shape[1:]), parts)
        keep = jax.tree.map(lambda h: lax.dynamic_index_in_dim(h, upper, 0, keepdims=False), halves)
        send = jax.tree.map(lambda h: lax.dynamic_index_in_dim(h, 1 - upper, 0, keepdims=False), halves)
        got = lax.ppermute(send, axis, xor_perm(count, bit))
        parts = merge(keep, got)
    for bit in reversed(bits):
        upper = (place // bit) % 2
        got = lax.ppermute(parts, axis, xor_perm(count, bit))

        def join(mine, theirs):
            pair = jnp.stack([mine, theirs])
            first = lax.dynamic_index_in_dim(pair, upper, 0, keepdims=False)
            second = lax.dynamic_index_in_dim(pair, 1 - upper, 0, keepdims=False)
            return jnp.concatenate([first, second], axis=0)

        parts = jax.tree.map(join, parts, got)
    return parts


def add_merge(a, b):
    return jax.tree.map(jnp.add, a, b)


def softmax_merge(a, b):
    width = a.shape[1] - 128
    heads = width // HEAD_DIM
    peak_a = a[:, width + heads : width + 2 * heads]
    peak_b = b[:, width + heads : width + 2 * heads]
    peak = jnp.maximum(peak_a, peak_b)
    scale_a = jnp.exp(peak_a - peak)
    scale_b = jnp.exp(peak_b - peak)
    rows = a.shape[0]
    mix = (
        a[:, :width].reshape(rows, heads, HEAD_DIM) * scale_a[..., None]
        + b[:, :width].reshape(rows, heads, HEAD_DIM) * scale_b[..., None]
    ).reshape(rows, width)
    total = a[:, width : width + heads] * scale_a + b[:, width : width + heads] * scale_b
    pad = jnp.zeros((rows, 128 - 2 * heads), a.dtype)
    return jnp.concatenate([mix, total, peak, pad], axis=1)


def head_partials(rows, out_weight):
    head_count = lax.axis_size("head")
    partial = lax.dot_general(
        out_weight, rows, (((0,), (1,)), ((), ())), preferred_element_type=jnp.float32
    ).astype(jnp.bfloat16)
    return partial.reshape(head_count, out_weight.shape[1] // head_count, rows.shape[0])


def sum_over_head(partial):
    gathered = lax.all_to_all(partial, "head", 0, 0, tiled=True)
    return jnp.sum(gathered.astype(jnp.float32), axis=0).T


def partial_attend(query_blocks, key_blocks, value_blocks, valid_slots):
    count_q, slot_count = (key_blocks.shape[0], key_blocks.shape[1])
    heads_here = query_blocks.shape[-1] // HEAD_DIM
    query_grid = query_blocks.reshape(count_q, BLOCK, heads_here, HEAD_DIM)
    key_grid = key_blocks.reshape(count_q, slot_count * BLOCK, heads_here, HEAD_DIM)
    value_grid = value_blocks.reshape(count_q, slot_count * BLOCK, heads_here, HEAD_DIM)
    scores = jnp.einsum(
        "bqhd,bshd->bhqs", query_grid, key_grid, preferred_element_type=jnp.float32
    ) * (1.0 / math.sqrt(HEAD_DIM))
    present = jnp.repeat(jnp.transpose(valid_slots, (0, 2, 1)), BLOCK, axis=2)[:, :, None, :]
    scores = jnp.where(present, scores, masked_score)
    peak = jnp.max(scores, axis=3)
    expo = jnp.exp(scores - peak[..., None])
    total = jnp.sum(expo, axis=3)
    mixture = jnp.einsum(
        "bhqs,bshd->bqhd", expo.astype(jnp.bfloat16), value_grid, preferred_element_type=jnp.float32
    )
    return mixture, total, peak


def merge_attend(first, second):
    mix_a, total_a, peak_a = first
    mix_b, total_b, peak_b = second
    peak = jnp.maximum(peak_a, peak_b)
    scale_a = jnp.exp(peak_a - peak)
    scale_b = jnp.exp(peak_b - peak)
    total = total_a * scale_a + total_b * scale_b
    mix = mix_a * jnp.transpose(scale_a, (0, 2, 1))[..., None] + mix_b * jnp.transpose(scale_b, (0, 2, 1))[..., None]
    mix = mix / jnp.transpose(total, (0, 2, 1))[..., None]
    count_q = mix.shape[0]
    return mix.reshape(count_q, BLOCK, -1).astype(jnp.bfloat16)


def on_device(
    queries,
    keys,
    values,
    out_weight,
    global_blocks,
    random_blocks,
    window_blocks,
    yarn_scale,
    yarn_context,
):
    tok_here, width_here = queries.shape
    heads_here = width_here // HEAD_DIM
    blocks_here = tok_here // BLOCK
    seq_count = lax.axis_size("seq")
    seq_place = lax.axis_index("seq")
    block_total = seq_count * blocks_here
    frequency, mscale = yarn_tables(yarn_scale, yarn_context)
    first_row = seq_place * tok_here
    query_rot = rotate(queries, first_row, frequency, mscale)
    key_rot = rotate(keys, first_row, frequency, mscale)
    pair_kv = jnp.stack([key_rot, values])
    halo = WMAX * BLOCK
    seq_ends = seq_count - 1
    from_left = lax.ppermute(
        pair_kv[:, tok_here - halo :], "seq", [(i, (i + 1) % seq_count) for i in range(seq_ends)]
    ).reshape(2, WMAX, BLOCK, width_here)
    from_right = lax.ppermute(
        pair_kv[:, :halo], "seq", [((i + 1) % seq_count, i) for i in range(seq_ends)]
    ).reshape(2, WMAX, BLOCK, width_here)
    local_blocks = pair_kv.reshape(2, blocks_here, BLOCK, width_here)

    def padded_block(index):
        if index < WMAX:
            return from_left[:, index]
        if index < WMAX + blocks_here:
            return local_blocks[:, index - WMAX]
        return from_right[:, index - WMAX - blocks_here]

    offsets = jnp.arange(-WMAX, WMAX + 1)
    window_ids = seq_place * blocks_here + jnp.arange(blocks_here)[:, None] + offsets[None, :]
    inside = (window_ids >= 0) & (window_ids < block_total)
    reach = jnp.abs(offsets)[None, :, None] <= window_blocks[None, None, :]
    window_valid = inside[:, :, None] & reach
    owner_global = global_blocks // blocks_here
    local_global = jnp.clip(global_blocks - seq_place * blocks_here, 0, blocks_here - 1)
    mine_global = owner_global == seq_place
    query_view = query_rot.reshape(blocks_here, BLOCK, width_here)
    key_view = key_rot.reshape(blocks_here, BLOCK, width_here)
    value_view = values.reshape(blocks_here, BLOCK, width_here)
    picked = jnp.stack([query_view[local_global], key_view[local_global], value_view[local_global]])
    masked = jnp.where(mine_global[None, :, None, None], picked, jnp.zeros_like(picked))
    shared = tree_reduce(masked.reshape(3 * GLOB * BLOCK, width_here), add_merge, "seq")
    shared = shared.reshape(3, GLOB, BLOCK, width_here)
    slot_parts = [
        jnp.stack(
            [padded_block(block + offset_slot) for offset_slot in range(2 * WMAX + 1)], axis=1
        )
        for block in range(blocks_here)
    ]
    global_kv = jnp.broadcast_to(shared[1:3][:, None], (2, blocks_here, GLOB, BLOCK, width_here))
    near_kv = jnp.concatenate([jnp.stack(slot_parts, axis=1), global_kv], axis=2)
    near_valid = jnp.concatenate(
        [window_valid, jnp.ones((blocks_here, GLOB, heads_here), dtype=bool)], axis=1
    )
    global_query = shared[0]
    key_later = key_rot
    value_later = values
    global_query = global_query.reshape(GLOB, BLOCK, heads_here, HEAD_DIM)
    key_grid = key_later.reshape(tok_here, heads_here, HEAD_DIM)
    value_grid = value_later.reshape(tok_here, heads_here, HEAD_DIM)
    global_scores = jnp.einsum(
        "gqhd,khd->gqhk", global_query, key_grid, preferred_element_type=jnp.float32
    ) * (1.0 / math.sqrt(HEAD_DIM))
    local_peak = jnp.max(global_scores, axis=3)
    expo = jnp.exp(global_scores - local_peak[..., None])
    partial_total = jnp.sum(expo, axis=3)
    partial_mix = jnp.einsum(
        "gqhk,khd->gqhd", expo.astype(jnp.bfloat16), value_grid, preferred_element_type=jnp.float32
    )
    row_total = GLOB * BLOCK
    packed = jnp.concatenate(
        [
            partial_mix.reshape(row_total, width_here),
            partial_total.reshape(row_total, heads_here),
            local_peak.reshape(row_total, heads_here),
            jnp.zeros((row_total, 128 - 2 * heads_here), jnp.float32),
        ],
        axis=1,
    )
    reduced = tree_reduce(packed, softmax_merge, "seq")
    slot_total = blocks_here * RAND
    capacity = (slot_total + seq_count - 1) // seq_count
    flat_ids = random_blocks.reshape(seq_count, slot_total)
    owners = flat_ids // blocks_here
    slot_order = jnp.arange(slot_total)
    same_owner = (owners[:, :, None] == owners[:, None, :]) & (
        slot_order[None, None, :] < slot_order[None, :, None]
    )
    ranks = jnp.sum(same_owner.astype(jnp.int32), axis=2)
    local_ids = flat_ids - owners * blocks_here
    wanted = (owners[:, None, :] == seq_place) & (
        ranks[:, None, :] == jnp.arange(capacity)[None, :, None]
    )
    send_local = jnp.sum(jnp.where(wanted, local_ids[:, None, :], 0), axis=2)
    kv_blocks = jnp.stack([key_rot.reshape(blocks_here, BLOCK, width_here), value_view], axis=1)
    outgoing = kv_blocks[send_local]
    outgoing, reduced = lax.optimization_barrier((outgoing, reduced))
    incoming = lax.all_to_all(outgoing, "seq", split_axis=0, concat_axis=0, tiled=True)
    my_owners = owners[seq_place]
    my_ranks = ranks[seq_place]
    random_k = incoming[my_owners, my_ranks, 0].reshape(blocks_here, RAND, BLOCK, width_here)
    random_v = incoming[my_owners, my_ranks, 1].reshape(blocks_here, RAND, BLOCK, width_here)
    random_kv = (random_k, random_v)
    near_part = partial_attend(query_view, near_kv[0], near_kv[1], near_valid)
    far_part = partial_attend(
        query_view, random_kv[0], random_kv[1], jnp.ones((blocks_here, RAND, heads_here), dtype=bool)
    )
    attended = merge_attend(near_part, far_part)
    mix_sum = reduced[:, :width_here].reshape(row_total, heads_here, HEAD_DIM)
    total_sum = reduced[:, width_here : width_here + heads_here]
    global_out = (mix_sum / total_sum[..., None]).reshape(row_total, width_here).astype(jnp.bfloat16)
    global_out = global_out.reshape(GLOB, BLOCK, width_here)
    block_index = jnp.arange(blocks_here)
    for global_slot in range(GLOB):
        hit = mine_global[global_slot] & (block_index == local_global[global_slot])
        attended = jnp.where(hit[:, None, None], global_out[global_slot][None], attended)
    mixed = sum_over_head(head_partials(attended.reshape(tok_here, width_here), out_weight))
    return mixed.astype(jnp.bfloat16)


def solution(mesh):
    in_specs = (
        P("seq", "head"),
        P("seq", "head"),
        P("seq", "head"),
        P("head", None),
        P(),
        P(),
        P("head"),
        P(),
        P(),
    )
    out_specs = P("seq", "head")
    return jax.shard_map(
        on_device, mesh=mesh, in_specs=in_specs, out_specs=out_specs, check_vma=False
    )
```

```python
import math

import jax
import jax.numpy as jnp
from jax import lax
from jax.sharding import PartitionSpec as P

HEAD_DIM = 128
BLOCK = 64
GLOB = 2
RAND = 3
WMAX = 2


masked_score = -1e30


def padded_2(cells, sides, width):
    for axis, dim in sides:
        count = lax.axis_size(axis)
        ends = count - 1
        head = lax.slice_in_dim(cells, 0, width, axis=dim)
        tail = lax.slice_in_dim(cells, cells.shape[dim] - width, cells.shape[dim], axis=dim)
        cells = jnp.concatenate(
            [
                lax.ppermute(tail, axis, [(i, (i + 1) % count) for i in range(ends)]),
                cells,
                lax.ppermute(head, axis, [((i + 1) % count, i) for i in range(ends)]),
            ],
            axis=dim,
        )
    return cells


def yarn_tables(yarn_scale, yarn_context):
    half_dim = HEAD_DIM // 2
    pair_index = jnp.arange(half_dim).astype(jnp.float32)
    base_rate = 10000.0 ** (-2.0 * pair_index / HEAD_DIM)
    factor = yarn_scale[0].astype(jnp.float32)
    context = yarn_context[0].astype(jnp.float32)
    turn_ratio = context * base_rate / (2.0 * math.pi)
    ramp_weight = jnp.clip((turn_ratio - 1.0) / 31.0, 0.0, 1.0)
    frequency = base_rate * ((1.0 - ramp_weight) / factor + ramp_weight)
    mscale = 0.1 * jnp.log(factor) + 1.0
    return (frequency, mscale)


def rotate(source, first_row, frequency, mscale):
    row_count, row_width = source.shape
    half_dim = HEAD_DIM // 2
    position = (first_row + jnp.arange(row_count)).astype(jnp.float32)
    angle_table = position[:, None] * frequency[None, :]
    cosine = jnp.cos(angle_table)[:, None, :] * mscale
    sine_part = jnp.sin(angle_table)[:, None, :] * mscale
    halves_view = source.astype(jnp.float32).reshape(row_count, row_width // HEAD_DIM, 2, half_dim)
    lower_half = halves_view[:, :, 0]
    upper_half = halves_view[:, :, 1]
    turned = jnp.stack(
        [
            lower_half * cosine - upper_half * sine_part,
            upper_half * cosine + lower_half * sine_part,
        ],
        axis=2,
    )
    return turned.reshape(row_count, row_width).astype(jnp.bfloat16)


def block_attend(query_blocks, key_blocks, value_blocks, valid_slots):
    count_q, slot_count = (key_blocks.shape[0], key_blocks.shape[1])
    heads_here = query_blocks.shape[-1] // HEAD_DIM
    query_grid = query_blocks.reshape(count_q, BLOCK, heads_here, HEAD_DIM)
    key_grid = key_blocks.reshape(count_q, slot_count * BLOCK, heads_here, HEAD_DIM)
    value_grid = value_blocks.reshape(count_q, slot_count * BLOCK, heads_here, HEAD_DIM)
    scores = jnp.einsum(
        "bqhd,bshd->bhqs", query_grid, key_grid, preferred_element_type=jnp.float32
    ) * (1.0 / math.sqrt(HEAD_DIM))
    present = jnp.repeat(jnp.transpose(valid_slots, (0, 2, 1)), BLOCK, axis=2)[:, :, None, :]
    scores = jnp.where(present, scores, masked_score)
    peak = jnp.max(scores, axis=3, keepdims=True)
    expo = jnp.exp(scores - peak)
    total = jnp.sum(expo, axis=3)
    weights = expo.astype(jnp.bfloat16)
    mixture = jnp.einsum("bhqs,bshd->bqhd", weights, value_grid, preferred_element_type=jnp.float32)
    mixture = mixture / jnp.transpose(total, (0, 2, 1))[..., None]
    return mixture.reshape(count_q, BLOCK, heads_here * HEAD_DIM).astype(jnp.bfloat16)


def xor_perm(count, bit):
    return [(i, i ^ bit) for i in range(count)]


def tree_reduce(parts, merge, axis):
    count = lax.axis_size(axis)
    place = lax.axis_index(axis)
    bits = []
    bit = 1
    while bit < count:
        bits.append(bit)
        bit *= 2
    for bit in bits:
        upper = (place // bit) % 2
        halves = jax.tree.map(lambda x: x.reshape((2, x.shape[0] // 2) + x.shape[1:]), parts)
        keep = jax.tree.map(lambda h: lax.dynamic_index_in_dim(h, upper, 0, keepdims=False), halves)
        send = jax.tree.map(lambda h: lax.dynamic_index_in_dim(h, 1 - upper, 0, keepdims=False), halves)
        got = lax.ppermute(send, axis, xor_perm(count, bit))
        parts = merge(keep, got)
    for bit in reversed(bits):
        upper = (place // bit) % 2
        got = lax.ppermute(parts, axis, xor_perm(count, bit))

        def join(mine, theirs):
            pair = jnp.stack([mine, theirs])
            first = lax.dynamic_index_in_dim(pair, upper, 0, keepdims=False)
            second = lax.dynamic_index_in_dim(pair, 1 - upper, 0, keepdims=False)
            return jnp.concatenate([first, second], axis=0)

        parts = jax.tree.map(join, parts, got)
    return parts


def add_merge(a, b):
    return jax.tree.map(jnp.add, a, b)


def softmax_merge(a, b):
    width = a.shape[1] - 128
    heads = width // HEAD_DIM
    peak_a = a[:, width + heads : width + 2 * heads]
    peak_b = b[:, width + heads : width + 2 * heads]
    peak = jnp.maximum(peak_a, peak_b)
    scale_a = jnp.exp(peak_a - peak)
    scale_b = jnp.exp(peak_b - peak)
    rows = a.shape[0]
    mix = (
        a[:, :width].reshape(rows, heads, HEAD_DIM) * scale_a[..., None]
        + b[:, :width].reshape(rows, heads, HEAD_DIM) * scale_b[..., None]
    ).reshape(rows, width)
    total = a[:, width : width + heads] * scale_a + b[:, width : width + heads] * scale_b
    pad = jnp.zeros((rows, 128 - 2 * heads), a.dtype)
    return jnp.concatenate([mix, total, peak, pad], axis=1)


def head_partials(rows, out_weight):
    head_count = lax.axis_size("head")
    partial = lax.dot_general(
        out_weight, rows, (((0,), (1,)), ((), ())), preferred_element_type=jnp.float32
    ).astype(jnp.bfloat16)
    return partial.reshape(head_count, out_weight.shape[1] // head_count, rows.shape[0])


def sum_over_head(partial):
    gathered = lax.all_to_all(partial, "head", 0, 0, tiled=True)
    return jnp.sum(gathered.astype(jnp.float32), axis=0).T


def partial_attend(query_blocks, key_blocks, value_blocks, valid_slots):
    count_q, slot_count = (key_blocks.shape[0], key_blocks.shape[1])
    heads_here = query_blocks.shape[-1] // HEAD_DIM
    query_grid = query_blocks.reshape(count_q, BLOCK, heads_here, HEAD_DIM)
    key_grid = key_blocks.reshape(count_q, slot_count * BLOCK, heads_here, HEAD_DIM)
    value_grid = value_blocks.reshape(count_q, slot_count * BLOCK, heads_here, HEAD_DIM)
    scores = jnp.einsum(
        "bqhd,bshd->bhqs", query_grid, key_grid, preferred_element_type=jnp.float32
    ) * (1.0 / math.sqrt(HEAD_DIM))
    present = jnp.repeat(jnp.transpose(valid_slots, (0, 2, 1)), BLOCK, axis=2)[:, :, None, :]
    scores = jnp.where(present, scores, masked_score)
    peak = jnp.max(scores, axis=3)
    expo = jnp.exp(scores - peak[..., None])
    total = jnp.sum(expo, axis=3)
    mixture = jnp.einsum(
        "bhqs,bshd->bqhd", expo.astype(jnp.bfloat16), value_grid, preferred_element_type=jnp.float32
    )
    return mixture, total, peak


def merge_attend(first, second):
    mix_a, total_a, peak_a = first
    mix_b, total_b, peak_b = second
    peak = jnp.maximum(peak_a, peak_b)
    scale_a = jnp.exp(peak_a - peak)
    scale_b = jnp.exp(peak_b - peak)
    total = total_a * scale_a + total_b * scale_b
    mix = mix_a * jnp.transpose(scale_a, (0, 2, 1))[..., None] + mix_b * jnp.transpose(scale_b, (0, 2, 1))[..., None]
    mix = mix / jnp.transpose(total, (0, 2, 1))[..., None]
    count_q = mix.shape[0]
    return mix.reshape(count_q, BLOCK, -1).astype(jnp.bfloat16)


def on_device(
    queries,
    keys,
    values,
    out_weight,
    global_blocks,
    random_blocks,
    window_blocks,
    yarn_scale,
    yarn_context,
):
    tok_here, width_here = queries.shape
    heads_here = width_here // HEAD_DIM
    blocks_here = tok_here // BLOCK
    seq_count = lax.axis_size("seq")
    seq_place = lax.axis_index("seq")
    block_total = seq_count * blocks_here
    frequency, mscale = yarn_tables(yarn_scale, yarn_context)
    first_row = seq_place * tok_here
    query_rot = rotate(queries, first_row, frequency, mscale)
    key_rot = rotate(keys, first_row, frequency, mscale)
    pair_kv = jnp.stack([key_rot, values])
    halo = WMAX * BLOCK
    seq_ends = seq_count - 1
    from_left = lax.ppermute(
        pair_kv[:, tok_here - halo :], "seq", [(i, (i + 1) % seq_count) for i in range(seq_ends)]
    ).reshape(2, WMAX, BLOCK, width_here)
    from_right = lax.ppermute(
        pair_kv[:, :halo], "seq", [((i + 1) % seq_count, i) for i in range(seq_ends)]
    ).reshape(2, WMAX, BLOCK, width_here)
    local_blocks = pair_kv.reshape(2, blocks_here, BLOCK, width_here)

    def padded_block(index):
        if index < WMAX:
            return from_left[:, index]
        if index < WMAX + blocks_here:
            return local_blocks[:, index - WMAX]
        return from_right[:, index - WMAX - blocks_here]

    offsets = jnp.arange(-WMAX, WMAX + 1)
    window_ids = seq_place * blocks_here + jnp.arange(blocks_here)[:, None] + offsets[None, :]
    inside = (window_ids >= 0) & (window_ids < block_total)
    reach = jnp.abs(offsets)[None, :, None] <= window_blocks[None, None, :]
    window_valid = inside[:, :, None] & reach
    owner_global = global_blocks // blocks_here
    local_global = jnp.clip(global_blocks - seq_place * blocks_here, 0, blocks_here - 1)
    mine_global = owner_global == seq_place
    query_view = query_rot.reshape(blocks_here, BLOCK, width_here)
    key_view = key_rot.reshape(blocks_here, BLOCK, width_here)
    value_view = values.reshape(blocks_here, BLOCK, width_here)
    picked = jnp.stack([query_view[local_global], key_view[local_global], value_view[local_global]])
    masked = jnp.where(mine_global[None, :, None, None], picked, jnp.zeros_like(picked))
    shared = tree_reduce(masked.reshape(3 * GLOB * BLOCK, width_here), add_merge, "seq")
    shared = shared.reshape(3, GLOB, BLOCK, width_here)
    slot_parts = [
        jnp.stack(
            [padded_block(block + offset_slot) for offset_slot in range(2 * WMAX + 1)], axis=1
        )
        for block in range(blocks_here)
    ]
    global_kv = jnp.broadcast_to(shared[1:3][:, None], (2, blocks_here, GLOB, BLOCK, width_here))
    near_kv = jnp.concatenate([jnp.stack(slot_parts, axis=1), global_kv], axis=2)
    near_valid = jnp.concatenate(
        [window_valid, jnp.ones((blocks_here, GLOB, heads_here), dtype=bool)], axis=1
    )
    global_query = shared[0]
    key_later = key_rot
    value_later = values
    global_query = global_query.reshape(GLOB, BLOCK, heads_here, HEAD_DIM)
    key_grid = key_later.reshape(tok_here, heads_here, HEAD_DIM)
    value_grid = value_later.reshape(tok_here, heads_here, HEAD_DIM)
    global_scores = jnp.einsum(
        "gqhd,khd->gqhk", global_query, key_grid, preferred_element_type=jnp.float32
    ) * (1.0 / math.sqrt(HEAD_DIM))
    local_peak = jnp.max(global_scores, axis=3)
    expo = jnp.exp(global_scores - local_peak[..., None])
    partial_total = jnp.sum(expo, axis=3)
    partial_mix = jnp.einsum(
        "gqhk,khd->gqhd", expo.astype(jnp.bfloat16), value_grid, preferred_element_type=jnp.float32
    )
    row_total = GLOB * BLOCK
    packed = jnp.concatenate(
        [
            partial_mix.reshape(row_total, width_here),
            partial_total.reshape(row_total, heads_here),
            local_peak.reshape(row_total, heads_here),
            jnp.zeros((row_total, 128 - 2 * heads_here), jnp.float32),
        ],
        axis=1,
    )
    slot_total = blocks_here * RAND
    capacity = (slot_total + seq_count - 1) // seq_count
    flat_ids = random_blocks.reshape(seq_count, slot_total)
    owners = flat_ids // blocks_here
    slot_order = jnp.arange(slot_total)
    same_owner = (owners[:, :, None] == owners[:, None, :]) & (
        slot_order[None, None, :] < slot_order[None, :, None]
    )
    ranks = jnp.sum(same_owner.astype(jnp.int32), axis=2)
    local_ids = flat_ids - owners * blocks_here
    wanted = (owners[:, None, :] == seq_place) & (
        ranks[:, None, :] == jnp.arange(capacity)[None, :, None]
    )
    send_local = jnp.sum(jnp.where(wanted, local_ids[:, None, :], 0), axis=2)
    kv_blocks = jnp.stack([key_rot.reshape(blocks_here, BLOCK, width_here), value_view], axis=1)
    outgoing = kv_blocks[send_local]
    outgoing, shared = lax.optimization_barrier((outgoing, shared))
    incoming = lax.all_to_all(outgoing, "seq", split_axis=0, concat_axis=0, tiled=True)
    my_owners = owners[seq_place]
    my_ranks = ranks[seq_place]
    random_k = incoming[my_owners, my_ranks, 0].reshape(blocks_here, RAND, BLOCK, width_here)
    random_v = incoming[my_owners, my_ranks, 1].reshape(blocks_here, RAND, BLOCK, width_here)
    random_kv = (random_k, random_v)
    near_part = partial_attend(query_view, near_kv[0], near_kv[1], near_valid)
    packed, near_part = lax.optimization_barrier((packed, near_part))
    reduced = tree_reduce(packed, softmax_merge, "seq")
    far_part = partial_attend(
        query_view, random_kv[0], random_kv[1], jnp.ones((blocks_here, RAND, heads_here), dtype=bool)
    )
    attended = merge_attend(near_part, far_part)
    mix_sum = reduced[:, :width_here].reshape(row_total, heads_here, HEAD_DIM)
    total_sum = reduced[:, width_here : width_here + heads_here]
    global_out = (mix_sum / total_sum[..., None]).reshape(row_total, width_here).astype(jnp.bfloat16)
    global_out = global_out.reshape(GLOB, BLOCK, width_here)
    block_index = jnp.arange(blocks_here)
    for global_slot in range(GLOB):
        hit = mine_global[global_slot] & (block_index == local_global[global_slot])
        attended = jnp.where(hit[:, None, None], global_out[global_slot][None], attended)
    mixed = sum_over_head(head_partials(attended.reshape(tok_here, width_here), out_weight))
    return mixed.astype(jnp.bfloat16)


def solution(mesh):
    in_specs = (
        P("seq", "head"),
        P("seq", "head"),
        P("seq", "head"),
        P("head", None),
        P(),
        P(),
        P("head"),
        P(),
        P(),
    )
    out_specs = P("seq", "head")
    return jax.shard_map(
        on_device, mesh=mesh, in_specs=in_specs, out_specs=out_specs, check_vma=False
    )
```

```python
import math

import jax
import jax.numpy as jnp
from jax import lax
from jax.sharding import PartitionSpec as P

HEAD_DIM = 128
BLOCK = 64
GLOB = 2
RAND = 3
WMAX = 2


masked_score = -1e30


def padded_2(cells, sides, width):
    for axis, dim in sides:
        count = lax.axis_size(axis)
        ends = count - 1
        head = lax.slice_in_dim(cells, 0, width, axis=dim)
        tail = lax.slice_in_dim(cells, cells.shape[dim] - width, cells.shape[dim], axis=dim)
        cells = jnp.concatenate(
            [
                lax.ppermute(tail, axis, [(i, (i + 1) % count) for i in range(ends)]),
                cells,
                lax.ppermute(head, axis, [((i + 1) % count, i) for i in range(ends)]),
            ],
            axis=dim,
        )
    return cells


def yarn_tables(yarn_scale, yarn_context):
    half_dim = HEAD_DIM // 2
    pair_index = jnp.arange(half_dim).astype(jnp.float32)
    base_rate = 10000.0 ** (-2.0 * pair_index / HEAD_DIM)
    factor = yarn_scale[0].astype(jnp.float32)
    context = yarn_context[0].astype(jnp.float32)
    turn_ratio = context * base_rate / (2.0 * math.pi)
    ramp_weight = jnp.clip((turn_ratio - 1.0) / 31.0, 0.0, 1.0)
    frequency = base_rate * ((1.0 - ramp_weight) / factor + ramp_weight)
    mscale = 0.1 * jnp.log(factor) + 1.0
    return (frequency, mscale)


def rotate(source, first_row, frequency, mscale):
    row_count, row_width = source.shape
    half_dim = HEAD_DIM // 2
    position = (first_row + jnp.arange(row_count)).astype(jnp.float32)
    angle_table = position[:, None] * frequency[None, :]
    cosine = jnp.cos(angle_table)[:, None, :] * mscale
    sine_part = jnp.sin(angle_table)[:, None, :] * mscale
    halves_view = source.astype(jnp.float32).reshape(row_count, row_width // HEAD_DIM, 2, half_dim)
    lower_half = halves_view[:, :, 0]
    upper_half = halves_view[:, :, 1]
    turned = jnp.stack(
        [
            lower_half * cosine - upper_half * sine_part,
            upper_half * cosine + lower_half * sine_part,
        ],
        axis=2,
    )
    return turned.reshape(row_count, row_width).astype(jnp.bfloat16)


def block_attend(query_blocks, key_blocks, value_blocks, valid_slots):
    count_q, slot_count = (key_blocks.shape[0], key_blocks.shape[1])
    heads_here = query_blocks.shape[-1] // HEAD_DIM
    query_grid = query_blocks.reshape(count_q, BLOCK, heads_here, HEAD_DIM)
    key_grid = key_blocks.reshape(count_q, slot_count * BLOCK, heads_here, HEAD_DIM)
    value_grid = value_blocks.reshape(count_q, slot_count * BLOCK, heads_here, HEAD_DIM)
    scores = jnp.einsum(
        "bqhd,bshd->bhqs", query_grid, key_grid, preferred_element_type=jnp.float32
    ) * (1.0 / math.sqrt(HEAD_DIM))
    present = jnp.repeat(jnp.transpose(valid_slots, (0, 2, 1)), BLOCK, axis=2)[:, :, None, :]
    scores = jnp.where(present, scores, masked_score)
    peak = jnp.max(scores, axis=3, keepdims=True)
    expo = jnp.exp(scores - peak)
    total = jnp.sum(expo, axis=3)
    weights = expo.astype(jnp.bfloat16)
    mixture = jnp.einsum("bhqs,bshd->bqhd", weights, value_grid, preferred_element_type=jnp.float32)
    mixture = mixture / jnp.transpose(total, (0, 2, 1))[..., None]
    return mixture.reshape(count_q, BLOCK, heads_here * HEAD_DIM).astype(jnp.bfloat16)


def xor_perm(count, bit):
    return [(i, i ^ bit) for i in range(count)]


def tree_reduce(parts, merge, axis):
    count = lax.axis_size(axis)
    place = lax.axis_index(axis)
    bits = []
    bit = 1
    while bit < count:
        bits.append(bit)
        bit *= 2
    for bit in bits:
        upper = (place // bit) % 2
        halves = jax.tree.map(lambda x: x.reshape((2, x.shape[0] // 2) + x.shape[1:]), parts)
        keep = jax.tree.map(lambda h: lax.dynamic_index_in_dim(h, upper, 0, keepdims=False), halves)
        send = jax.tree.map(lambda h: lax.dynamic_index_in_dim(h, 1 - upper, 0, keepdims=False), halves)
        got = lax.ppermute(send, axis, xor_perm(count, bit))
        parts = merge(keep, got)
    for bit in reversed(bits):
        upper = (place // bit) % 2
        got = lax.ppermute(parts, axis, xor_perm(count, bit))

        def join(mine, theirs):
            pair = jnp.stack([mine, theirs])
            first = lax.dynamic_index_in_dim(pair, upper, 0, keepdims=False)
            second = lax.dynamic_index_in_dim(pair, 1 - upper, 0, keepdims=False)
            return jnp.concatenate([first, second], axis=0)

        parts = jax.tree.map(join, parts, got)
    return parts


def add_merge(a, b):
    return jax.tree.map(jnp.add, a, b)


def softmax_merge(a, b):
    width = a.shape[1] - 128
    heads = width // HEAD_DIM
    peak_a = a[:, width + heads : width + 2 * heads]
    peak_b = b[:, width + heads : width + 2 * heads]
    peak = jnp.maximum(peak_a, peak_b)
    scale_a = jnp.exp(peak_a - peak)
    scale_b = jnp.exp(peak_b - peak)
    rows = a.shape[0]
    mix = (
        a[:, :width].reshape(rows, heads, HEAD_DIM) * scale_a[..., None]
        + b[:, :width].reshape(rows, heads, HEAD_DIM) * scale_b[..., None]
    ).reshape(rows, width)
    total = a[:, width : width + heads] * scale_a + b[:, width : width + heads] * scale_b
    pad = jnp.zeros((rows, 128 - 2 * heads), a.dtype)
    return jnp.concatenate([mix, total, peak, pad], axis=1)


def head_partials(rows, out_weight):
    head_count = lax.axis_size("head")
    partial = lax.dot_general(
        out_weight, rows, (((0,), (1,)), ((), ())), preferred_element_type=jnp.float32
    ).astype(jnp.bfloat16)
    return partial.reshape(head_count, out_weight.shape[1] // head_count, rows.shape[0])


def sum_over_head(partial):
    gathered = lax.all_to_all(partial, "head", 0, 0, tiled=True)
    return jnp.sum(gathered.astype(jnp.float32), axis=0).T


def partial_attend(query_blocks, key_blocks, value_blocks, valid_slots):
    count_q, slot_count = (key_blocks.shape[0], key_blocks.shape[1])
    heads_here = query_blocks.shape[-1] // HEAD_DIM
    query_grid = query_blocks.reshape(count_q, BLOCK, heads_here, HEAD_DIM)
    key_grid = key_blocks.reshape(count_q, slot_count * BLOCK, heads_here, HEAD_DIM)
    value_grid = value_blocks.reshape(count_q, slot_count * BLOCK, heads_here, HEAD_DIM)
    scores = jnp.einsum(
        "bqhd,bshd->bhqs", query_grid, key_grid, preferred_element_type=jnp.float32
    ) * (1.0 / math.sqrt(HEAD_DIM))
    present = jnp.repeat(jnp.transpose(valid_slots, (0, 2, 1)), BLOCK, axis=2)[:, :, None, :]
    scores = jnp.where(present, scores, masked_score)
    peak = jnp.max(scores, axis=3)
    expo = jnp.exp(scores - peak[..., None])
    total = jnp.sum(expo, axis=3)
    mixture = jnp.einsum(
        "bhqs,bshd->bqhd", expo.astype(jnp.bfloat16), value_grid, preferred_element_type=jnp.float32
    )
    return mixture, total, peak


def merge_attend(first, second):
    mix_a, total_a, peak_a = first
    mix_b, total_b, peak_b = second
    peak = jnp.maximum(peak_a, peak_b)
    scale_a = jnp.exp(peak_a - peak)
    scale_b = jnp.exp(peak_b - peak)
    total = total_a * scale_a + total_b * scale_b
    mix = mix_a * jnp.transpose(scale_a, (0, 2, 1))[..., None] + mix_b * jnp.transpose(scale_b, (0, 2, 1))[..., None]
    mix = mix / jnp.transpose(total, (0, 2, 1))[..., None]
    count_q = mix.shape[0]
    return mix.reshape(count_q, BLOCK, -1).astype(jnp.bfloat16)


def on_device(
    queries,
    keys,
    values,
    out_weight,
    global_blocks,
    random_blocks,
    window_blocks,
    yarn_scale,
    yarn_context,
):
    tok_here, width_here = queries.shape
    heads_here = width_here // HEAD_DIM
    blocks_here = tok_here // BLOCK
    seq_count = lax.axis_size("seq")
    seq_place = lax.axis_index("seq")
    block_total = seq_count * blocks_here
    frequency, mscale = yarn_tables(yarn_scale, yarn_context)
    first_row = seq_place * tok_here
    query_rot = rotate(queries, first_row, frequency, mscale)
    key_rot = rotate(keys, first_row, frequency, mscale)
    pair_kv = jnp.stack([key_rot, values])
    halo = WMAX * BLOCK
    seq_ends = seq_count - 1
    from_left = lax.ppermute(
        pair_kv[:, tok_here - halo :], "seq", [(i, (i + 1) % seq_count) for i in range(seq_ends)]
    ).reshape(2, WMAX, BLOCK, width_here)
    from_right = lax.ppermute(
        pair_kv[:, :halo], "seq", [((i + 1) % seq_count, i) for i in range(seq_ends)]
    ).reshape(2, WMAX, BLOCK, width_here)
    local_blocks = pair_kv.reshape(2, blocks_here, BLOCK, width_here)

    def padded_block(index):
        if index < WMAX:
            return from_left[:, index]
        if index < WMAX + blocks_here:
            return local_blocks[:, index - WMAX]
        return from_right[:, index - WMAX - blocks_here]

    offsets = jnp.arange(-WMAX, WMAX + 1)
    window_ids = seq_place * blocks_here + jnp.arange(blocks_here)[:, None] + offsets[None, :]
    inside = (window_ids >= 0) & (window_ids < block_total)
    reach = jnp.abs(offsets)[None, :, None] <= window_blocks[None, None, :]
    window_valid = inside[:, :, None] & reach
    owner_global = global_blocks // blocks_here
    local_global = jnp.clip(global_blocks - seq_place * blocks_here, 0, blocks_here - 1)
    mine_global = owner_global == seq_place
    query_view = query_rot.reshape(blocks_here, BLOCK, width_here)
    key_view = key_rot.reshape(blocks_here, BLOCK, width_here)
    value_view = values.reshape(blocks_here, BLOCK, width_here)
    picked = jnp.stack([query_view[local_global], key_view[local_global], value_view[local_global]])
    masked = jnp.where(mine_global[None, :, None, None], picked, jnp.zeros_like(picked))
    shared = tree_reduce(masked.reshape(3 * GLOB * BLOCK, width_here), add_merge, "seq")
    shared = shared.reshape(3, GLOB, BLOCK, width_here)
    slot_parts = [
        jnp.stack(
            [padded_block(block + offset_slot) for offset_slot in range(2 * WMAX + 1)], axis=1
        )
        for block in range(blocks_here)
    ]
    global_kv = jnp.broadcast_to(shared[1:3][:, None], (2, blocks_here, GLOB, BLOCK, width_here))
    near_kv = jnp.concatenate([jnp.stack(slot_parts, axis=1), global_kv], axis=2)
    near_valid = jnp.concatenate(
        [window_valid, jnp.ones((blocks_here, GLOB, heads_here), dtype=bool)], axis=1
    )
    global_query = shared[0]
    key_later = key_rot
    value_later = values
    global_query = global_query.reshape(GLOB, BLOCK, heads_here, HEAD_DIM)
    key_grid = key_later.reshape(tok_here, heads_here, HEAD_DIM)
    value_grid = value_later.reshape(tok_here, heads_here, HEAD_DIM)
    global_scores = jnp.einsum(
        "gqhd,khd->gqhk", global_query, key_grid, preferred_element_type=jnp.float32
    ) * (1.0 / math.sqrt(HEAD_DIM))
    local_peak = jnp.max(global_scores, axis=3)
    expo = jnp.exp(global_scores - local_peak[..., None])
    partial_total = jnp.sum(expo, axis=3)
    partial_mix = jnp.einsum(
        "gqhk,khd->gqhd", expo.astype(jnp.bfloat16), value_grid, preferred_element_type=jnp.float32
    )
    row_total = GLOB * BLOCK
    packed = jnp.concatenate(
        [
            partial_mix.reshape(row_total, width_here),
            partial_total.reshape(row_total, heads_here),
            local_peak.reshape(row_total, heads_here),
            jnp.zeros((row_total, 128 - 2 * heads_here), jnp.float32),
        ],
        axis=1,
    )
    reduced = tree_reduce(packed, softmax_merge, "seq")
    slot_total = blocks_here * RAND
    capacity = (slot_total + seq_count - 1) // seq_count
    flat_ids = random_blocks.reshape(seq_count, slot_total)
    owners = flat_ids // blocks_here
    slot_order = jnp.arange(slot_total)
    same_owner = (owners[:, :, None] == owners[:, None, :]) & (
        slot_order[None, None, :] < slot_order[None, :, None]
    )
    ranks = jnp.sum(same_owner.astype(jnp.int32), axis=2)
    local_ids = flat_ids - owners * blocks_here
    wanted = (owners[:, None, :] == seq_place) & (
        ranks[:, None, :] == jnp.arange(capacity)[None, :, None]
    )
    send_local = jnp.sum(jnp.where(wanted, local_ids[:, None, :], 0), axis=2)
    key_blocks = key_rot.reshape(blocks_here, BLOCK, width_here)
    outgoing = jnp.stack([key_blocks[send_local], value_view[send_local]], axis=2)
    outgoing, reduced = lax.optimization_barrier((outgoing, reduced))
    incoming = lax.all_to_all(outgoing, "seq", split_axis=0, concat_axis=0, tiled=True)
    my_owners = owners[seq_place]
    my_ranks = ranks[seq_place]
    random_k = incoming[my_owners, my_ranks, 0].reshape(blocks_here, RAND, BLOCK, width_here)
    random_v = incoming[my_owners, my_ranks, 1].reshape(blocks_here, RAND, BLOCK, width_here)
    random_kv = (random_k, random_v)
    near_part = partial_attend(query_view, near_kv[0], near_kv[1], near_valid)
    mix_sum = reduced[:, :width_here].reshape(row_total, heads_here, HEAD_DIM)
    total_sum = reduced[:, width_here : width_here + heads_here]
    global_out = (mix_sum / total_sum[..., None]).reshape(row_total, width_here).astype(jnp.bfloat16)
    global_out = global_out.reshape(GLOB, BLOCK, width_here)
    pieces = 2 if blocks_here % 2 == 0 else 1
    span = blocks_here // pieces
    outputs = []
    for piece in range(pieces):
        lo = piece * span
        hi = lo + span
        near_piece = jax.tree.map(lambda x: x[lo:hi], near_part)
        far_part = partial_attend(
            query_view[lo:hi],
            random_k[lo:hi],
            random_v[lo:hi],
            jnp.ones((span, RAND, heads_here), dtype=bool),
        )
        attended = merge_attend(near_piece, far_part)
        block_index = jnp.arange(lo, hi)
        for global_slot in range(GLOB):
            hit = mine_global[global_slot] & (block_index == local_global[global_slot])
            attended = jnp.where(hit[:, None, None], global_out[global_slot][None], attended)
        outputs.append(
            sum_over_head(head_partials(attended.reshape(span * BLOCK, width_here), out_weight))
        )
    mixed = jnp.concatenate(outputs, axis=0)
    return mixed.astype(jnp.bfloat16)


def solution(mesh):
    in_specs = (
        P("seq", "head"),
        P("seq", "head"),
        P("seq", "head"),
        P("head", None),
        P(),
        P(),
        P("head"),
        P(),
        P(),
    )
    out_specs = P("seq", "head")
    return jax.shard_map(
        on_device, mesh=mesh, in_specs=in_specs, out_specs=out_specs, check_vma=False
    )
```

```python
import math

import jax
import jax.numpy as jnp
from jax import lax
from jax.sharding import PartitionSpec as P

HEAD_DIM = 128
BLOCK = 64
GLOB = 2
RAND = 3
WMAX = 2


masked_score = -1e30


def padded_2(cells, sides, width):
    for axis, dim in sides:
        count = lax.axis_size(axis)
        ends = count - 1
        head = lax.slice_in_dim(cells, 0, width, axis=dim)
        tail = lax.slice_in_dim(cells, cells.shape[dim] - width, cells.shape[dim], axis=dim)
        cells = jnp.concatenate(
            [
                lax.ppermute(tail, axis, [(i, (i + 1) % count) for i in range(ends)]),
                cells,
                lax.ppermute(head, axis, [((i + 1) % count, i) for i in range(ends)]),
            ],
            axis=dim,
        )
    return cells


def yarn_tables(yarn_scale, yarn_context):
    half_dim = HEAD_DIM // 2
    pair_index = jnp.arange(half_dim).astype(jnp.float32)
    base_rate = 10000.0 ** (-2.0 * pair_index / HEAD_DIM)
    factor = yarn_scale[0].astype(jnp.float32)
    context = yarn_context[0].astype(jnp.float32)
    turn_ratio = context * base_rate / (2.0 * math.pi)
    ramp_weight = jnp.clip((turn_ratio - 1.0) / 31.0, 0.0, 1.0)
    frequency = base_rate * ((1.0 - ramp_weight) / factor + ramp_weight)
    mscale = 0.1 * jnp.log(factor) + 1.0
    return (frequency, mscale)


def rotate(source, first_row, frequency, mscale):
    row_count, row_width = source.shape
    half_dim = HEAD_DIM // 2
    position = (first_row + jnp.arange(row_count)).astype(jnp.float32)
    angle_table = position[:, None] * frequency[None, :]
    cosine = jnp.cos(angle_table)[:, None, :] * mscale
    sine_part = jnp.sin(angle_table)[:, None, :] * mscale
    halves_view = source.astype(jnp.float32).reshape(row_count, row_width // HEAD_DIM, 2, half_dim)
    lower_half = halves_view[:, :, 0]
    upper_half = halves_view[:, :, 1]
    turned = jnp.stack(
        [
            lower_half * cosine - upper_half * sine_part,
            upper_half * cosine + lower_half * sine_part,
        ],
        axis=2,
    )
    return turned.reshape(row_count, row_width).astype(jnp.bfloat16)


def rotate_at(source, position, frequency, mscale):
    row_count, row_width = source.shape
    half_dim = HEAD_DIM // 2
    angle_table = position.astype(jnp.float32)[:, None] * frequency[None, :]
    cosine = jnp.cos(angle_table)[:, None, :] * mscale
    sine_part = jnp.sin(angle_table)[:, None, :] * mscale
    halves_view = source.astype(jnp.float32).reshape(row_count, row_width // HEAD_DIM, 2, half_dim)
    lower_half = halves_view[:, :, 0]
    upper_half = halves_view[:, :, 1]
    turned = jnp.stack(
        [
            lower_half * cosine - upper_half * sine_part,
            upper_half * cosine + lower_half * sine_part,
        ],
        axis=2,
    )
    return turned.reshape(row_count, row_width).astype(jnp.bfloat16)


def block_attend(query_blocks, key_blocks, value_blocks, valid_slots):
    count_q, slot_count = (key_blocks.shape[0], key_blocks.shape[1])
    heads_here = query_blocks.shape[-1] // HEAD_DIM
    query_grid = query_blocks.reshape(count_q, BLOCK, heads_here, HEAD_DIM)
    key_grid = key_blocks.reshape(count_q, slot_count * BLOCK, heads_here, HEAD_DIM)
    value_grid = value_blocks.reshape(count_q, slot_count * BLOCK, heads_here, HEAD_DIM)
    scores = jnp.einsum(
        "bqhd,bshd->bhqs", query_grid, key_grid, preferred_element_type=jnp.float32
    ) * (1.0 / math.sqrt(HEAD_DIM))
    present = jnp.repeat(jnp.transpose(valid_slots, (0, 2, 1)), BLOCK, axis=2)[:, :, None, :]
    scores = jnp.where(present, scores, masked_score)
    peak = jnp.max(scores, axis=3, keepdims=True)
    expo = jnp.exp(scores - peak)
    total = jnp.sum(expo, axis=3)
    weights = expo.astype(jnp.bfloat16)
    mixture = jnp.einsum("bhqs,bshd->bqhd", weights, value_grid, preferred_element_type=jnp.float32)
    mixture = mixture / jnp.transpose(total, (0, 2, 1))[..., None]
    return mixture.reshape(count_q, BLOCK, heads_here * HEAD_DIM).astype(jnp.bfloat16)


def xor_perm(count, bit):
    return [(i, i ^ bit) for i in range(count)]


def tree_reduce(parts, merge, axis):
    count = lax.axis_size(axis)
    place = lax.axis_index(axis)
    bits = []
    bit = 1
    while bit < count:
        bits.append(bit)
        bit *= 2
    for bit in bits:
        upper = (place // bit) % 2
        halves = jax.tree.map(lambda x: x.reshape((2, x.shape[0] // 2) + x.shape[1:]), parts)
        keep = jax.tree.map(lambda h: lax.dynamic_index_in_dim(h, upper, 0, keepdims=False), halves)
        send = jax.tree.map(lambda h: lax.dynamic_index_in_dim(h, 1 - upper, 0, keepdims=False), halves)
        got = lax.ppermute(send, axis, xor_perm(count, bit))
        parts = merge(keep, got)
    for bit in reversed(bits):
        upper = (place // bit) % 2
        got = lax.ppermute(parts, axis, xor_perm(count, bit))

        def join(mine, theirs):
            pair = jnp.stack([mine, theirs])
            first = lax.dynamic_index_in_dim(pair, upper, 0, keepdims=False)
            second = lax.dynamic_index_in_dim(pair, 1 - upper, 0, keepdims=False)
            return jnp.concatenate([first, second], axis=0)

        parts = jax.tree.map(join, parts, got)
    return parts


def add_merge(a, b):
    return jax.tree.map(jnp.add, a, b)


def softmax_merge(a, b):
    width = a.shape[1] - 128
    heads = width // HEAD_DIM
    peak_a = a[:, width + heads : width + 2 * heads]
    peak_b = b[:, width + heads : width + 2 * heads]
    peak = jnp.maximum(peak_a, peak_b)
    scale_a = jnp.exp(peak_a - peak)
    scale_b = jnp.exp(peak_b - peak)
    rows = a.shape[0]
    mix = (
        a[:, :width].reshape(rows, heads, HEAD_DIM) * scale_a[..., None]
        + b[:, :width].reshape(rows, heads, HEAD_DIM) * scale_b[..., None]
    ).reshape(rows, width)
    total = a[:, width : width + heads] * scale_a + b[:, width : width + heads] * scale_b
    pad = jnp.zeros((rows, 128 - 2 * heads), a.dtype)
    return jnp.concatenate([mix, total, peak, pad], axis=1)


def head_partials(rows, out_weight):
    head_count = lax.axis_size("head")
    partial = lax.dot_general(
        out_weight, rows, (((0,), (1,)), ((), ())), preferred_element_type=jnp.float32
    ).astype(jnp.bfloat16)
    return partial.reshape(head_count, out_weight.shape[1] // head_count, rows.shape[0])


def sum_over_head(partial):
    gathered = lax.all_to_all(partial, "head", 0, 0, tiled=True)
    return jnp.sum(gathered.astype(jnp.float32), axis=0).T


def partial_attend(query_blocks, key_blocks, value_blocks, valid_slots):
    count_q, slot_count = (key_blocks.shape[0], key_blocks.shape[1])
    heads_here = query_blocks.shape[-1] // HEAD_DIM
    query_grid = query_blocks.reshape(count_q, BLOCK, heads_here, HEAD_DIM)
    key_grid = key_blocks.reshape(count_q, slot_count * BLOCK, heads_here, HEAD_DIM)
    value_grid = value_blocks.reshape(count_q, slot_count * BLOCK, heads_here, HEAD_DIM)
    scores = jnp.einsum(
        "bqhd,bshd->bhqs", query_grid, key_grid, preferred_element_type=jnp.float32
    ) * (1.0 / math.sqrt(HEAD_DIM))
    present = jnp.repeat(jnp.transpose(valid_slots, (0, 2, 1)), BLOCK, axis=2)[:, :, None, :]
    scores = jnp.where(present, scores, masked_score)
    peak = jnp.max(scores, axis=3)
    expo = jnp.exp(scores - peak[..., None])
    total = jnp.sum(expo, axis=3)
    mixture = jnp.einsum(
        "bhqs,bshd->bqhd", expo.astype(jnp.bfloat16), value_grid, preferred_element_type=jnp.float32
    )
    return mixture, total, peak


def merge_attend(first, second):
    mix_a, total_a, peak_a = first
    mix_b, total_b, peak_b = second
    peak = jnp.maximum(peak_a, peak_b)
    scale_a = jnp.exp(peak_a - peak)
    scale_b = jnp.exp(peak_b - peak)
    total = total_a * scale_a + total_b * scale_b
    mix = mix_a * jnp.transpose(scale_a, (0, 2, 1))[..., None] + mix_b * jnp.transpose(scale_b, (0, 2, 1))[..., None]
    mix = mix / jnp.transpose(total, (0, 2, 1))[..., None]
    count_q = mix.shape[0]
    return mix.reshape(count_q, BLOCK, -1).astype(jnp.bfloat16)


def on_device(
    queries,
    keys,
    values,
    out_weight,
    global_blocks,
    random_blocks,
    window_blocks,
    yarn_scale,
    yarn_context,
):
    tok_here, width_here = queries.shape
    heads_here = width_here // HEAD_DIM
    blocks_here = tok_here // BLOCK
    seq_count = lax.axis_size("seq")
    seq_place = lax.axis_index("seq")
    block_total = seq_count * blocks_here
    frequency, mscale = yarn_tables(yarn_scale, yarn_context)
    first_row = seq_place * tok_here
    query_rot = rotate(queries, first_row, frequency, mscale)
    key_rot = rotate(keys, first_row, frequency, mscale)
    pair_kv = jnp.stack([key_rot, values])
    halo = WMAX * BLOCK
    seq_ends = seq_count - 1
    from_left = lax.ppermute(
        pair_kv[:, tok_here - halo :], "seq", [(i, (i + 1) % seq_count) for i in range(seq_ends)]
    ).reshape(2, WMAX, BLOCK, width_here)
    from_right = lax.ppermute(
        pair_kv[:, :halo], "seq", [((i + 1) % seq_count, i) for i in range(seq_ends)]
    ).reshape(2, WMAX, BLOCK, width_here)
    local_blocks = pair_kv.reshape(2, blocks_here, BLOCK, width_here)

    def padded_block(index):
        if index < WMAX:
            return from_left[:, index]
        if index < WMAX + blocks_here:
            return local_blocks[:, index - WMAX]
        return from_right[:, index - WMAX - blocks_here]

    offsets = jnp.arange(-WMAX, WMAX + 1)
    window_ids = seq_place * blocks_here + jnp.arange(blocks_here)[:, None] + offsets[None, :]
    inside = (window_ids >= 0) & (window_ids < block_total)
    reach = jnp.abs(offsets)[None, :, None] <= window_blocks[None, None, :]
    window_valid = inside[:, :, None] & reach
    owner_global = global_blocks // blocks_here
    local_global = jnp.clip(global_blocks - seq_place * blocks_here, 0, blocks_here - 1)
    mine_global = owner_global == seq_place
    query_view = query_rot.reshape(blocks_here, BLOCK, width_here)
    key_view = key_rot.reshape(blocks_here, BLOCK, width_here)
    value_view = values.reshape(blocks_here, BLOCK, width_here)
    raw_q = queries.reshape(blocks_here, BLOCK, width_here)[local_global].reshape(GLOB * BLOCK, width_here)
    raw_k = keys.reshape(blocks_here, BLOCK, width_here)[local_global].reshape(GLOB * BLOCK, width_here)
    picked_rows = (first_row + local_global * BLOCK)[:, None] + jnp.arange(BLOCK)[None, :]
    picked_rows = picked_rows.reshape(GLOB * BLOCK)
    picked = jnp.stack(
        [
            rotate_at(raw_q, picked_rows, frequency, mscale).reshape(GLOB, BLOCK, width_here),
            rotate_at(raw_k, picked_rows, frequency, mscale).reshape(GLOB, BLOCK, width_here),
            value_view[local_global],
        ]
    )
    masked = jnp.where(mine_global[None, :, None, None], picked, jnp.zeros_like(picked))
    shared = tree_reduce(masked.reshape(3 * GLOB * BLOCK, width_here), add_merge, "seq")
    shared = shared.reshape(3, GLOB, BLOCK, width_here)
    slot_parts = [
        jnp.stack(
            [padded_block(block + offset_slot) for offset_slot in range(2 * WMAX + 1)], axis=1
        )
        for block in range(blocks_here)
    ]
    global_kv = jnp.broadcast_to(shared[1:3][:, None], (2, blocks_here, GLOB, BLOCK, width_here))
    near_kv = jnp.concatenate([jnp.stack(slot_parts, axis=1), global_kv], axis=2)
    near_valid = jnp.concatenate(
        [window_valid, jnp.ones((blocks_here, GLOB, heads_here), dtype=bool)], axis=1
    )
    global_query = shared[0]
    key_later = key_rot
    value_later = values
    global_query = global_query.reshape(GLOB, BLOCK, heads_here, HEAD_DIM)
    key_grid = key_later.reshape(tok_here, heads_here, HEAD_DIM)
    value_grid = value_later.reshape(tok_here, heads_here, HEAD_DIM)
    global_scores = jnp.einsum(
        "gqhd,khd->gqhk", global_query, key_grid, preferred_element_type=jnp.float32
    ) * (1.0 / math.sqrt(HEAD_DIM))
    local_peak = jnp.max(global_scores, axis=3)
    expo = jnp.exp(global_scores - local_peak[..., None])
    partial_total = jnp.sum(expo, axis=3)
    partial_mix = jnp.einsum(
        "gqhk,khd->gqhd", expo.astype(jnp.bfloat16), value_grid, preferred_element_type=jnp.float32
    )
    row_total = GLOB * BLOCK
    packed = jnp.concatenate(
        [
            partial_mix.reshape(row_total, width_here),
            partial_total.reshape(row_total, heads_here),
            local_peak.reshape(row_total, heads_here),
            jnp.zeros((row_total, 128 - 2 * heads_here), jnp.float32),
        ],
        axis=1,
    )
    reduced = tree_reduce(packed, softmax_merge, "seq")
    slot_total = blocks_here * RAND
    capacity = (slot_total + seq_count - 1) // seq_count
    flat_ids = random_blocks.reshape(seq_count, slot_total)
    owners = flat_ids // blocks_here
    slot_order = jnp.arange(slot_total)
    same_owner = (owners[:, :, None] == owners[:, None, :]) & (
        slot_order[None, None, :] < slot_order[None, :, None]
    )
    ranks = jnp.sum(same_owner.astype(jnp.int32), axis=2)
    local_ids = flat_ids - owners * blocks_here
    wanted = (owners[:, None, :] == seq_place) & (
        ranks[:, None, :] == jnp.arange(capacity)[None, :, None]
    )
    send_local = jnp.sum(jnp.where(wanted, local_ids[:, None, :], 0), axis=2)
    kv_blocks = jnp.stack([key_rot.reshape(blocks_here, BLOCK, width_here), value_view], axis=1)
    outgoing = kv_blocks[send_local]
    outgoing, reduced = lax.optimization_barrier((outgoing, reduced))
    incoming = lax.all_to_all(outgoing, "seq", split_axis=0, concat_axis=0, tiled=True)
    my_owners = owners[seq_place]
    my_ranks = ranks[seq_place]
    random_k = incoming[my_owners, my_ranks, 0].reshape(blocks_here, RAND, BLOCK, width_here)
    random_v = incoming[my_owners, my_ranks, 1].reshape(blocks_here, RAND, BLOCK, width_here)
    random_kv = (random_k, random_v)
    near_part = partial_attend(query_view, near_kv[0], near_kv[1], near_valid)
    far_part = partial_attend(
        query_view, random_kv[0], random_kv[1], jnp.ones((blocks_here, RAND, heads_here), dtype=bool)
    )
    attended = merge_attend(near_part, far_part)
    mix_sum = reduced[:, :width_here].reshape(row_total, heads_here, HEAD_DIM)
    total_sum = reduced[:, width_here : width_here + heads_here]
    global_out = (mix_sum / total_sum[..., None]).reshape(row_total, width_here).astype(jnp.bfloat16)
    global_out = global_out.reshape(GLOB, BLOCK, width_here)
    block_index = jnp.arange(blocks_here)
    for global_slot in range(GLOB):
        hit = mine_global[global_slot] & (block_index == local_global[global_slot])
        attended = jnp.where(hit[:, None, None], global_out[global_slot][None], attended)
    mixed = sum_over_head(head_partials(attended.reshape(tok_here, width_here), out_weight))
    return mixed.astype(jnp.bfloat16)


def solution(mesh):
    in_specs = (
        P("seq", "head"),
        P("seq", "head"),
        P("seq", "head"),
        P("head", None),
        P(),
        P(),
        P("head"),
        P(),
        P(),
    )
    out_specs = P("seq", "head")
    return jax.shard_map(
        on_device, mesh=mesh, in_specs=in_specs, out_specs=out_specs, check_vma=False
    )
```

```python
import math

import jax
import jax.numpy as jnp
from jax import lax
from jax.sharding import PartitionSpec as P

HEAD_DIM = 128
BLOCK = 64
GLOB = 2
RAND = 3
WMAX = 2


masked_score = -1e30


def padded_2(cells, sides, width):
    for axis, dim in sides:
        count = lax.axis_size(axis)
        ends = count - 1
        head = lax.slice_in_dim(cells, 0, width, axis=dim)
        tail = lax.slice_in_dim(cells, cells.shape[dim] - width, cells.shape[dim], axis=dim)
        cells = jnp.concatenate(
            [
                lax.ppermute(tail, axis, [(i, (i + 1) % count) for i in range(ends)]),
                cells,
                lax.ppermute(head, axis, [((i + 1) % count, i) for i in range(ends)]),
            ],
            axis=dim,
        )
    return cells


def yarn_tables(yarn_scale, yarn_context):
    half_dim = HEAD_DIM // 2
    pair_index = jnp.arange(half_dim).astype(jnp.float32)
    base_rate = 10000.0 ** (-2.0 * pair_index / HEAD_DIM)
    factor = yarn_scale[0].astype(jnp.float32)
    context = yarn_context[0].astype(jnp.float32)
    turn_ratio = context * base_rate / (2.0 * math.pi)
    ramp_weight = jnp.clip((turn_ratio - 1.0) / 31.0, 0.0, 1.0)
    frequency = base_rate * ((1.0 - ramp_weight) / factor + ramp_weight)
    mscale = 0.1 * jnp.log(factor) + 1.0
    return (frequency, mscale)


def rotate(source, first_row, frequency, mscale):
    row_count, row_width = source.shape
    half_dim = HEAD_DIM // 2
    position = (first_row + jnp.arange(row_count)).astype(jnp.float32)
    angle_table = position[:, None] * frequency[None, :]
    cosine = jnp.cos(angle_table)[:, None, :] * mscale
    sine_part = jnp.sin(angle_table)[:, None, :] * mscale
    halves_view = source.astype(jnp.float32).reshape(row_count, row_width // HEAD_DIM, 2, half_dim)
    lower_half = halves_view[:, :, 0]
    upper_half = halves_view[:, :, 1]
    turned = jnp.stack(
        [
            lower_half * cosine - upper_half * sine_part,
            upper_half * cosine + lower_half * sine_part,
        ],
        axis=2,
    )
    return turned.reshape(row_count, row_width).astype(jnp.bfloat16)


def block_attend(query_blocks, key_blocks, value_blocks, valid_slots):
    count_q, slot_count = (key_blocks.shape[0], key_blocks.shape[1])
    heads_here = query_blocks.shape[-1] // HEAD_DIM
    query_grid = query_blocks.reshape(count_q, BLOCK, heads_here, HEAD_DIM)
    key_grid = key_blocks.reshape(count_q, slot_count * BLOCK, heads_here, HEAD_DIM)
    value_grid = value_blocks.reshape(count_q, slot_count * BLOCK, heads_here, HEAD_DIM)
    scores = jnp.einsum(
        "bqhd,bshd->bhqs", query_grid, key_grid, preferred_element_type=jnp.float32
    ) * (1.0 / math.sqrt(HEAD_DIM))
    present = jnp.repeat(jnp.transpose(valid_slots, (0, 2, 1)), BLOCK, axis=2)[:, :, None, :]
    scores = jnp.where(present, scores, masked_score)
    peak = jnp.max(scores, axis=3, keepdims=True)
    expo = jnp.exp(scores - peak)
    total = jnp.sum(expo, axis=3)
    weights = expo.astype(jnp.bfloat16)
    mixture = jnp.einsum("bhqs,bshd->bqhd", weights, value_grid, preferred_element_type=jnp.float32)
    mixture = mixture / jnp.transpose(total, (0, 2, 1))[..., None]
    return mixture.reshape(count_q, BLOCK, heads_here * HEAD_DIM).astype(jnp.bfloat16)


def xor_perm(count, bit):
    return [(i, i ^ bit) for i in range(count)]


def tree_reduce(parts, merge, axis):
    count = lax.axis_size(axis)
    place = lax.axis_index(axis)
    bits = []
    bit = 1
    while bit < count:
        bits.append(bit)
        bit *= 2
    for bit in bits:
        upper = (place // bit) % 2
        halves = jax.tree.map(lambda x: x.reshape((2, x.shape[0] // 2) + x.shape[1:]), parts)
        keep = jax.tree.map(lambda h: lax.dynamic_index_in_dim(h, upper, 0, keepdims=False), halves)
        send = jax.tree.map(lambda h: lax.dynamic_index_in_dim(h, 1 - upper, 0, keepdims=False), halves)
        got = lax.ppermute(send, axis, xor_perm(count, bit))
        parts = merge(keep, got)
    for bit in reversed(bits):
        upper = (place // bit) % 2
        got = lax.ppermute(parts, axis, xor_perm(count, bit))

        def join(mine, theirs):
            pair = jnp.stack([mine, theirs])
            first = lax.dynamic_index_in_dim(pair, upper, 0, keepdims=False)
            second = lax.dynamic_index_in_dim(pair, 1 - upper, 0, keepdims=False)
            return jnp.concatenate([first, second], axis=0)

        parts = jax.tree.map(join, parts, got)
    return parts


def add_merge(a, b):
    return jax.tree.map(jnp.add, a, b)


def softmax_merge(a, b):
    width = a.shape[1] - 128
    heads = width // HEAD_DIM
    peak_a = a[:, width + heads : width + 2 * heads]
    peak_b = b[:, width + heads : width + 2 * heads]
    peak = jnp.maximum(peak_a, peak_b)
    scale_a = jnp.exp(peak_a - peak)
    scale_b = jnp.exp(peak_b - peak)
    rows = a.shape[0]
    mix = (
        a[:, :width].reshape(rows, heads, HEAD_DIM) * scale_a[..., None]
        + b[:, :width].reshape(rows, heads, HEAD_DIM) * scale_b[..., None]
    ).reshape(rows, width)
    total = a[:, width : width + heads] * scale_a + b[:, width : width + heads] * scale_b
    pad = jnp.zeros((rows, 128 - 2 * heads), a.dtype)
    return jnp.concatenate([mix, total, peak, pad], axis=1)


def head_partials(rows, out_weight):
    head_count = lax.axis_size("head")
    partial = lax.dot_general(
        out_weight, rows, (((0,), (1,)), ((), ())), preferred_element_type=jnp.float32
    ).astype(jnp.bfloat16)
    return partial.reshape(head_count, out_weight.shape[1] // head_count, rows.shape[0])


def sum_over_head(partial):
    gathered = lax.all_to_all(partial, "head", 0, 0, tiled=True)
    return jnp.sum(gathered.astype(jnp.float32), axis=0).T


def partial_attend(query_blocks, key_blocks, value_blocks, valid_slots):
    count_q, slot_count = (key_blocks.shape[0], key_blocks.shape[1])
    heads_here = query_blocks.shape[-1] // HEAD_DIM
    query_grid = query_blocks.reshape(count_q, BLOCK, heads_here, HEAD_DIM)
    key_grid = key_blocks.reshape(count_q, slot_count * BLOCK, heads_here, HEAD_DIM)
    value_grid = value_blocks.reshape(count_q, slot_count * BLOCK, heads_here, HEAD_DIM)
    scores = jnp.einsum(
        "bqhd,bshd->bhqs", query_grid, key_grid, preferred_element_type=jnp.float32
    ) * (1.0 / math.sqrt(HEAD_DIM))
    present = jnp.repeat(jnp.transpose(valid_slots, (0, 2, 1)), BLOCK, axis=2)[:, :, None, :]
    scores = jnp.where(present, scores, masked_score)
    peak = jnp.max(scores, axis=3)
    expo = jnp.exp(scores - peak[..., None])
    total = jnp.sum(expo, axis=3)
    mixture = jnp.einsum(
        "bhqs,bshd->bqhd", expo.astype(jnp.bfloat16), value_grid, preferred_element_type=jnp.float32
    )
    return mixture, total, peak


def shared_attend(query_blocks, key_chunks, value_chunks, chunk_valid):
    count_q = query_blocks.shape[0]
    chunk_count = key_chunks.shape[0]
    heads_here = query_blocks.shape[-1] // HEAD_DIM
    query_grid = query_blocks.reshape(count_q, BLOCK, heads_here, HEAD_DIM)
    key_grid = key_chunks.reshape(chunk_count * BLOCK, heads_here, HEAD_DIM)
    value_grid = value_chunks.reshape(chunk_count * BLOCK, heads_here, HEAD_DIM)
    scores = jnp.einsum(
        "bqhd,shd->bhqs", query_grid, key_grid, preferred_element_type=jnp.float32
    ) * (1.0 / math.sqrt(HEAD_DIM))
    present = jnp.repeat(chunk_valid, BLOCK, axis=1)[:, None, None, :]
    scores = jnp.where(present, scores, masked_score)
    peak = jnp.max(scores, axis=3)
    expo = jnp.exp(scores - peak[..., None])
    total = jnp.sum(expo, axis=3)
    mixture = jnp.einsum(
        "bhqs,shd->bqhd", expo.astype(jnp.bfloat16), value_grid, preferred_element_type=jnp.float32
    )
    return mixture, total, peak


def merge_attend(first, second):
    mix_a, total_a, peak_a = first
    mix_b, total_b, peak_b = second
    peak = jnp.maximum(peak_a, peak_b)
    scale_a = jnp.exp(peak_a - peak)
    scale_b = jnp.exp(peak_b - peak)
    total = total_a * scale_a + total_b * scale_b
    mix = mix_a * jnp.transpose(scale_a, (0, 2, 1))[..., None] + mix_b * jnp.transpose(scale_b, (0, 2, 1))[..., None]
    mix = mix / jnp.transpose(total, (0, 2, 1))[..., None]
    count_q = mix.shape[0]
    return mix.reshape(count_q, BLOCK, -1).astype(jnp.bfloat16)


def on_device(
    queries,
    keys,
    values,
    out_weight,
    global_blocks,
    random_blocks,
    window_blocks,
    yarn_scale,
    yarn_context,
):
    tok_here, width_here = queries.shape
    heads_here = width_here // HEAD_DIM
    blocks_here = tok_here // BLOCK
    seq_count = lax.axis_size("seq")
    seq_place = lax.axis_index("seq")
    block_total = seq_count * blocks_here
    frequency, mscale = yarn_tables(yarn_scale, yarn_context)
    first_row = seq_place * tok_here
    query_rot = rotate(queries, first_row, frequency, mscale)
    key_rot = rotate(keys, first_row, frequency, mscale)
    pair_kv = jnp.stack([key_rot, values])
    halo = WMAX * BLOCK
    seq_ends = seq_count - 1
    from_left = lax.ppermute(
        pair_kv[:, tok_here - halo :], "seq", [(i, (i + 1) % seq_count) for i in range(seq_ends)]
    ).reshape(2, WMAX, BLOCK, width_here)
    from_right = lax.ppermute(
        pair_kv[:, :halo], "seq", [((i + 1) % seq_count, i) for i in range(seq_ends)]
    ).reshape(2, WMAX, BLOCK, width_here)
    local_blocks = pair_kv.reshape(2, blocks_here, BLOCK, width_here)

    def padded_block(index):
        if index < WMAX:
            return from_left[:, index]
        if index < WMAX + blocks_here:
            return local_blocks[:, index - WMAX]
        return from_right[:, index - WMAX - blocks_here]

    offsets = jnp.arange(-WMAX, WMAX + 1)
    window_ids = seq_place * blocks_here + jnp.arange(blocks_here)[:, None] + offsets[None, :]
    inside = (window_ids >= 0) & (window_ids < block_total)
    reach = jnp.abs(offsets)[None, :, None] <= window_blocks[None, None, :]
    window_valid = inside[:, :, None] & reach
    owner_global = global_blocks // blocks_here
    local_global = jnp.clip(global_blocks - seq_place * blocks_here, 0, blocks_here - 1)
    mine_global = owner_global == seq_place
    query_view = query_rot.reshape(blocks_here, BLOCK, width_here)
    key_view = key_rot.reshape(blocks_here, BLOCK, width_here)
    value_view = values.reshape(blocks_here, BLOCK, width_here)
    picked = jnp.stack([query_view[local_global], key_view[local_global], value_view[local_global]])
    masked = jnp.where(mine_global[None, :, None, None], picked, jnp.zeros_like(picked))
    shared = tree_reduce(masked.reshape(3 * GLOB * BLOCK, width_here), add_merge, "seq")
    shared = shared.reshape(3, GLOB, BLOCK, width_here)
    slot_parts = [
        jnp.stack(
            [padded_block(block + offset_slot) for offset_slot in range(2 * WMAX + 1)], axis=1
        )
        for block in range(blocks_here)
    ]
    global_kv = jnp.broadcast_to(shared[1:3][:, None], (2, blocks_here, GLOB, BLOCK, width_here))
    near_kv = jnp.concatenate([jnp.stack(slot_parts, axis=1), global_kv], axis=2)
    near_valid = jnp.concatenate(
        [window_valid, jnp.ones((blocks_here, GLOB, heads_here), dtype=bool)], axis=1
    )
    global_query = shared[0]
    key_later = key_rot
    value_later = values
    global_query = global_query.reshape(GLOB, BLOCK, heads_here, HEAD_DIM)
    key_grid = key_later.reshape(tok_here, heads_here, HEAD_DIM)
    value_grid = value_later.reshape(tok_here, heads_here, HEAD_DIM)
    global_scores = jnp.einsum(
        "gqhd,khd->gqhk", global_query, key_grid, preferred_element_type=jnp.float32
    ) * (1.0 / math.sqrt(HEAD_DIM))
    local_peak = jnp.max(global_scores, axis=3)
    expo = jnp.exp(global_scores - local_peak[..., None])
    partial_total = jnp.sum(expo, axis=3)
    partial_mix = jnp.einsum(
        "gqhk,khd->gqhd", expo.astype(jnp.bfloat16), value_grid, preferred_element_type=jnp.float32
    )
    row_total = GLOB * BLOCK
    packed = jnp.concatenate(
        [
            partial_mix.reshape(row_total, width_here),
            partial_total.reshape(row_total, heads_here),
            local_peak.reshape(row_total, heads_here),
            jnp.zeros((row_total, 128 - 2 * heads_here), jnp.float32),
        ],
        axis=1,
    )
    reduced = tree_reduce(packed, softmax_merge, "seq")
    slot_total = blocks_here * RAND
    capacity = (slot_total + seq_count - 1) // seq_count
    flat_ids = random_blocks.reshape(seq_count, slot_total)
    owners = flat_ids // blocks_here
    slot_order = jnp.arange(slot_total)
    same_owner = (owners[:, :, None] == owners[:, None, :]) & (
        slot_order[None, None, :] < slot_order[None, :, None]
    )
    ranks = jnp.sum(same_owner.astype(jnp.int32), axis=2)
    local_ids = flat_ids - owners * blocks_here
    wanted = (owners[:, None, :] == seq_place) & (
        ranks[:, None, :] == jnp.arange(capacity)[None, :, None]
    )
    send_local = jnp.sum(jnp.where(wanted, local_ids[:, None, :], 0), axis=2)
    kv_blocks = jnp.stack([key_rot.reshape(blocks_here, BLOCK, width_here), value_view], axis=1)
    outgoing = kv_blocks[send_local]
    outgoing, reduced = lax.optimization_barrier((outgoing, reduced))
    incoming = lax.all_to_all(outgoing, "seq", split_axis=0, concat_axis=0, tiled=True)
    my_owners = owners[seq_place]
    my_ranks = ranks[seq_place]
    chunk_count = seq_count * capacity
    slot_chunk = (my_owners * capacity + my_ranks).reshape(blocks_here, RAND)
    chunk_valid = jnp.any(
        slot_chunk[:, :, None] == jnp.arange(chunk_count)[None, None, :], axis=1
    )
    incoming = incoming.reshape(chunk_count, 2, BLOCK, width_here)
    near_part = partial_attend(query_view, near_kv[0], near_kv[1], near_valid)
    far_part = shared_attend(query_view, incoming[:, 0], incoming[:, 1], chunk_valid)
    attended = merge_attend(near_part, far_part)
    mix_sum = reduced[:, :width_here].reshape(row_total, heads_here, HEAD_DIM)
    total_sum = reduced[:, width_here : width_here + heads_here]
    global_out = (mix_sum / total_sum[..., None]).reshape(row_total, width_here).astype(jnp.bfloat16)
    global_out = global_out.reshape(GLOB, BLOCK, width_here)
    block_index = jnp.arange(blocks_here)
    for global_slot in range(GLOB):
        hit = mine_global[global_slot] & (block_index == local_global[global_slot])
        attended = jnp.where(hit[:, None, None], global_out[global_slot][None], attended)
    mixed = sum_over_head(head_partials(attended.reshape(tok_here, width_here), out_weight))
    return mixed.astype(jnp.bfloat16)


def solution(mesh):
    in_specs = (
        P("seq", "head"),
        P("seq", "head"),
        P("seq", "head"),
        P("head", None),
        P(),
        P(),
        P("head"),
        P(),
        P(),
    )
    out_specs = P("seq", "head")
    return jax.shard_map(
        on_device, mesh=mesh, in_specs=in_specs, out_specs=out_specs, check_vma=False
    )
```

```python
import math

import jax
import jax.numpy as jnp
from jax import lax
from jax.sharding import PartitionSpec as P

HEAD_DIM = 128
BLOCK = 64
GLOB = 2
RAND = 3
WMAX = 2


masked_score = -1e30


def padded_2(cells, sides, width):
    for axis, dim in sides:
        count = lax.axis_size(axis)
        ends = count - 1
        head = lax.slice_in_dim(cells, 0, width, axis=dim)
        tail = lax.slice_in_dim(cells, cells.shape[dim] - width, cells.shape[dim], axis=dim)
        cells = jnp.concatenate(
            [
                lax.ppermute(tail, axis, [(i, (i + 1) % count) for i in range(ends)]),
                cells,
                lax.ppermute(head, axis, [((i + 1) % count, i) for i in range(ends)]),
            ],
            axis=dim,
        )
    return cells


def yarn_tables(yarn_scale, yarn_context):
    half_dim = HEAD_DIM // 2
    pair_index = jnp.arange(half_dim).astype(jnp.float32)
    base_rate = 10000.0 ** (-2.0 * pair_index / HEAD_DIM)
    factor = yarn_scale[0].astype(jnp.float32)
    context = yarn_context[0].astype(jnp.float32)
    turn_ratio = context * base_rate / (2.0 * math.pi)
    ramp_weight = jnp.clip((turn_ratio - 1.0) / 31.0, 0.0, 1.0)
    frequency = base_rate * ((1.0 - ramp_weight) / factor + ramp_weight)
    mscale = 0.1 * jnp.log(factor) + 1.0
    return (frequency, mscale)


def rotate(source, first_row, frequency, mscale):
    row_count, row_width = source.shape
    half_dim = HEAD_DIM // 2
    position = (first_row + jnp.arange(row_count)).astype(jnp.float32)
    angle_table = position[:, None] * frequency[None, :]
    cosine = jnp.cos(angle_table) * mscale
    sine_part = jnp.sin(angle_table) * mscale
    cosine = jnp.concatenate([cosine, cosine], axis=1)[:, None, :]
    sine_part = jnp.concatenate([sine_part, sine_part], axis=1)[:, None, :]
    grid = source.astype(jnp.float32).reshape(row_count, row_width // HEAD_DIM, HEAD_DIM)
    turned_half = jnp.concatenate([-grid[..., half_dim:], grid[..., :half_dim]], axis=2)
    turned = grid * cosine + turned_half * sine_part
    return turned.reshape(row_count, row_width).astype(jnp.bfloat16)


def block_attend(query_blocks, key_blocks, value_blocks, valid_slots):
    count_q, slot_count = (key_blocks.shape[0], key_blocks.shape[1])
    heads_here = query_blocks.shape[-1] // HEAD_DIM
    query_grid = query_blocks.reshape(count_q, BLOCK, heads_here, HEAD_DIM)
    key_grid = key_blocks.reshape(count_q, slot_count * BLOCK, heads_here, HEAD_DIM)
    value_grid = value_blocks.reshape(count_q, slot_count * BLOCK, heads_here, HEAD_DIM)
    scores = jnp.einsum(
        "bqhd,bshd->bhqs", query_grid, key_grid, preferred_element_type=jnp.float32
    ) * (1.0 / math.sqrt(HEAD_DIM))
    present = jnp.repeat(jnp.transpose(valid_slots, (0, 2, 1)), BLOCK, axis=2)[:, :, None, :]
    scores = jnp.where(present, scores, masked_score)
    peak = jnp.max(scores, axis=3, keepdims=True)
    expo = jnp.exp(scores - peak)
    total = jnp.sum(expo, axis=3)
    weights = expo.astype(jnp.bfloat16)
    mixture = jnp.einsum("bhqs,bshd->bqhd", weights, value_grid, preferred_element_type=jnp.float32)
    mixture = mixture / jnp.transpose(total, (0, 2, 1))[..., None]
    return mixture.reshape(count_q, BLOCK, heads_here * HEAD_DIM).astype(jnp.bfloat16)


def xor_perm(count, bit):
    return [(i, i ^ bit) for i in range(count)]


def tree_reduce(parts, merge, axis):
    count = lax.axis_size(axis)
    place = lax.axis_index(axis)
    bits = []
    bit = 1
    while bit < count:
        bits.append(bit)
        bit *= 2
    for bit in bits:
        upper = (place // bit) % 2
        halves = jax.tree.map(lambda x: x.reshape((2, x.shape[0] // 2) + x.shape[1:]), parts)
        keep = jax.tree.map(lambda h: lax.dynamic_index_in_dim(h, upper, 0, keepdims=False), halves)
        send = jax.tree.map(lambda h: lax.dynamic_index_in_dim(h, 1 - upper, 0, keepdims=False), halves)
        got = lax.ppermute(send, axis, xor_perm(count, bit))
        parts = merge(keep, got)
    for bit in reversed(bits):
        upper = (place // bit) % 2
        got = lax.ppermute(parts, axis, xor_perm(count, bit))

        def join(mine, theirs):
            pair = jnp.stack([mine, theirs])
            first = lax.dynamic_index_in_dim(pair, upper, 0, keepdims=False)
            second = lax.dynamic_index_in_dim(pair, 1 - upper, 0, keepdims=False)
            return jnp.concatenate([first, second], axis=0)

        parts = jax.tree.map(join, parts, got)
    return parts


def add_merge(a, b):
    return jax.tree.map(jnp.add, a, b)


def softmax_merge(a, b):
    width = a.shape[1] - 128
    heads = width // HEAD_DIM
    peak_a = a[:, width + heads : width + 2 * heads]
    peak_b = b[:, width + heads : width + 2 * heads]
    peak = jnp.maximum(peak_a, peak_b)
    scale_a = jnp.exp(peak_a - peak)
    scale_b = jnp.exp(peak_b - peak)
    rows = a.shape[0]
    mix = (
        a[:, :width].reshape(rows, heads, HEAD_DIM) * scale_a[..., None]
        + b[:, :width].reshape(rows, heads, HEAD_DIM) * scale_b[..., None]
    ).reshape(rows, width)
    total = a[:, width : width + heads] * scale_a + b[:, width : width + heads] * scale_b
    pad = jnp.zeros((rows, 128 - 2 * heads), a.dtype)
    return jnp.concatenate([mix, total, peak, pad], axis=1)


def head_partials(rows, out_weight):
    head_count = lax.axis_size("head")
    partial = lax.dot_general(
        out_weight, rows, (((0,), (1,)), ((), ())), preferred_element_type=jnp.float32
    ).astype(jnp.bfloat16)
    return partial.reshape(head_count, out_weight.shape[1] // head_count, rows.shape[0])


def sum_over_head(partial):
    gathered = lax.all_to_all(partial, "head", 0, 0, tiled=True)
    return jnp.sum(gathered.astype(jnp.float32), axis=0).T


def partial_attend(query_blocks, key_blocks, value_blocks, valid_slots):
    count_q, slot_count = (key_blocks.shape[0], key_blocks.shape[1])
    heads_here = query_blocks.shape[-1] // HEAD_DIM
    query_grid = query_blocks.reshape(count_q, BLOCK, heads_here, HEAD_DIM)
    key_grid = key_blocks.reshape(count_q, slot_count * BLOCK, heads_here, HEAD_DIM)
    value_grid = value_blocks.reshape(count_q, slot_count * BLOCK, heads_here, HEAD_DIM)
    scores = jnp.einsum(
        "bqhd,bshd->bhqs", query_grid, key_grid, preferred_element_type=jnp.float32
    ) * (1.0 / math.sqrt(HEAD_DIM))
    present = jnp.repeat(jnp.transpose(valid_slots, (0, 2, 1)), BLOCK, axis=2)[:, :, None, :]
    scores = jnp.where(present, scores, masked_score)
    peak = jnp.max(scores, axis=3)
    expo = jnp.exp(scores - peak[..., None])
    total = jnp.sum(expo, axis=3)
    mixture = jnp.einsum(
        "bhqs,bshd->bqhd", expo.astype(jnp.bfloat16), value_grid, preferred_element_type=jnp.float32
    )
    return mixture, total, peak


def merge_attend(first, second):
    mix_a, total_a, peak_a = first
    mix_b, total_b, peak_b = second
    peak = jnp.maximum(peak_a, peak_b)
    scale_a = jnp.exp(peak_a - peak)
    scale_b = jnp.exp(peak_b - peak)
    total = total_a * scale_a + total_b * scale_b
    mix = mix_a * jnp.transpose(scale_a, (0, 2, 1))[..., None] + mix_b * jnp.transpose(scale_b, (0, 2, 1))[..., None]
    mix = mix / jnp.transpose(total, (0, 2, 1))[..., None]
    count_q = mix.shape[0]
    return mix.reshape(count_q, BLOCK, -1).astype(jnp.bfloat16)


def on_device(
    queries,
    keys,
    values,
    out_weight,
    global_blocks,
    random_blocks,
    window_blocks,
    yarn_scale,
    yarn_context,
):
    tok_here, width_here = queries.shape
    heads_here = width_here // HEAD_DIM
    blocks_here = tok_here // BLOCK
    seq_count = lax.axis_size("seq")
    seq_place = lax.axis_index("seq")
    block_total = seq_count * blocks_here
    frequency, mscale = yarn_tables(yarn_scale, yarn_context)
    first_row = seq_place * tok_here
    query_rot = rotate(queries, first_row, frequency, mscale)
    key_rot = rotate(keys, first_row, frequency, mscale)
    pair_kv = jnp.stack([key_rot, values])
    halo = WMAX * BLOCK
    seq_ends = seq_count - 1
    from_left = lax.ppermute(
        pair_kv[:, tok_here - halo :], "seq", [(i, (i + 1) % seq_count) for i in range(seq_ends)]
    ).reshape(2, WMAX, BLOCK, width_here)
    from_right = lax.ppermute(
        pair_kv[:, :halo], "seq", [((i + 1) % seq_count, i) for i in range(seq_ends)]
    ).reshape(2, WMAX, BLOCK, width_here)
    local_blocks = pair_kv.reshape(2, blocks_here, BLOCK, width_here)

    def padded_block(index):
        if index < WMAX:
            return from_left[:, index]
        if index < WMAX + blocks_here:
            return local_blocks[:, index - WMAX]
        return from_right[:, index - WMAX - blocks_here]

    offsets = jnp.arange(-WMAX, WMAX + 1)
    window_ids = seq_place * blocks_here + jnp.arange(blocks_here)[:, None] + offsets[None, :]
    inside = (window_ids >= 0) & (window_ids < block_total)
    reach = jnp.abs(offsets)[None, :, None] <= window_blocks[None, None, :]
    window_valid = inside[:, :, None] & reach
    owner_global = global_blocks // blocks_here
    local_global = jnp.clip(global_blocks - seq_place * blocks_here, 0, blocks_here - 1)
    mine_global = owner_global == seq_place
    query_view = query_rot.reshape(blocks_here, BLOCK, width_here)
    key_view = key_rot.reshape(blocks_here, BLOCK, width_here)
    value_view = values.reshape(blocks_here, BLOCK, width_here)
    picked = jnp.stack([query_view[local_global], key_view[local_global], value_view[local_global]])
    masked = jnp.where(mine_global[None, :, None, None], picked, jnp.zeros_like(picked))
    shared = tree_reduce(masked.reshape(3 * GLOB * BLOCK, width_here), add_merge, "seq")
    shared = shared.reshape(3, GLOB, BLOCK, width_here)
    slot_parts = [
        jnp.stack(
            [padded_block(block + offset_slot) for offset_slot in range(2 * WMAX + 1)], axis=1
        )
        for block in range(blocks_here)
    ]
    global_kv = jnp.broadcast_to(shared[1:3][:, None], (2, blocks_here, GLOB, BLOCK, width_here))
    near_kv = jnp.concatenate([jnp.stack(slot_parts, axis=1), global_kv], axis=2)
    near_valid = jnp.concatenate(
        [window_valid, jnp.ones((blocks_here, GLOB, heads_here), dtype=bool)], axis=1
    )
    global_query = shared[0]
    key_later = key_rot
    value_later = values
    global_query = global_query.reshape(GLOB, BLOCK, heads_here, HEAD_DIM)
    key_grid = key_later.reshape(tok_here, heads_here, HEAD_DIM)
    value_grid = value_later.reshape(tok_here, heads_here, HEAD_DIM)
    global_scores = jnp.einsum(
        "gqhd,khd->gqhk", global_query, key_grid, preferred_element_type=jnp.float32
    ) * (1.0 / math.sqrt(HEAD_DIM))
    local_peak = jnp.max(global_scores, axis=3)
    expo = jnp.exp(global_scores - local_peak[..., None])
    partial_total = jnp.sum(expo, axis=3)
    partial_mix = jnp.einsum(
        "gqhk,khd->gqhd", expo.astype(jnp.bfloat16), value_grid, preferred_element_type=jnp.float32
    )
    row_total = GLOB * BLOCK
    packed = jnp.concatenate(
        [
            partial_mix.reshape(row_total, width_here),
            partial_total.reshape(row_total, heads_here),
            local_peak.reshape(row_total, heads_here),
            jnp.zeros((row_total, 128 - 2 * heads_here), jnp.float32),
        ],
        axis=1,
    )
    reduced = tree_reduce(packed, softmax_merge, "seq")
    slot_total = blocks_here * RAND
    capacity = (slot_total + seq_count - 1) // seq_count
    flat_ids = random_blocks.reshape(seq_count, slot_total)
    owners = flat_ids // blocks_here
    slot_order = jnp.arange(slot_total)
    same_owner = (owners[:, :, None] == owners[:, None, :]) & (
        slot_order[None, None, :] < slot_order[None, :, None]
    )
    ranks = jnp.sum(same_owner.astype(jnp.int32), axis=2)
    local_ids = flat_ids - owners * blocks_here
    wanted = (owners[:, None, :] == seq_place) & (
        ranks[:, None, :] == jnp.arange(capacity)[None, :, None]
    )
    send_local = jnp.sum(jnp.where(wanted, local_ids[:, None, :], 0), axis=2)
    kv_blocks = jnp.stack([key_rot.reshape(blocks_here, BLOCK, width_here), value_view], axis=1)
    outgoing = kv_blocks[send_local]
    outgoing, reduced = lax.optimization_barrier((outgoing, reduced))
    incoming = lax.all_to_all(outgoing, "seq", split_axis=0, concat_axis=0, tiled=True)
    my_owners = owners[seq_place]
    my_ranks = ranks[seq_place]
    random_k = incoming[my_owners, my_ranks, 0].reshape(blocks_here, RAND, BLOCK, width_here)
    random_v = incoming[my_owners, my_ranks, 1].reshape(blocks_here, RAND, BLOCK, width_here)
    random_kv = (random_k, random_v)
    near_part = partial_attend(query_view, near_kv[0], near_kv[1], near_valid)
    far_part = partial_attend(
        query_view, random_kv[0], random_kv[1], jnp.ones((blocks_here, RAND, heads_here), dtype=bool)
    )
    attended = merge_attend(near_part, far_part)
    mix_sum = reduced[:, :width_here].reshape(row_total, heads_here, HEAD_DIM)
    total_sum = reduced[:, width_here : width_here + heads_here]
    global_out = (mix_sum / total_sum[..., None]).reshape(row_total, width_here).astype(jnp.bfloat16)
    global_out = global_out.reshape(GLOB, BLOCK, width_here)
    block_index = jnp.arange(blocks_here)
    for global_slot in range(GLOB):
        hit = mine_global[global_slot] & (block_index == local_global[global_slot])
        attended = jnp.where(hit[:, None, None], global_out[global_slot][None], attended)
    mixed = sum_over_head(head_partials(attended.reshape(tok_here, width_here), out_weight))
    return mixed.astype(jnp.bfloat16)


def solution(mesh):
    in_specs = (
        P("seq", "head"),
        P("seq", "head"),
        P("seq", "head"),
        P("head", None),
        P(),
        P(),
        P("head"),
        P(),
        P(),
    )
    out_specs = P("seq", "head")
    return jax.shard_map(
        on_device, mesh=mesh, in_specs=in_specs, out_specs=out_specs, check_vma=False
    )
```

```python
import math

import jax
import jax.numpy as jnp
from jax import lax
from jax.sharding import PartitionSpec as P

HEAD_DIM = 128
BLOCK = 64
GLOB = 2
RAND = 3
WMAX = 2


masked_score = -1e30


def padded_2(cells, sides, width):
    for axis, dim in sides:
        count = lax.axis_size(axis)
        ends = count - 1
        head = lax.slice_in_dim(cells, 0, width, axis=dim)
        tail = lax.slice_in_dim(cells, cells.shape[dim] - width, cells.shape[dim], axis=dim)
        cells = jnp.concatenate(
            [
                lax.ppermute(tail, axis, [(i, (i + 1) % count) for i in range(ends)]),
                cells,
                lax.ppermute(head, axis, [((i + 1) % count, i) for i in range(ends)]),
            ],
            axis=dim,
        )
    return cells


def yarn_tables(yarn_scale, yarn_context):
    half_dim = HEAD_DIM // 2
    pair_index = jnp.arange(half_dim).astype(jnp.float32)
    base_rate = 10000.0 ** (-2.0 * pair_index / HEAD_DIM)
    factor = yarn_scale[0].astype(jnp.float32)
    context = yarn_context[0].astype(jnp.float32)
    turn_ratio = context * base_rate / (2.0 * math.pi)
    ramp_weight = jnp.clip((turn_ratio - 1.0) / 31.0, 0.0, 1.0)
    frequency = base_rate * ((1.0 - ramp_weight) / factor + ramp_weight)
    mscale = 0.1 * jnp.log(factor) + 1.0
    return (frequency, mscale)


def rotate(source, first_row, frequency, mscale):
    row_count, row_width = source.shape
    half_dim = HEAD_DIM // 2
    position = (first_row + jnp.arange(row_count)).astype(jnp.float32)
    angle_table = position[:, None] * frequency[None, :]
    cosine = jnp.cos(angle_table) * mscale
    sine_part = jnp.sin(angle_table) * mscale
    cosine = jnp.concatenate([cosine, cosine], axis=1)[:, None, :]
    sine_part = jnp.concatenate([sine_part, sine_part], axis=1)[:, None, :]
    grid = source.astype(jnp.float32).reshape(row_count, row_width // HEAD_DIM, HEAD_DIM)
    turned_half = jnp.concatenate([-grid[..., half_dim:], grid[..., :half_dim]], axis=2)
    turned = grid * cosine + turned_half * sine_part
    return turned.reshape(row_count, row_width).astype(jnp.bfloat16)


def block_attend(query_blocks, key_blocks, value_blocks, valid_slots):
    count_q, slot_count = (key_blocks.shape[0], key_blocks.shape[1])
    heads_here = query_blocks.shape[-1] // HEAD_DIM
    query_grid = query_blocks.reshape(count_q, BLOCK, heads_here, HEAD_DIM)
    key_grid = key_blocks.reshape(count_q, slot_count * BLOCK, heads_here, HEAD_DIM)
    value_grid = value_blocks.reshape(count_q, slot_count * BLOCK, heads_here, HEAD_DIM)
    scores = jnp.einsum(
        "bqhd,bshd->bhqs", query_grid, key_grid, preferred_element_type=jnp.float32
    ) * (1.0 / math.sqrt(HEAD_DIM))
    present = jnp.repeat(jnp.transpose(valid_slots, (0, 2, 1)), BLOCK, axis=2)[:, :, None, :]
    scores = jnp.where(present, scores, masked_score)
    peak = jnp.max(scores, axis=3, keepdims=True)
    expo = jnp.exp(scores - peak)
    total = jnp.sum(expo, axis=3)
    weights = expo.astype(jnp.bfloat16)
    mixture = jnp.einsum("bhqs,bshd->bqhd", weights, value_grid, preferred_element_type=jnp.float32)
    mixture = mixture / jnp.transpose(total, (0, 2, 1))[..., None]
    return mixture.reshape(count_q, BLOCK, heads_here * HEAD_DIM).astype(jnp.bfloat16)


def xor_perm(count, bit):
    return [(i, i ^ bit) for i in range(count)]


def tree_reduce(parts, merge, axis):
    count = lax.axis_size(axis)
    place = lax.axis_index(axis)
    bits = []
    bit = 1
    while bit < count:
        bits.append(bit)
        bit *= 2
    for bit in bits:
        upper = (place // bit) % 2
        halves = jax.tree.map(lambda x: x.reshape((2, x.shape[0] // 2) + x.shape[1:]), parts)
        keep = jax.tree.map(lambda h: lax.dynamic_index_in_dim(h, upper, 0, keepdims=False), halves)
        send = jax.tree.map(lambda h: lax.dynamic_index_in_dim(h, 1 - upper, 0, keepdims=False), halves)
        got = lax.ppermute(send, axis, xor_perm(count, bit))
        parts = merge(keep, got)
    for bit in reversed(bits):
        upper = (place // bit) % 2
        got = lax.ppermute(parts, axis, xor_perm(count, bit))

        def join(mine, theirs):
            pair = jnp.stack([mine, theirs])
            first = lax.dynamic_index_in_dim(pair, upper, 0, keepdims=False)
            second = lax.dynamic_index_in_dim(pair, 1 - upper, 0, keepdims=False)
            return jnp.concatenate([first, second], axis=0)

        parts = jax.tree.map(join, parts, got)
    return parts


def add_merge(a, b):
    return jax.tree.map(jnp.add, a, b)


def softmax_merge(a, b):
    width = a.shape[1] - 128
    heads = width // HEAD_DIM
    peak_a = a[:, width + heads : width + 2 * heads]
    peak_b = b[:, width + heads : width + 2 * heads]
    peak = jnp.maximum(peak_a, peak_b)
    scale_a = jnp.exp(peak_a - peak)
    scale_b = jnp.exp(peak_b - peak)
    rows = a.shape[0]
    mix = (
        a[:, :width].reshape(rows, heads, HEAD_DIM) * scale_a[..., None]
        + b[:, :width].reshape(rows, heads, HEAD_DIM) * scale_b[..., None]
    ).reshape(rows, width)
    total = a[:, width : width + heads] * scale_a + b[:, width : width + heads] * scale_b
    pad = jnp.zeros((rows, 128 - 2 * heads), a.dtype)
    return jnp.concatenate([mix, total, peak, pad], axis=1)


def head_partials(rows, out_weight):
    head_count = lax.axis_size("head")
    partial = lax.dot_general(
        out_weight, rows, (((0,), (1,)), ((), ())), preferred_element_type=jnp.float32
    ).astype(jnp.bfloat16)
    return partial.reshape(head_count, out_weight.shape[1] // head_count, rows.shape[0])


def sum_over_head(partial):
    gathered = lax.all_to_all(partial, "head", 0, 0, tiled=True)
    return jnp.sum(gathered.astype(jnp.float32), axis=0).T


def partial_attend(query_blocks, key_blocks, value_blocks, valid_slots):
    count_q, slot_count = (key_blocks.shape[0], key_blocks.shape[1])
    heads_here = query_blocks.shape[-1] // HEAD_DIM
    query_grid = query_blocks.reshape(count_q, BLOCK, heads_here, HEAD_DIM)
    key_grid = key_blocks.reshape(count_q, slot_count * BLOCK, heads_here, HEAD_DIM)
    value_grid = value_blocks.reshape(count_q, slot_count * BLOCK, heads_here, HEAD_DIM)
    scores = jnp.einsum(
        "bqhd,bshd->bhqs", query_grid, key_grid, preferred_element_type=jnp.float32
    ) * (1.0 / math.sqrt(HEAD_DIM))
    present = jnp.repeat(jnp.transpose(valid_slots, (0, 2, 1)), BLOCK, axis=2)[:, :, None, :]
    scores = jnp.where(present, scores, masked_score)
    peak = jnp.max(scores, axis=3)
    expo = jnp.exp(scores - peak[..., None])
    total = jnp.sum(expo, axis=3)
    mixture = jnp.einsum(
        "bhqs,bshd->bqhd", expo.astype(jnp.bfloat16), value_grid, preferred_element_type=jnp.float32
    )
    return mixture, total, peak


def merge_attend(first, second):
    mix_a, total_a, peak_a = first
    mix_b, total_b, peak_b = second
    peak = jnp.maximum(peak_a, peak_b)
    scale_a = jnp.exp(peak_a - peak)
    scale_b = jnp.exp(peak_b - peak)
    total = total_a * scale_a + total_b * scale_b
    mix = mix_a * jnp.transpose(scale_a, (0, 2, 1))[..., None] + mix_b * jnp.transpose(scale_b, (0, 2, 1))[..., None]
    mix = mix / jnp.transpose(total, (0, 2, 1))[..., None]
    count_q = mix.shape[0]
    return mix.reshape(count_q, BLOCK, -1).astype(jnp.bfloat16)


def on_device(
    queries,
    keys,
    values,
    out_weight,
    global_blocks,
    random_blocks,
    window_blocks,
    yarn_scale,
    yarn_context,
):
    tok_here, width_here = queries.shape
    heads_here = width_here // HEAD_DIM
    blocks_here = tok_here // BLOCK
    seq_count = lax.axis_size("seq")
    seq_place = lax.axis_index("seq")
    block_total = seq_count * blocks_here
    frequency, mscale = yarn_tables(yarn_scale, yarn_context)
    first_row = seq_place * tok_here
    query_rot = rotate(queries, first_row, frequency, mscale)
    key_rot = rotate(keys, first_row, frequency, mscale)
    pair_kv = jnp.stack([key_rot, values])
    local_blocks = pair_kv.reshape(2, blocks_here, BLOCK, width_here)

    def padded_block(index):
        if index < WMAX:
            return from_left[:, index]
        if index < WMAX + blocks_here:
            return local_blocks[:, index - WMAX]
        return from_right[:, index - WMAX - blocks_here]

    offsets = jnp.arange(-WMAX, WMAX + 1)
    window_ids = seq_place * blocks_here + jnp.arange(blocks_here)[:, None] + offsets[None, :]
    inside = (window_ids >= 0) & (window_ids < block_total)
    reach = jnp.abs(offsets)[None, :, None] <= window_blocks[None, None, :]
    window_valid = inside[:, :, None] & reach
    owner_global = global_blocks // blocks_here
    local_global = jnp.clip(global_blocks - seq_place * blocks_here, 0, blocks_here - 1)
    mine_global = owner_global == seq_place
    query_view = query_rot.reshape(blocks_here, BLOCK, width_here)
    key_view = key_rot.reshape(blocks_here, BLOCK, width_here)
    value_view = values.reshape(blocks_here, BLOCK, width_here)
    picked = jnp.stack([query_view[local_global], key_view[local_global], value_view[local_global]])
    masked = jnp.where(mine_global[None, :, None, None], picked, jnp.zeros_like(picked))
    shared = tree_reduce(masked.reshape(3 * GLOB * BLOCK, width_here), add_merge, "seq")
    shared = shared.reshape(3, GLOB, BLOCK, width_here)
    halo = WMAX * BLOCK
    seq_ends = seq_count - 1
    halo_kv, shared = lax.optimization_barrier((pair_kv, shared))
    from_left = lax.ppermute(
        halo_kv[:, tok_here - halo :], "seq", [(i, (i + 1) % seq_count) for i in range(seq_ends)]
    ).reshape(2, WMAX, BLOCK, width_here)
    from_right = lax.ppermute(
        halo_kv[:, :halo], "seq", [((i + 1) % seq_count, i) for i in range(seq_ends)]
    ).reshape(2, WMAX, BLOCK, width_here)
    slot_parts = [
        jnp.stack(
            [padded_block(block + offset_slot) for offset_slot in range(2 * WMAX + 1)], axis=1
        )
        for block in range(blocks_here)
    ]
    global_kv = jnp.broadcast_to(shared[1:3][:, None], (2, blocks_here, GLOB, BLOCK, width_here))
    near_kv = jnp.concatenate([jnp.stack(slot_parts, axis=1), global_kv], axis=2)
    near_valid = jnp.concatenate(
        [window_valid, jnp.ones((blocks_here, GLOB, heads_here), dtype=bool)], axis=1
    )
    global_query = shared[0]
    key_later = key_rot
    value_later = values
    global_query = global_query.reshape(GLOB, BLOCK, heads_here, HEAD_DIM)
    key_grid = key_later.reshape(tok_here, heads_here, HEAD_DIM)
    value_grid = value_later.reshape(tok_here, heads_here, HEAD_DIM)
    global_scores = jnp.einsum(
        "gqhd,khd->gqhk", global_query, key_grid, preferred_element_type=jnp.float32
    ) * (1.0 / math.sqrt(HEAD_DIM))
    local_peak = jnp.max(global_scores, axis=3)
    expo = jnp.exp(global_scores - local_peak[..., None])
    partial_total = jnp.sum(expo, axis=3)
    partial_mix = jnp.einsum(
        "gqhk,khd->gqhd", expo.astype(jnp.bfloat16), value_grid, preferred_element_type=jnp.float32
    )
    row_total = GLOB * BLOCK
    packed = jnp.concatenate(
        [
            partial_mix.reshape(row_total, width_here),
            partial_total.reshape(row_total, heads_here),
            local_peak.reshape(row_total, heads_here),
            jnp.zeros((row_total, 128 - 2 * heads_here), jnp.float32),
        ],
        axis=1,
    )
    packed, from_left, from_right = lax.optimization_barrier((packed, from_left, from_right))
    reduced = tree_reduce(packed, softmax_merge, "seq")
    slot_total = blocks_here * RAND
    capacity = (slot_total + seq_count - 1) // seq_count
    flat_ids = random_blocks.reshape(seq_count, slot_total)
    owners = flat_ids // blocks_here
    slot_order = jnp.arange(slot_total)
    same_owner = (owners[:, :, None] == owners[:, None, :]) & (
        slot_order[None, None, :] < slot_order[None, :, None]
    )
    ranks = jnp.sum(same_owner.astype(jnp.int32), axis=2)
    local_ids = flat_ids - owners * blocks_here
    wanted = (owners[:, None, :] == seq_place) & (
        ranks[:, None, :] == jnp.arange(capacity)[None, :, None]
    )
    send_local = jnp.sum(jnp.where(wanted, local_ids[:, None, :], 0), axis=2)
    kv_blocks = jnp.stack([key_rot.reshape(blocks_here, BLOCK, width_here), value_view], axis=1)
    outgoing = kv_blocks[send_local]
    outgoing, reduced = lax.optimization_barrier((outgoing, reduced))
    incoming = lax.all_to_all(outgoing, "seq", split_axis=0, concat_axis=0, tiled=True)
    my_owners = owners[seq_place]
    my_ranks = ranks[seq_place]
    random_k = incoming[my_owners, my_ranks, 0].reshape(blocks_here, RAND, BLOCK, width_here)
    random_v = incoming[my_owners, my_ranks, 1].reshape(blocks_here, RAND, BLOCK, width_here)
    random_kv = (random_k, random_v)
    near_part = partial_attend(query_view, near_kv[0], near_kv[1], near_valid)
    far_part = partial_attend(
        query_view, random_kv[0], random_kv[1], jnp.ones((blocks_here, RAND, heads_here), dtype=bool)
    )
    attended = merge_attend(near_part, far_part)
    mix_sum = reduced[:, :width_here].reshape(row_total, heads_here, HEAD_DIM)
    total_sum = reduced[:, width_here : width_here + heads_here]
    global_out = (mix_sum / total_sum[..., None]).reshape(row_total, width_here).astype(jnp.bfloat16)
    global_out = global_out.reshape(GLOB, BLOCK, width_here)
    block_index = jnp.arange(blocks_here)
    for global_slot in range(GLOB):
        hit = mine_global[global_slot] & (block_index == local_global[global_slot])
        attended = jnp.where(hit[:, None, None], global_out[global_slot][None], attended)
    mixed = sum_over_head(head_partials(attended.reshape(tok_here, width_here), out_weight))
    return mixed.astype(jnp.bfloat16)


def solution(mesh):
    in_specs = (
        P("seq", "head"),
        P("seq", "head"),
        P("seq", "head"),
        P("head", None),
        P(),
        P(),
        P("head"),
        P(),
        P(),
    )
    out_specs = P("seq", "head")
    return jax.shard_map(
        on_device, mesh=mesh, in_specs=in_specs, out_specs=out_specs, check_vma=False
    )
```

```python
import math

import jax
import jax.numpy as jnp
from jax import lax
from jax.sharding import PartitionSpec as P

HEAD_DIM = 128
BLOCK = 64
GLOB = 2
RAND = 3
WMAX = 2


masked_score = -1e30


def padded_2(cells, sides, width):
    for axis, dim in sides:
        count = lax.axis_size(axis)
        ends = count - 1
        head = lax.slice_in_dim(cells, 0, width, axis=dim)
        tail = lax.slice_in_dim(cells, cells.shape[dim] - width, cells.shape[dim], axis=dim)
        cells = jnp.concatenate(
            [
                lax.ppermute(tail, axis, [(i, (i + 1) % count) for i in range(ends)]),
                cells,
                lax.ppermute(head, axis, [((i + 1) % count, i) for i in range(ends)]),
            ],
            axis=dim,
        )
    return cells


def yarn_tables(yarn_scale, yarn_context):
    half_dim = HEAD_DIM // 2
    pair_index = jnp.arange(half_dim).astype(jnp.float32)
    base_rate = 10000.0 ** (-2.0 * pair_index / HEAD_DIM)
    factor = yarn_scale[0].astype(jnp.float32)
    context = yarn_context[0].astype(jnp.float32)
    turn_ratio = context * base_rate / (2.0 * math.pi)
    ramp_weight = jnp.clip((turn_ratio - 1.0) / 31.0, 0.0, 1.0)
    frequency = base_rate * ((1.0 - ramp_weight) / factor + ramp_weight)
    mscale = 0.1 * jnp.log(factor) + 1.0
    return (frequency, mscale)


def rotate(source, first_row, frequency, mscale):
    row_count, row_width = source.shape
    half_dim = HEAD_DIM // 2
    position = (first_row + jnp.arange(row_count)).astype(jnp.float32)
    angle_table = position[:, None] * frequency[None, :]
    cosine = jnp.cos(angle_table) * mscale
    sine_part = jnp.sin(angle_table) * mscale
    cosine = jnp.concatenate([cosine, cosine], axis=1)[:, None, :]
    sine_part = jnp.concatenate([sine_part, sine_part], axis=1)[:, None, :]
    grid = source.astype(jnp.float32).reshape(row_count, row_width // HEAD_DIM, HEAD_DIM)
    turned_half = jnp.concatenate([-grid[..., half_dim:], grid[..., :half_dim]], axis=2)
    turned = grid * cosine + turned_half * sine_part
    return turned.reshape(row_count, row_width).astype(jnp.bfloat16)


def block_attend(query_blocks, key_blocks, value_blocks, valid_slots):
    count_q, slot_count = (key_blocks.shape[0], key_blocks.shape[1])
    heads_here = query_blocks.shape[-1] // HEAD_DIM
    query_grid = query_blocks.reshape(count_q, BLOCK, heads_here, HEAD_DIM)
    key_grid = key_blocks.reshape(count_q, slot_count * BLOCK, heads_here, HEAD_DIM)
    value_grid = value_blocks.reshape(count_q, slot_count * BLOCK, heads_here, HEAD_DIM)
    scores = jnp.einsum(
        "bqhd,bshd->bhqs", query_grid, key_grid, preferred_element_type=jnp.float32
    ) * (1.0 / math.sqrt(HEAD_DIM))
    present = jnp.repeat(jnp.transpose(valid_slots, (0, 2, 1)), BLOCK, axis=2)[:, :, None, :]
    scores = jnp.where(present, scores, masked_score)
    peak = jnp.max(scores, axis=3, keepdims=True)
    expo = jnp.exp(scores - peak)
    total = jnp.sum(expo, axis=3)
    weights = expo.astype(jnp.bfloat16)
    mixture = jnp.einsum("bhqs,bshd->bqhd", weights, value_grid, preferred_element_type=jnp.float32)
    mixture = mixture / jnp.transpose(total, (0, 2, 1))[..., None]
    return mixture.reshape(count_q, BLOCK, heads_here * HEAD_DIM).astype(jnp.bfloat16)


def xor_perm(count, bit):
    return [(i, i ^ bit) for i in range(count)]


def tree_reduce(parts, merge, axis):
    count = lax.axis_size(axis)
    place = lax.axis_index(axis)
    bits = []
    bit = 1
    while bit < count:
        bits.append(bit)
        bit *= 2
    for bit in bits:
        upper = (place // bit) % 2
        halves = jax.tree.map(lambda x: x.reshape((2, x.shape[0] // 2) + x.shape[1:]), parts)
        keep = jax.tree.map(lambda h: lax.dynamic_index_in_dim(h, upper, 0, keepdims=False), halves)
        send = jax.tree.map(lambda h: lax.dynamic_index_in_dim(h, 1 - upper, 0, keepdims=False), halves)
        got = lax.ppermute(send, axis, xor_perm(count, bit))
        parts = merge(keep, got)
    for bit in reversed(bits):
        upper = (place // bit) % 2
        got = lax.ppermute(parts, axis, xor_perm(count, bit))

        def join(mine, theirs):
            pair = jnp.stack([mine, theirs])
            first = lax.dynamic_index_in_dim(pair, upper, 0, keepdims=False)
            second = lax.dynamic_index_in_dim(pair, 1 - upper, 0, keepdims=False)
            return jnp.concatenate([first, second], axis=0)

        parts = jax.tree.map(join, parts, got)
    return parts


def add_merge(a, b):
    return jax.tree.map(jnp.add, a, b)


def softmax_merge(a, b):
    width = a.shape[1] - 128
    heads = width // HEAD_DIM
    peak_a = a[:, width + heads : width + 2 * heads]
    peak_b = b[:, width + heads : width + 2 * heads]
    peak = jnp.maximum(peak_a, peak_b)
    scale_a = jnp.exp(peak_a - peak)
    scale_b = jnp.exp(peak_b - peak)
    rows = a.shape[0]
    mix = (
        a[:, :width].reshape(rows, heads, HEAD_DIM) * scale_a[..., None]
        + b[:, :width].reshape(rows, heads, HEAD_DIM) * scale_b[..., None]
    ).reshape(rows, width)
    total = a[:, width : width + heads] * scale_a + b[:, width : width + heads] * scale_b
    pad = jnp.zeros((rows, 128 - 2 * heads), a.dtype)
    return jnp.concatenate([mix, total, peak, pad], axis=1)


def head_partials(rows, out_weight):
    head_count = lax.axis_size("head")
    partial = lax.dot_general(
        out_weight, rows, (((0,), (1,)), ((), ())), preferred_element_type=jnp.float32
    ).astype(jnp.bfloat16)
    return partial.reshape(head_count, out_weight.shape[1] // head_count, rows.shape[0])


def sum_over_head(partial):
    gathered = lax.all_to_all(partial, "head", 0, 0, tiled=True)
    return jnp.sum(gathered.astype(jnp.float32), axis=0).T


def partial_attend(query_blocks, key_blocks, value_blocks, valid_slots):
    count_q, slot_count = (key_blocks.shape[0], key_blocks.shape[1])
    heads_here = query_blocks.shape[-1] // HEAD_DIM
    query_grid = query_blocks.reshape(count_q, BLOCK, heads_here, HEAD_DIM)
    key_grid = key_blocks.reshape(count_q, slot_count * BLOCK, heads_here, HEAD_DIM)
    value_grid = value_blocks.reshape(count_q, slot_count * BLOCK, heads_here, HEAD_DIM)
    scores = jnp.einsum(
        "bqhd,bshd->bhqs", query_grid, key_grid, preferred_element_type=jnp.float32
    ) * (1.0 / math.sqrt(HEAD_DIM))
    present = jnp.repeat(jnp.transpose(valid_slots, (0, 2, 1)), BLOCK, axis=2)[:, :, None, :]
    scores = jnp.where(present, scores, masked_score)
    peak = jnp.max(scores, axis=3)
    expo = jnp.exp(scores - peak[..., None])
    total = jnp.sum(expo, axis=3)
    mixture = jnp.einsum(
        "bhqs,bshd->bqhd", expo.astype(jnp.bfloat16), value_grid, preferred_element_type=jnp.float32
    )
    return mixture, total, peak


def merge_attend(first, second):
    mix_a, total_a, peak_a = first
    mix_b, total_b, peak_b = second
    peak = jnp.maximum(peak_a, peak_b)
    scale_a = jnp.exp(peak_a - peak)
    scale_b = jnp.exp(peak_b - peak)
    total = total_a * scale_a + total_b * scale_b
    mix = mix_a * jnp.transpose(scale_a, (0, 2, 1))[..., None] + mix_b * jnp.transpose(scale_b, (0, 2, 1))[..., None]
    mix = mix / jnp.transpose(total, (0, 2, 1))[..., None]
    count_q = mix.shape[0]
    return mix.reshape(count_q, BLOCK, -1).astype(jnp.bfloat16)


def on_device(
    queries,
    keys,
    values,
    out_weight,
    global_blocks,
    random_blocks,
    window_blocks,
    yarn_scale,
    yarn_context,
):
    tok_here, width_here = queries.shape
    heads_here = width_here // HEAD_DIM
    blocks_here = tok_here // BLOCK
    seq_count = lax.axis_size("seq")
    seq_place = lax.axis_index("seq")
    block_total = seq_count * blocks_here
    frequency, mscale = yarn_tables(yarn_scale, yarn_context)
    first_row = seq_place * tok_here
    query_rot = rotate(queries, first_row, frequency, mscale)
    key_rot = rotate(keys, first_row, frequency, mscale)
    pair_kv = jnp.stack([key_rot, values])
    local_blocks = pair_kv.reshape(2, blocks_here, BLOCK, width_here)

    def padded_block(index):
        if index < WMAX:
            return from_left[:, index]
        if index < WMAX + blocks_here:
            return local_blocks[:, index - WMAX]
        return from_right[:, index - WMAX - blocks_here]

    offsets = jnp.arange(-WMAX, WMAX + 1)
    window_ids = seq_place * blocks_here + jnp.arange(blocks_here)[:, None] + offsets[None, :]
    inside = (window_ids >= 0) & (window_ids < block_total)
    reach = jnp.abs(offsets)[None, :, None] <= window_blocks[None, None, :]
    window_valid = inside[:, :, None] & reach
    owner_global = global_blocks // blocks_here
    local_global = jnp.clip(global_blocks - seq_place * blocks_here, 0, blocks_here - 1)
    mine_global = owner_global == seq_place
    query_view = query_rot.reshape(blocks_here, BLOCK, width_here)
    key_view = key_rot.reshape(blocks_here, BLOCK, width_here)
    value_view = values.reshape(blocks_here, BLOCK, width_here)
    picked = jnp.stack([query_view[local_global], key_view[local_global], value_view[local_global]])
    masked = jnp.where(mine_global[None, :, None, None], picked, jnp.zeros_like(picked))
    shared = tree_reduce(masked.reshape(3 * GLOB * BLOCK, width_here), add_merge, "seq")
    shared = shared.reshape(3, GLOB, BLOCK, width_here)
    halo = WMAX * BLOCK
    seq_ends = seq_count - 1
    halo_kv, shared = lax.optimization_barrier((pair_kv, shared))
    from_left = lax.ppermute(
        halo_kv[:, tok_here - halo :], "seq", [(i, (i + 1) % seq_count) for i in range(seq_ends)]
    ).reshape(2, WMAX, BLOCK, width_here)
    from_right = lax.ppermute(
        halo_kv[:, :halo], "seq", [((i + 1) % seq_count, i) for i in range(seq_ends)]
    ).reshape(2, WMAX, BLOCK, width_here)
    slot_parts = [
        jnp.stack(
            [padded_block(block + offset_slot) for offset_slot in range(2 * WMAX + 1)], axis=1
        )
        for block in range(blocks_here)
    ]
    global_kv = jnp.broadcast_to(shared[1:3][:, None], (2, blocks_here, GLOB, BLOCK, width_here))
    near_kv = jnp.concatenate([jnp.stack(slot_parts, axis=1), global_kv], axis=2)
    near_valid = jnp.concatenate(
        [window_valid, jnp.ones((blocks_here, GLOB, heads_here), dtype=bool)], axis=1
    )
    global_query = shared[0]
    key_later = key_rot
    value_later = values
    global_query = global_query.reshape(GLOB, BLOCK, heads_here, HEAD_DIM)
    key_grid = key_later.reshape(tok_here, heads_here, HEAD_DIM)
    value_grid = value_later.reshape(tok_here, heads_here, HEAD_DIM)
    global_scores = jnp.einsum(
        "gqhd,khd->gqhk", global_query, key_grid, preferred_element_type=jnp.float32
    ) * (1.0 / math.sqrt(HEAD_DIM))
    local_peak = jnp.max(global_scores, axis=3)
    expo = jnp.exp(global_scores - local_peak[..., None])
    partial_total = jnp.sum(expo, axis=3)
    partial_mix = jnp.einsum(
        "gqhk,khd->gqhd", expo.astype(jnp.bfloat16), value_grid, preferred_element_type=jnp.float32
    )
    row_total = GLOB * BLOCK
    packed = jnp.concatenate(
        [
            partial_mix.reshape(row_total, width_here),
            partial_total.reshape(row_total, heads_here),
            local_peak.reshape(row_total, heads_here),
            jnp.zeros((row_total, 128 - 2 * heads_here), jnp.float32),
        ],
        axis=1,
    )
    packed, from_left, from_right = lax.optimization_barrier((packed, from_left, from_right))
    reduced = tree_reduce(packed, softmax_merge, "seq")
    slot_total = blocks_here * RAND
    capacity = (slot_total + seq_count - 1) // seq_count
    flat_ids = random_blocks.reshape(seq_count, slot_total)
    owners = flat_ids // blocks_here
    slot_order = jnp.arange(slot_total)
    same_owner = (owners[:, :, None] == owners[:, None, :]) & (
        slot_order[None, None, :] < slot_order[None, :, None]
    )
    ranks = jnp.sum(same_owner.astype(jnp.int32), axis=2)
    local_ids = flat_ids - owners * blocks_here
    wanted = (owners[:, None, :] == seq_place) & (
        ranks[:, None, :] == jnp.arange(capacity)[None, :, None]
    )
    send_local = jnp.sum(jnp.where(wanted, local_ids[:, None, :], 0), axis=2)
    key_blocks = key_rot.reshape(blocks_here, BLOCK, width_here)
    out_k = key_blocks[send_local]
    out_v = value_view[send_local]
    out_k, out_v, reduced = lax.optimization_barrier((out_k, out_v, reduced))
    in_k = lax.all_to_all(out_k, "seq", split_axis=0, concat_axis=0, tiled=True)
    out_v, in_k = lax.optimization_barrier((out_v, in_k))
    in_v = lax.all_to_all(out_v, "seq", split_axis=0, concat_axis=0, tiled=True)
    my_owners = owners[seq_place]
    my_ranks = ranks[seq_place]
    random_k = in_k[my_owners, my_ranks].reshape(blocks_here, RAND, BLOCK, width_here)
    random_v = in_v[my_owners, my_ranks].reshape(blocks_here, RAND, BLOCK, width_here)
    random_kv = (random_k, random_v)
    near_part = partial_attend(query_view, near_kv[0], near_kv[1], near_valid)
    far_part = partial_attend(
        query_view, random_kv[0], random_kv[1], jnp.ones((blocks_here, RAND, heads_here), dtype=bool)
    )
    attended = merge_attend(near_part, far_part)
    mix_sum = reduced[:, :width_here].reshape(row_total, heads_here, HEAD_DIM)
    total_sum = reduced[:, width_here : width_here + heads_here]
    global_out = (mix_sum / total_sum[..., None]).reshape(row_total, width_here).astype(jnp.bfloat16)
    global_out = global_out.reshape(GLOB, BLOCK, width_here)
    block_index = jnp.arange(blocks_here)
    for global_slot in range(GLOB):
        hit = mine_global[global_slot] & (block_index == local_global[global_slot])
        attended = jnp.where(hit[:, None, None], global_out[global_slot][None], attended)
    mixed = sum_over_head(head_partials(attended.reshape(tok_here, width_here), out_weight))
    return mixed.astype(jnp.bfloat16)


def solution(mesh):
    in_specs = (
        P("seq", "head"),
        P("seq", "head"),
        P("seq", "head"),
        P("head", None),
        P(),
        P(),
        P("head"),
        P(),
        P(),
    )
    out_specs = P("seq", "head")
    return jax.shard_map(
        on_device, mesh=mesh, in_specs=in_specs, out_specs=out_specs, check_vma=False
    )
```

```python
import math

import jax
import jax.numpy as jnp
from jax import lax
from jax.sharding import PartitionSpec as P

HEAD_DIM = 128
BLOCK = 64
GLOB = 2
RAND = 3
WMAX = 2


masked_score = -1e30


def padded_2(cells, sides, width):
    for axis, dim in sides:
        count = lax.axis_size(axis)
        ends = count - 1
        head = lax.slice_in_dim(cells, 0, width, axis=dim)
        tail = lax.slice_in_dim(cells, cells.shape[dim] - width, cells.shape[dim], axis=dim)
        cells = jnp.concatenate(
            [
                lax.ppermute(tail, axis, [(i, (i + 1) % count) for i in range(ends)]),
                cells,
                lax.ppermute(head, axis, [((i + 1) % count, i) for i in range(ends)]),
            ],
            axis=dim,
        )
    return cells


def yarn_tables(yarn_scale, yarn_context):
    half_dim = HEAD_DIM // 2
    pair_index = jnp.arange(half_dim).astype(jnp.float32)
    base_rate = 10000.0 ** (-2.0 * pair_index / HEAD_DIM)
    factor = yarn_scale[0].astype(jnp.float32)
    context = yarn_context[0].astype(jnp.float32)
    turn_ratio = context * base_rate / (2.0 * math.pi)
    ramp_weight = jnp.clip((turn_ratio - 1.0) / 31.0, 0.0, 1.0)
    frequency = base_rate * ((1.0 - ramp_weight) / factor + ramp_weight)
    mscale = 0.1 * jnp.log(factor) + 1.0
    return (frequency, mscale)


def rotate(source, first_row, frequency, mscale):
    row_count, row_width = source.shape
    half_dim = HEAD_DIM // 2
    position = (first_row + jnp.arange(row_count)).astype(jnp.float32)
    angle_table = position[:, None] * frequency[None, :]
    cosine = jnp.cos(angle_table) * mscale
    sine_part = jnp.sin(angle_table) * mscale
    cosine = jnp.concatenate([cosine, cosine], axis=1)[:, None, :]
    sine_part = jnp.concatenate([sine_part, sine_part], axis=1)[:, None, :]
    grid = source.astype(jnp.float32).reshape(row_count, row_width // HEAD_DIM, HEAD_DIM)
    turned_half = jnp.concatenate([-grid[..., half_dim:], grid[..., :half_dim]], axis=2)
    turned = grid * cosine + turned_half * sine_part
    return turned.reshape(row_count, row_width).astype(jnp.bfloat16)


def block_attend(query_blocks, key_blocks, value_blocks, valid_slots):
    count_q, slot_count = (key_blocks.shape[0], key_blocks.shape[1])
    heads_here = query_blocks.shape[-1] // HEAD_DIM
    query_grid = query_blocks.reshape(count_q, BLOCK, heads_here, HEAD_DIM)
    key_grid = key_blocks.reshape(count_q, slot_count * BLOCK, heads_here, HEAD_DIM)
    value_grid = value_blocks.reshape(count_q, slot_count * BLOCK, heads_here, HEAD_DIM)
    scores = jnp.einsum(
        "bqhd,bshd->bhqs", query_grid, key_grid, preferred_element_type=jnp.float32
    ) * (1.0 / math.sqrt(HEAD_DIM))
    present = jnp.repeat(jnp.transpose(valid_slots, (0, 2, 1)), BLOCK, axis=2)[:, :, None, :]
    scores = jnp.where(present, scores, masked_score)
    peak = jnp.max(scores, axis=3, keepdims=True)
    expo = jnp.exp(scores - peak)
    total = jnp.sum(expo, axis=3)
    weights = expo.astype(jnp.bfloat16)
    mixture = jnp.einsum("bhqs,bshd->bqhd", weights, value_grid, preferred_element_type=jnp.float32)
    mixture = mixture / jnp.transpose(total, (0, 2, 1))[..., None]
    return mixture.reshape(count_q, BLOCK, heads_here * HEAD_DIM).astype(jnp.bfloat16)


def xor_perm(count, bit):
    return [(i, i ^ bit) for i in range(count)]


def tree_reduce(parts, merge, axis):
    count = lax.axis_size(axis)
    place = lax.axis_index(axis)
    bits = []
    bit = 1
    while bit < count:
        bits.append(bit)
        bit *= 2
    for bit in bits:
        upper = (place // bit) % 2
        halves = jax.tree.map(lambda x: x.reshape((2, x.shape[0] // 2) + x.shape[1:]), parts)
        keep = jax.tree.map(lambda h: lax.dynamic_index_in_dim(h, upper, 0, keepdims=False), halves)
        send = jax.tree.map(lambda h: lax.dynamic_index_in_dim(h, 1 - upper, 0, keepdims=False), halves)
        got = lax.ppermute(send, axis, xor_perm(count, bit))
        parts = merge(keep, got)
    for bit in reversed(bits):
        upper = (place // bit) % 2
        got = lax.ppermute(parts, axis, xor_perm(count, bit))

        def join(mine, theirs):
            pair = jnp.stack([mine, theirs])
            first = lax.dynamic_index_in_dim(pair, upper, 0, keepdims=False)
            second = lax.dynamic_index_in_dim(pair, 1 - upper, 0, keepdims=False)
            return jnp.concatenate([first, second], axis=0)

        parts = jax.tree.map(join, parts, got)
    return parts


def add_merge(a, b):
    return jax.tree.map(jnp.add, a, b)


def softmax_merge(a, b):
    width = a.shape[1] - 128
    heads = width // HEAD_DIM
    peak_a = a[:, width + heads : width + 2 * heads]
    peak_b = b[:, width + heads : width + 2 * heads]
    peak = jnp.maximum(peak_a, peak_b)
    scale_a = jnp.exp(peak_a - peak)
    scale_b = jnp.exp(peak_b - peak)
    rows = a.shape[0]
    mix = (
        a[:, :width].reshape(rows, heads, HEAD_DIM) * scale_a[..., None]
        + b[:, :width].reshape(rows, heads, HEAD_DIM) * scale_b[..., None]
    ).reshape(rows, width)
    total = a[:, width : width + heads] * scale_a + b[:, width : width + heads] * scale_b
    pad = jnp.zeros((rows, 128 - 2 * heads), a.dtype)
    return jnp.concatenate([mix, total, peak, pad], axis=1)


def head_partials(rows, out_weight):
    head_count = lax.axis_size("head")
    partial = lax.dot_general(
        out_weight, rows, (((0,), (1,)), ((), ())), preferred_element_type=jnp.float32
    ).astype(jnp.bfloat16)
    return partial.reshape(head_count, out_weight.shape[1] // head_count, rows.shape[0])


def sum_over_head(partial):
    gathered = lax.all_to_all(partial, "head", 0, 0, tiled=True)
    return jnp.sum(gathered.astype(jnp.float32), axis=0).T


def partial_attend(query_blocks, key_blocks, value_blocks, valid_slots):
    count_q, slot_count = (key_blocks.shape[0], key_blocks.shape[1])
    heads_here = query_blocks.shape[-1] // HEAD_DIM
    query_grid = query_blocks.reshape(count_q, BLOCK, heads_here, HEAD_DIM)
    key_grid = key_blocks.reshape(count_q, slot_count * BLOCK, heads_here, HEAD_DIM)
    value_grid = value_blocks.reshape(count_q, slot_count * BLOCK, heads_here, HEAD_DIM)
    scores = jnp.einsum(
        "bqhd,bshd->bhqs", query_grid, key_grid, preferred_element_type=jnp.float32
    ) * (1.0 / math.sqrt(HEAD_DIM))
    present = jnp.repeat(jnp.transpose(valid_slots, (0, 2, 1)), BLOCK, axis=2)[:, :, None, :]
    scores = jnp.where(present, scores, masked_score)
    peak = jnp.max(scores, axis=3)
    expo = jnp.exp(scores - peak[..., None])
    total = jnp.sum(expo, axis=3)
    mixture = jnp.einsum(
        "bhqs,bshd->bqhd", expo.astype(jnp.bfloat16), value_grid, preferred_element_type=jnp.float32
    )
    return mixture, total, peak


def merge_attend(first, second):
    mix_a, total_a, peak_a = first
    mix_b, total_b, peak_b = second
    peak = jnp.maximum(peak_a, peak_b)
    scale_a = jnp.exp(peak_a - peak)
    scale_b = jnp.exp(peak_b - peak)
    total = total_a * scale_a + total_b * scale_b
    mix = mix_a * jnp.transpose(scale_a, (0, 2, 1))[..., None] + mix_b * jnp.transpose(scale_b, (0, 2, 1))[..., None]
    mix = mix / jnp.transpose(total, (0, 2, 1))[..., None]
    count_q = mix.shape[0]
    return mix.reshape(count_q, BLOCK, -1).astype(jnp.bfloat16)


def on_device(
    queries,
    keys,
    values,
    out_weight,
    global_blocks,
    random_blocks,
    window_blocks,
    yarn_scale,
    yarn_context,
):
    tok_here, width_here = queries.shape
    heads_here = width_here // HEAD_DIM
    blocks_here = tok_here // BLOCK
    seq_count = lax.axis_size("seq")
    seq_place = lax.axis_index("seq")
    block_total = seq_count * blocks_here
    frequency, mscale = yarn_tables(yarn_scale, yarn_context)
    first_row = seq_place * tok_here
    query_rot = rotate(queries, first_row, frequency, mscale)
    key_rot = rotate(keys, first_row, frequency, mscale)
    pair_kv = jnp.stack([key_rot, values])
    local_blocks = pair_kv.reshape(2, blocks_here, BLOCK, width_here)

    def padded_block(index):
        if index < WMAX:
            return from_left[:, index]
        if index < WMAX + blocks_here:
            return local_blocks[:, index - WMAX]
        return from_right[:, index - WMAX - blocks_here]

    offsets = jnp.arange(-WMAX, WMAX + 1)
    window_ids = seq_place * blocks_here + jnp.arange(blocks_here)[:, None] + offsets[None, :]
    inside = (window_ids >= 0) & (window_ids < block_total)
    reach = jnp.abs(offsets)[None, :, None] <= window_blocks[None, None, :]
    window_valid = inside[:, :, None] & reach
    owner_global = global_blocks // blocks_here
    local_global = jnp.clip(global_blocks - seq_place * blocks_here, 0, blocks_here - 1)
    mine_global = owner_global == seq_place
    query_view = query_rot.reshape(blocks_here, BLOCK, width_here)
    key_view = key_rot.reshape(blocks_here, BLOCK, width_here)
    value_view = values.reshape(blocks_here, BLOCK, width_here)
    picked = jnp.stack([query_view[local_global], key_view[local_global], value_view[local_global]])
    masked = jnp.where(mine_global[None, :, None, None], picked, jnp.zeros_like(picked))
    shared = tree_reduce(masked.reshape(3 * GLOB * BLOCK, width_here), add_merge, "seq")
    shared = shared.reshape(3, GLOB, BLOCK, width_here)
    halo = WMAX * BLOCK
    seq_ends = seq_count - 1
    halo_kv, shared = lax.optimization_barrier((pair_kv, shared))
    from_left = lax.ppermute(
        halo_kv[:, tok_here - halo :], "seq", [(i, (i + 1) % seq_count) for i in range(seq_ends)]
    ).reshape(2, WMAX, BLOCK, width_here)
    from_right = lax.ppermute(
        halo_kv[:, :halo], "seq", [((i + 1) % seq_count, i) for i in range(seq_ends)]
    ).reshape(2, WMAX, BLOCK, width_here)
    slot_parts = [
        jnp.stack(
            [padded_block(block + offset_slot) for offset_slot in range(2 * WMAX + 1)], axis=1
        )
        for block in range(blocks_here)
    ]
    global_kv = jnp.broadcast_to(shared[1:3][:, None], (2, blocks_here, GLOB, BLOCK, width_here))
    near_kv = jnp.concatenate([jnp.stack(slot_parts, axis=1), global_kv], axis=2)
    near_valid = jnp.concatenate(
        [window_valid, jnp.ones((blocks_here, GLOB, heads_here), dtype=bool)], axis=1
    )
    global_query = shared[0]
    key_later = key_rot
    value_later = values
    global_query = global_query.reshape(GLOB, BLOCK, heads_here, HEAD_DIM)
    key_grid = key_later.reshape(tok_here, heads_here, HEAD_DIM)
    value_grid = value_later.reshape(tok_here, heads_here, HEAD_DIM)
    global_scores = jnp.einsum(
        "gqhd,khd->gqhk", global_query, key_grid, preferred_element_type=jnp.float32
    ) * (1.0 / math.sqrt(HEAD_DIM))
    local_peak = jnp.max(global_scores, axis=3)
    expo = jnp.exp(global_scores - local_peak[..., None])
    partial_total = jnp.sum(expo, axis=3)
    partial_mix = jnp.einsum(
        "gqhk,khd->gqhd", expo.astype(jnp.bfloat16), value_grid, preferred_element_type=jnp.float32
    )
    row_total = GLOB * BLOCK
    packed = jnp.concatenate(
        [
            partial_mix.reshape(row_total, width_here),
            partial_total.reshape(row_total, heads_here),
            local_peak.reshape(row_total, heads_here),
            jnp.zeros((row_total, 128 - 2 * heads_here), jnp.float32),
        ],
        axis=1,
    )
    packed, from_left, from_right = lax.optimization_barrier((packed, from_left, from_right))
    reduced = tree_reduce(packed, softmax_merge, "seq")
    slot_total = blocks_here * RAND
    capacity = (slot_total + seq_count - 1) // seq_count
    flat_ids = random_blocks.reshape(seq_count, slot_total)
    owners = flat_ids // blocks_here
    slot_order = jnp.arange(slot_total)
    same_owner = (owners[:, :, None] == owners[:, None, :]) & (
        slot_order[None, None, :] < slot_order[None, :, None]
    )
    ranks = jnp.sum(same_owner.astype(jnp.int32), axis=2)
    local_ids = flat_ids - owners * blocks_here
    wanted = (owners[:, None, :] == seq_place) & (
        ranks[:, None, :] == jnp.arange(capacity)[None, :, None]
    )
    send_local = jnp.sum(jnp.where(wanted, local_ids[:, None, :], 0), axis=2)
    kv_blocks = jnp.stack([key_rot.reshape(blocks_here, BLOCK, width_here), value_view], axis=1)
    outgoing = kv_blocks[send_local]
    outgoing, reduced = lax.optimization_barrier((outgoing, reduced))
    incoming = lax.all_to_all(outgoing, "seq", split_axis=0, concat_axis=0, tiled=True)
    my_owners = owners[seq_place]
    my_ranks = ranks[seq_place]
    chunk_count = seq_count * capacity
    slot_chunk = my_owners * capacity + my_ranks
    pick = (slot_chunk[:, None] == jnp.arange(chunk_count)[None, :]).astype(jnp.bfloat16)
    chunks = incoming.reshape(chunk_count, 2 * BLOCK * width_here)
    selected = jnp.dot(pick, chunks, preferred_element_type=jnp.float32).astype(jnp.bfloat16)
    selected = selected.reshape(blocks_here, RAND, 2, BLOCK, width_here)
    random_k = selected[:, :, 0]
    random_v = selected[:, :, 1]
    random_kv = (random_k, random_v)
    near_part = partial_attend(query_view, near_kv[0], near_kv[1], near_valid)
    far_part = partial_attend(
        query_view, random_kv[0], random_kv[1], jnp.ones((blocks_here, RAND, heads_here), dtype=bool)
    )
    attended = merge_attend(near_part, far_part)
    mix_sum = reduced[:, :width_here].reshape(row_total, heads_here, HEAD_DIM)
    total_sum = reduced[:, width_here : width_here + heads_here]
    global_out = (mix_sum / total_sum[..., None]).reshape(row_total, width_here).astype(jnp.bfloat16)
    global_out = global_out.reshape(GLOB, BLOCK, width_here)
    block_index = jnp.arange(blocks_here)
    for global_slot in range(GLOB):
        hit = mine_global[global_slot] & (block_index == local_global[global_slot])
        attended = jnp.where(hit[:, None, None], global_out[global_slot][None], attended)
    mixed = sum_over_head(head_partials(attended.reshape(tok_here, width_here), out_weight))
    return mixed.astype(jnp.bfloat16)


def solution(mesh):
    in_specs = (
        P("seq", "head"),
        P("seq", "head"),
        P("seq", "head"),
        P("head", None),
        P(),
        P(),
        P("head"),
        P(),
        P(),
    )
    out_specs = P("seq", "head")
    return jax.shard_map(
        on_device, mesh=mesh, in_specs=in_specs, out_specs=out_specs, check_vma=False
    )
```

```python
import math

import jax
import jax.numpy as jnp
from jax import lax
from jax.sharding import PartitionSpec as P

HEAD_DIM = 128
BLOCK = 64
GLOB = 2
RAND = 3
WMAX = 2


masked_score = -1e30


def padded_2(cells, sides, width):
    for axis, dim in sides:
        count = lax.axis_size(axis)
        ends = count - 1
        head = lax.slice_in_dim(cells, 0, width, axis=dim)
        tail = lax.slice_in_dim(cells, cells.shape[dim] - width, cells.shape[dim], axis=dim)
        cells = jnp.concatenate(
            [
                lax.ppermute(tail, axis, [(i, (i + 1) % count) for i in range(ends)]),
                cells,
                lax.ppermute(head, axis, [((i + 1) % count, i) for i in range(ends)]),
            ],
            axis=dim,
        )
    return cells


def yarn_tables(yarn_scale, yarn_context):
    half_dim = HEAD_DIM // 2
    pair_index = jnp.arange(half_dim).astype(jnp.float32)
    base_rate = 10000.0 ** (-2.0 * pair_index / HEAD_DIM)
    factor = yarn_scale[0].astype(jnp.float32)
    context = yarn_context[0].astype(jnp.float32)
    turn_ratio = context * base_rate / (2.0 * math.pi)
    ramp_weight = jnp.clip((turn_ratio - 1.0) / 31.0, 0.0, 1.0)
    frequency = base_rate * ((1.0 - ramp_weight) / factor + ramp_weight)
    mscale = 0.1 * jnp.log(factor) + 1.0
    return (frequency, mscale)


def rotate(source, first_row, frequency, mscale):
    row_count, row_width = source.shape
    half_dim = HEAD_DIM // 2
    position = (first_row + jnp.arange(row_count)).astype(jnp.float32)
    angle_table = position[:, None] * frequency[None, :]
    cosine = jnp.cos(angle_table) * mscale
    sine_part = jnp.sin(angle_table) * mscale
    cosine = jnp.concatenate([cosine, cosine], axis=1)[:, None, :]
    sine_part = jnp.concatenate([sine_part, sine_part], axis=1)[:, None, :]
    grid = source.astype(jnp.float32).reshape(row_count, row_width // HEAD_DIM, HEAD_DIM)
    turned_half = jnp.concatenate([-grid[..., half_dim:], grid[..., :half_dim]], axis=2)
    turned = grid * cosine + turned_half * sine_part
    return turned.reshape(row_count, row_width).astype(jnp.bfloat16)


def block_attend(query_blocks, key_blocks, value_blocks, valid_slots):
    count_q, slot_count = (key_blocks.shape[0], key_blocks.shape[1])
    heads_here = query_blocks.shape[-1] // HEAD_DIM
    query_grid = query_blocks.reshape(count_q, BLOCK, heads_here, HEAD_DIM)
    key_grid = key_blocks.reshape(count_q, slot_count * BLOCK, heads_here, HEAD_DIM)
    value_grid = value_blocks.reshape(count_q, slot_count * BLOCK, heads_here, HEAD_DIM)
    scores = jnp.einsum(
        "bqhd,bshd->bhqs", query_grid, key_grid, preferred_element_type=jnp.float32
    ) * (1.0 / math.sqrt(HEAD_DIM))
    present = jnp.repeat(jnp.transpose(valid_slots, (0, 2, 1)), BLOCK, axis=2)[:, :, None, :]
    scores = jnp.where(present, scores, masked_score)
    peak = jnp.max(scores, axis=3, keepdims=True)
    expo = jnp.exp(scores - peak)
    total = jnp.sum(expo, axis=3)
    weights = expo.astype(jnp.bfloat16)
    mixture = jnp.einsum("bhqs,bshd->bqhd", weights, value_grid, preferred_element_type=jnp.float32)
    mixture = mixture / jnp.transpose(total, (0, 2, 1))[..., None]
    return mixture.reshape(count_q, BLOCK, heads_here * HEAD_DIM).astype(jnp.bfloat16)


def xor_perm(count, bit):
    return [(i, i ^ bit) for i in range(count)]


def tree_reduce(parts, merge, axis):
    count = lax.axis_size(axis)
    place = lax.axis_index(axis)
    bits = []
    bit = 1
    while bit < count:
        bits.append(bit)
        bit *= 2
    for bit in bits:
        upper = (place // bit) % 2
        halves = jax.tree.map(lambda x: x.reshape((2, x.shape[0] // 2) + x.shape[1:]), parts)
        keep = jax.tree.map(lambda h: lax.dynamic_index_in_dim(h, upper, 0, keepdims=False), halves)
        send = jax.tree.map(lambda h: lax.dynamic_index_in_dim(h, 1 - upper, 0, keepdims=False), halves)
        got = lax.ppermute(send, axis, xor_perm(count, bit))
        parts = merge(keep, got)
    for bit in reversed(bits):
        upper = (place // bit) % 2
        got = lax.ppermute(parts, axis, xor_perm(count, bit))

        def join(mine, theirs):
            pair = jnp.stack([mine, theirs])
            first = lax.dynamic_index_in_dim(pair, upper, 0, keepdims=False)
            second = lax.dynamic_index_in_dim(pair, 1 - upper, 0, keepdims=False)
            return jnp.concatenate([first, second], axis=0)

        parts = jax.tree.map(join, parts, got)
    return parts


def add_merge(a, b):
    return jax.tree.map(jnp.add, a, b)


def softmax_merge(a, b):
    width = a.shape[1] - 128
    heads = width // HEAD_DIM
    peak_a = a[:, width + heads : width + 2 * heads]
    peak_b = b[:, width + heads : width + 2 * heads]
    peak = jnp.maximum(peak_a, peak_b)
    scale_a = jnp.exp(peak_a - peak)
    scale_b = jnp.exp(peak_b - peak)
    rows = a.shape[0]
    mix = (
        a[:, :width].reshape(rows, heads, HEAD_DIM) * scale_a[..., None]
        + b[:, :width].reshape(rows, heads, HEAD_DIM) * scale_b[..., None]
    ).reshape(rows, width)
    total = a[:, width : width + heads] * scale_a + b[:, width : width + heads] * scale_b
    pad = jnp.zeros((rows, 128 - 2 * heads), a.dtype)
    return jnp.concatenate([mix, total, peak, pad], axis=1)


def head_partials(rows, out_weight):
    head_count = lax.axis_size("head")
    partial = lax.dot_general(
        out_weight, rows, (((0,), (1,)), ((), ())), preferred_element_type=jnp.float32
    ).astype(jnp.bfloat16)
    return partial.reshape(head_count, out_weight.shape[1] // head_count, rows.shape[0])


def sum_over_head(partial):
    gathered = lax.all_to_all(partial, "head", 0, 0, tiled=True)
    return jnp.sum(gathered.astype(jnp.float32), axis=0).T


def partial_attend(query_blocks, key_blocks, value_blocks, valid_slots):
    count_q, slot_count = (key_blocks.shape[0], key_blocks.shape[1])
    heads_here = query_blocks.shape[-1] // HEAD_DIM
    query_grid = query_blocks.reshape(count_q, BLOCK, heads_here, HEAD_DIM)
    key_grid = key_blocks.reshape(count_q, slot_count * BLOCK, heads_here, HEAD_DIM)
    value_grid = value_blocks.reshape(count_q, slot_count * BLOCK, heads_here, HEAD_DIM)
    scores = jnp.einsum(
        "bqhd,bshd->bhqs", query_grid, key_grid, preferred_element_type=jnp.float32
    ) * (1.0 / math.sqrt(HEAD_DIM))
    present = jnp.repeat(jnp.transpose(valid_slots, (0, 2, 1)), BLOCK, axis=2)[:, :, None, :]
    scores = jnp.where(present, scores, masked_score)
    peak = jnp.max(scores, axis=3)
    expo = jnp.exp(scores - peak[..., None])
    total = jnp.sum(expo, axis=3)
    mixture = jnp.einsum(
        "bhqs,bshd->bqhd", expo.astype(jnp.bfloat16), value_grid, preferred_element_type=jnp.float32
    )
    return mixture, total, peak


def merge_attend(first, second):
    mix_a, total_a, peak_a = first
    mix_b, total_b, peak_b = second
    peak = jnp.maximum(peak_a, peak_b)
    scale_a = jnp.exp(peak_a - peak)
    scale_b = jnp.exp(peak_b - peak)
    total = total_a * scale_a + total_b * scale_b
    mix = mix_a * jnp.transpose(scale_a, (0, 2, 1))[..., None] + mix_b * jnp.transpose(scale_b, (0, 2, 1))[..., None]
    mix = mix / jnp.transpose(total, (0, 2, 1))[..., None]
    count_q = mix.shape[0]
    return mix.reshape(count_q, BLOCK, -1).astype(jnp.bfloat16)


def on_device(
    queries,
    keys,
    values,
    out_weight,
    global_blocks,
    random_blocks,
    window_blocks,
    yarn_scale,
    yarn_context,
):
    tok_here, width_here = queries.shape
    heads_here = width_here // HEAD_DIM
    blocks_here = tok_here // BLOCK
    seq_count = lax.axis_size("seq")
    seq_place = lax.axis_index("seq")
    block_total = seq_count * blocks_here
    frequency, mscale = yarn_tables(yarn_scale, yarn_context)
    first_row = seq_place * tok_here
    query_rot = rotate(queries, first_row, frequency, mscale)
    key_rot = rotate(keys, first_row, frequency, mscale)
    pair_kv = jnp.stack([key_rot, values])
    local_blocks = pair_kv.reshape(2, blocks_here, BLOCK, width_here)

    def padded_block(index):
        if index < WMAX:
            return from_left[:, index]
        if index < WMAX + blocks_here:
            return local_blocks[:, index - WMAX]
        return from_right[:, index - WMAX - blocks_here]

    offsets = jnp.arange(-WMAX, WMAX + 1)
    window_ids = seq_place * blocks_here + jnp.arange(blocks_here)[:, None] + offsets[None, :]
    inside = (window_ids >= 0) & (window_ids < block_total)
    reach = jnp.abs(offsets)[None, :, None] <= window_blocks[None, None, :]
    window_valid = inside[:, :, None] & reach
    owner_global = global_blocks // blocks_here
    local_global = jnp.clip(global_blocks - seq_place * blocks_here, 0, blocks_here - 1)
    mine_global = owner_global == seq_place
    query_view = query_rot.reshape(blocks_here, BLOCK, width_here)
    key_view = key_rot.reshape(blocks_here, BLOCK, width_here)
    value_view = values.reshape(blocks_here, BLOCK, width_here)
    picked = jnp.stack([query_view[local_global], key_view[local_global], value_view[local_global]])
    masked = jnp.where(mine_global[None, :, None, None], picked, jnp.zeros_like(picked))
    shared = tree_reduce(masked.reshape(3 * GLOB * BLOCK, width_here), add_merge, "seq")
    shared = shared.reshape(3, GLOB, BLOCK, width_here)
    halo = WMAX * BLOCK
    seq_ends = seq_count - 1
    halo_kv, shared = lax.optimization_barrier((pair_kv, shared))
    from_left = lax.ppermute(
        halo_kv[:, tok_here - halo :], "seq", [(i, (i + 1) % seq_count) for i in range(seq_ends)]
    ).reshape(2, WMAX, BLOCK, width_here)
    from_right = lax.ppermute(
        halo_kv[:, :halo], "seq", [((i + 1) % seq_count, i) for i in range(seq_ends)]
    ).reshape(2, WMAX, BLOCK, width_here)
    slot_parts = [
        jnp.stack(
            [padded_block(block + offset_slot) for offset_slot in range(2 * WMAX + 1)], axis=1
        )
        for block in range(blocks_here)
    ]
    global_kv = jnp.broadcast_to(shared[1:3][:, None], (2, blocks_here, GLOB, BLOCK, width_here))
    near_kv = jnp.concatenate([jnp.stack(slot_parts, axis=1), global_kv], axis=2)
    near_valid = jnp.concatenate(
        [window_valid, jnp.ones((blocks_here, GLOB, heads_here), dtype=bool)], axis=1
    )
    global_query = shared[0]
    key_later = key_rot
    value_later = values
    global_query = global_query.reshape(GLOB, BLOCK, heads_here, HEAD_DIM)
    key_grid = key_later.reshape(tok_here, heads_here, HEAD_DIM)
    value_grid = value_later.reshape(tok_here, heads_here, HEAD_DIM)
    global_scores = jnp.einsum(
        "gqhd,khd->gqhk", global_query, key_grid, preferred_element_type=jnp.float32
    ) * (1.0 / math.sqrt(HEAD_DIM))
    local_peak = jnp.max(global_scores, axis=3)
    expo = jnp.exp(global_scores - local_peak[..., None])
    partial_total = jnp.sum(expo, axis=3)
    partial_mix = jnp.einsum(
        "gqhk,khd->gqhd", expo.astype(jnp.bfloat16), value_grid, preferred_element_type=jnp.float32
    )
    row_total = GLOB * BLOCK
    packed = jnp.concatenate(
        [
            partial_mix.reshape(row_total, width_here),
            partial_total.reshape(row_total, heads_here),
            local_peak.reshape(row_total, heads_here),
            jnp.zeros((row_total, 128 - 2 * heads_here), jnp.float32),
        ],
        axis=1,
    )
    slot_total = blocks_here * RAND
    capacity = (slot_total + seq_count - 1) // seq_count
    flat_ids = random_blocks.reshape(seq_count, slot_total)
    owners = flat_ids // blocks_here
    slot_order = jnp.arange(slot_total)
    same_owner = (owners[:, :, None] == owners[:, None, :]) & (
        slot_order[None, None, :] < slot_order[None, :, None]
    )
    ranks = jnp.sum(same_owner.astype(jnp.int32), axis=2)
    local_ids = flat_ids - owners * blocks_here
    wanted = (owners[:, None, :] == seq_place) & (
        ranks[:, None, :] == jnp.arange(capacity)[None, :, None]
    )
    send_local = jnp.sum(jnp.where(wanted, local_ids[:, None, :], 0), axis=2)
    kv_blocks = jnp.transpose(halo_kv.reshape(2, blocks_here, BLOCK, width_here), (1, 0, 2, 3))
    outgoing = kv_blocks[send_local]
    packed, from_left, from_right, outgoing = lax.optimization_barrier(
        (packed, from_left, from_right, outgoing)
    )
    reduced = tree_reduce(packed, softmax_merge, "seq")
    outgoing, reduced = lax.optimization_barrier((outgoing, reduced))
    incoming = lax.all_to_all(outgoing, "seq", split_axis=0, concat_axis=0, tiled=True)
    my_owners = owners[seq_place]
    my_ranks = ranks[seq_place]
    random_k = incoming[my_owners, my_ranks, 0].reshape(blocks_here, RAND, BLOCK, width_here)
    random_v = incoming[my_owners, my_ranks, 1].reshape(blocks_here, RAND, BLOCK, width_here)
    random_kv = (random_k, random_v)
    near_part = partial_attend(query_view, near_kv[0], near_kv[1], near_valid)
    far_part = partial_attend(
        query_view, random_kv[0], random_kv[1], jnp.ones((blocks_here, RAND, heads_here), dtype=bool)
    )
    attended = merge_attend(near_part, far_part)
    mix_sum = reduced[:, :width_here].reshape(row_total, heads_here, HEAD_DIM)
    total_sum = reduced[:, width_here : width_here + heads_here]
    global_out = (mix_sum / total_sum[..., None]).reshape(row_total, width_here).astype(jnp.bfloat16)
    global_out = global_out.reshape(GLOB, BLOCK, width_here)
    block_index = jnp.arange(blocks_here)
    for global_slot in range(GLOB):
        hit = mine_global[global_slot] & (block_index == local_global[global_slot])
        attended = jnp.where(hit[:, None, None], global_out[global_slot][None], attended)
    mixed = sum_over_head(head_partials(attended.reshape(tok_here, width_here), out_weight))
    return mixed.astype(jnp.bfloat16)


def solution(mesh):
    in_specs = (
        P("seq", "head"),
        P("seq", "head"),
        P("seq", "head"),
        P("head", None),
        P(),
        P(),
        P("head"),
        P(),
        P(),
    )
    out_specs = P("seq", "head")
    return jax.shard_map(
        on_device, mesh=mesh, in_specs=in_specs, out_specs=out_specs, check_vma=False
    )
```

```python
import math

import jax
import jax.numpy as jnp
from jax import lax
from jax.sharding import PartitionSpec as P

HEAD_DIM = 128
BLOCK = 64
GLOB = 2
RAND = 3
WMAX = 2


masked_score = -1e30


def padded_2(cells, sides, width):
    for axis, dim in sides:
        count = lax.axis_size(axis)
        ends = count - 1
        head = lax.slice_in_dim(cells, 0, width, axis=dim)
        tail = lax.slice_in_dim(cells, cells.shape[dim] - width, cells.shape[dim], axis=dim)
        cells = jnp.concatenate(
            [
                lax.ppermute(tail, axis, [(i, (i + 1) % count) for i in range(ends)]),
                cells,
                lax.ppermute(head, axis, [((i + 1) % count, i) for i in range(ends)]),
            ],
            axis=dim,
        )
    return cells


def yarn_tables(yarn_scale, yarn_context):
    half_dim = HEAD_DIM // 2
    pair_index = jnp.arange(half_dim).astype(jnp.float32)
    base_rate = 10000.0 ** (-2.0 * pair_index / HEAD_DIM)
    factor = yarn_scale[0].astype(jnp.float32)
    context = yarn_context[0].astype(jnp.float32)
    turn_ratio = context * base_rate / (2.0 * math.pi)
    ramp_weight = jnp.clip((turn_ratio - 1.0) / 31.0, 0.0, 1.0)
    frequency = base_rate * ((1.0 - ramp_weight) / factor + ramp_weight)
    mscale = 0.1 * jnp.log(factor) + 1.0
    return (frequency, mscale)


def rotate(source, first_row, frequency, mscale):
    row_count, row_width = source.shape
    half_dim = HEAD_DIM // 2
    position = (first_row + jnp.arange(row_count)).astype(jnp.float32)
    angle_table = position[:, None] * frequency[None, :]
    cosine = jnp.cos(angle_table) * mscale
    sine_part = jnp.sin(angle_table) * mscale
    cosine = jnp.concatenate([cosine, cosine], axis=1)[:, None, :]
    sine_part = jnp.concatenate([sine_part, sine_part], axis=1)[:, None, :]
    grid = source.astype(jnp.float32).reshape(row_count, row_width // HEAD_DIM, HEAD_DIM)
    turned_half = jnp.concatenate([-grid[..., half_dim:], grid[..., :half_dim]], axis=2)
    turned = grid * cosine + turned_half * sine_part
    return turned.reshape(row_count, row_width).astype(jnp.bfloat16)


def block_attend(query_blocks, key_blocks, value_blocks, valid_slots):
    count_q, slot_count = (key_blocks.shape[0], key_blocks.shape[1])
    heads_here = query_blocks.shape[-1] // HEAD_DIM
    query_grid = query_blocks.reshape(count_q, BLOCK, heads_here, HEAD_DIM)
    key_grid = key_blocks.reshape(count_q, slot_count * BLOCK, heads_here, HEAD_DIM)
    value_grid = value_blocks.reshape(count_q, slot_count * BLOCK, heads_here, HEAD_DIM)
    scores = jnp.einsum(
        "bqhd,bshd->bhqs", query_grid, key_grid, preferred_element_type=jnp.float32
    ) * (1.0 / math.sqrt(HEAD_DIM))
    present = jnp.repeat(jnp.transpose(valid_slots, (0, 2, 1)), BLOCK, axis=2)[:, :, None, :]
    scores = jnp.where(present, scores, masked_score)
    peak = jnp.max(scores, axis=3, keepdims=True)
    expo = jnp.exp(scores - peak)
    total = jnp.sum(expo, axis=3)
    weights = expo.astype(jnp.bfloat16)
    mixture = jnp.einsum("bhqs,bshd->bqhd", weights, value_grid, preferred_element_type=jnp.float32)
    mixture = mixture / jnp.transpose(total, (0, 2, 1))[..., None]
    return mixture.reshape(count_q, BLOCK, heads_here * HEAD_DIM).astype(jnp.bfloat16)


def xor_perm(count, bit):
    return [(i, i ^ bit) for i in range(count)]


def tree_reduce(parts, merge, axis):
    count = lax.axis_size(axis)
    place = lax.axis_index(axis)
    bits = []
    bit = 1
    while bit < count:
        bits.append(bit)
        bit *= 2
    for bit in bits:
        upper = (place // bit) % 2
        halves = jax.tree.map(lambda x: x.reshape((2, x.shape[0] // 2) + x.shape[1:]), parts)
        keep = jax.tree.map(lambda h: lax.dynamic_index_in_dim(h, upper, 0, keepdims=False), halves)
        send = jax.tree.map(lambda h: lax.dynamic_index_in_dim(h, 1 - upper, 0, keepdims=False), halves)
        got = lax.ppermute(send, axis, xor_perm(count, bit))
        parts = merge(keep, got)
    for bit in reversed(bits):
        upper = (place // bit) % 2
        got = lax.ppermute(parts, axis, xor_perm(count, bit))

        def join(mine, theirs):
            pair = jnp.stack([mine, theirs])
            first = lax.dynamic_index_in_dim(pair, upper, 0, keepdims=False)
            second = lax.dynamic_index_in_dim(pair, 1 - upper, 0, keepdims=False)
            return jnp.concatenate([first, second], axis=0)

        parts = jax.tree.map(join, parts, got)
    return parts


def add_merge(a, b):
    return jax.tree.map(jnp.add, a, b)


def softmax_merge(a, b):
    width = a.shape[1] - 128
    heads = width // HEAD_DIM
    peak_a = a[:, width + heads : width + 2 * heads]
    peak_b = b[:, width + heads : width + 2 * heads]
    peak = jnp.maximum(peak_a, peak_b)
    scale_a = jnp.exp(peak_a - peak)
    scale_b = jnp.exp(peak_b - peak)
    rows = a.shape[0]
    mix = (
        a[:, :width].reshape(rows, heads, HEAD_DIM) * scale_a[..., None]
        + b[:, :width].reshape(rows, heads, HEAD_DIM) * scale_b[..., None]
    ).reshape(rows, width)
    total = a[:, width : width + heads] * scale_a + b[:, width : width + heads] * scale_b
    pad = jnp.zeros((rows, 128 - 2 * heads), a.dtype)
    return jnp.concatenate([mix, total, peak, pad], axis=1)


def head_partials(rows, out_weight):
    head_count = lax.axis_size("head")
    partial = lax.dot_general(
        out_weight, rows, (((0,), (1,)), ((), ())), preferred_element_type=jnp.float32
    ).astype(jnp.bfloat16)
    return partial.reshape(head_count, out_weight.shape[1] // head_count, rows.shape[0])


def sum_over_head(partial):
    gathered = lax.all_to_all(partial, "head", 0, 0, tiled=True)
    return jnp.sum(gathered.astype(jnp.float32), axis=0).T


def partial_attend(query_blocks, key_blocks, value_blocks, valid_slots):
    count_q, slot_count = (key_blocks.shape[0], key_blocks.shape[1])
    heads_here = query_blocks.shape[-1] // HEAD_DIM
    query_grid = query_blocks.reshape(count_q, BLOCK, heads_here, HEAD_DIM)
    key_grid = key_blocks.reshape(count_q, slot_count * BLOCK, heads_here, HEAD_DIM)
    value_grid = value_blocks.reshape(count_q, slot_count * BLOCK, heads_here, HEAD_DIM)
    scores = jnp.einsum(
        "bqhd,bshd->bhqs", query_grid, key_grid, preferred_element_type=jnp.float32
    ) * (1.0 / math.sqrt(HEAD_DIM))
    present = jnp.repeat(jnp.transpose(valid_slots, (0, 2, 1)), BLOCK, axis=2)[:, :, None, :]
    scores = jnp.where(present, scores, masked_score)
    peak = jnp.max(scores, axis=3)
    expo = jnp.exp(scores - peak[..., None])
    total = jnp.sum(expo, axis=3)
    mixture = jnp.einsum(
        "bhqs,bshd->bqhd", expo.astype(jnp.bfloat16), value_grid, preferred_element_type=jnp.float32
    )
    return mixture, total, peak


def merge_attend(first, second):
    mix_a, total_a, peak_a = first
    mix_b, total_b, peak_b = second
    peak = jnp.maximum(peak_a, peak_b)
    scale_a = jnp.exp(peak_a - peak)
    scale_b = jnp.exp(peak_b - peak)
    total = total_a * scale_a + total_b * scale_b
    mix = mix_a * jnp.transpose(scale_a, (0, 2, 1))[..., None] + mix_b * jnp.transpose(scale_b, (0, 2, 1))[..., None]
    mix = mix / jnp.transpose(total, (0, 2, 1))[..., None]
    count_q = mix.shape[0]
    return mix.reshape(count_q, BLOCK, -1).astype(jnp.bfloat16)


def on_device(
    queries,
    keys,
    values,
    out_weight,
    global_blocks,
    random_blocks,
    window_blocks,
    yarn_scale,
    yarn_context,
):
    tok_here, width_here = queries.shape
    heads_here = width_here // HEAD_DIM
    blocks_here = tok_here // BLOCK
    seq_count = lax.axis_size("seq")
    seq_place = lax.axis_index("seq")
    block_total = seq_count * blocks_here
    frequency, mscale = yarn_tables(yarn_scale, yarn_context)
    first_row = seq_place * tok_here
    query_rot = rotate(queries, first_row, frequency, mscale)
    key_rot = rotate(keys, first_row, frequency, mscale)
    pair_kv = jnp.stack([key_rot, values])
    local_blocks = pair_kv.reshape(2, blocks_here, BLOCK, width_here)

    def padded_block(index):
        if index < WMAX:
            return from_left[:, index]
        if index < WMAX + blocks_here:
            return local_blocks[:, index - WMAX]
        return from_right[:, index - WMAX - blocks_here]

    offsets = jnp.arange(-WMAX, WMAX + 1)
    window_ids = seq_place * blocks_here + jnp.arange(blocks_here)[:, None] + offsets[None, :]
    inside = (window_ids >= 0) & (window_ids < block_total)
    reach = jnp.abs(offsets)[None, :, None] <= window_blocks[None, None, :]
    window_valid = inside[:, :, None] & reach
    owner_global = global_blocks // blocks_here
    local_global = jnp.clip(global_blocks - seq_place * blocks_here, 0, blocks_here - 1)
    mine_global = owner_global == seq_place
    query_view = query_rot.reshape(blocks_here, BLOCK, width_here)
    key_view = key_rot.reshape(blocks_here, BLOCK, width_here)
    value_view = values.reshape(blocks_here, BLOCK, width_here)
    picked = jnp.stack([query_view[local_global], key_view[local_global], value_view[local_global]])
    masked = jnp.where(mine_global[None, :, None, None], picked, jnp.zeros_like(picked))
    shared = tree_reduce(masked.reshape(3 * GLOB * BLOCK, width_here), add_merge, "seq")
    shared = shared.reshape(3, GLOB, BLOCK, width_here)
    halo = WMAX * BLOCK
    seq_ends = seq_count - 1
    halo_kv, shared = lax.optimization_barrier((pair_kv, shared))
    from_left = lax.ppermute(
        halo_kv[:, tok_here - halo :], "seq", [(i, (i + 1) % seq_count) for i in range(seq_ends)]
    ).reshape(2, WMAX, BLOCK, width_here)
    from_right = lax.ppermute(
        halo_kv[:, :halo], "seq", [((i + 1) % seq_count, i) for i in range(seq_ends)]
    ).reshape(2, WMAX, BLOCK, width_here)
    slot_parts = [
        jnp.stack(
            [padded_block(block + offset_slot) for offset_slot in range(2 * WMAX + 1)], axis=1
        )
        for block in range(blocks_here)
    ]
    global_kv = jnp.broadcast_to(shared[1:3][:, None], (2, blocks_here, GLOB, BLOCK, width_here))
    near_kv = jnp.concatenate([jnp.stack(slot_parts, axis=1), global_kv], axis=2)
    near_valid = jnp.concatenate(
        [window_valid, jnp.ones((blocks_here, GLOB, heads_here), dtype=bool)], axis=1
    )
    global_query = shared[0]
    key_later = key_rot
    value_later = values
    global_query = global_query.reshape(GLOB, BLOCK, heads_here, HEAD_DIM)
    key_grid = key_later.reshape(tok_here, heads_here, HEAD_DIM)
    value_grid = value_later.reshape(tok_here, heads_here, HEAD_DIM)
    global_scores = jnp.einsum(
        "gqhd,khd->gqhk", global_query, key_grid, preferred_element_type=jnp.float32
    ) * (1.0 / math.sqrt(HEAD_DIM))
    local_peak = jnp.max(global_scores, axis=3)
    expo = jnp.exp(global_scores - local_peak[..., None])
    partial_total = jnp.sum(expo, axis=3)
    partial_mix = jnp.einsum(
        "gqhk,khd->gqhd", expo.astype(jnp.bfloat16), value_grid, preferred_element_type=jnp.float32
    )
    row_total = GLOB * BLOCK
    packed = jnp.concatenate(
        [
            partial_mix.reshape(row_total, width_here),
            partial_total.reshape(row_total, heads_here),
            local_peak.reshape(row_total, heads_here),
            jnp.zeros((row_total, 128 - 2 * heads_here), jnp.float32),
        ],
        axis=1,
    )
    slot_total = blocks_here * RAND
    capacity = (slot_total + seq_count - 1) // seq_count
    flat_ids = random_blocks.reshape(seq_count, slot_total)
    owners = flat_ids // blocks_here
    slot_order = jnp.arange(slot_total)
    same_owner = (owners[:, :, None] == owners[:, None, :]) & (
        slot_order[None, None, :] < slot_order[None, :, None]
    )
    ranks = jnp.sum(same_owner.astype(jnp.int32), axis=2)
    local_ids = flat_ids - owners * blocks_here
    wanted = (owners[:, None, :] == seq_place) & (
        ranks[:, None, :] == jnp.arange(capacity)[None, :, None]
    )
    send_local = jnp.sum(jnp.where(wanted, local_ids[:, None, :], 0), axis=2)
    kv_blocks = jnp.transpose(halo_kv.reshape(2, blocks_here, BLOCK, width_here), (1, 0, 2, 3))
    outgoing = kv_blocks[send_local]
    packed, from_left, from_right, outgoing = lax.optimization_barrier(
        (packed, from_left, from_right, outgoing)
    )
    incoming = lax.all_to_all(outgoing, "seq", split_axis=0, concat_axis=0, tiled=True)
    packed, incoming = lax.optimization_barrier((packed, incoming))
    reduced = tree_reduce(packed, softmax_merge, "seq")
    my_owners = owners[seq_place]
    my_ranks = ranks[seq_place]
    random_k = incoming[my_owners, my_ranks, 0].reshape(blocks_here, RAND, BLOCK, width_here)
    random_v = incoming[my_owners, my_ranks, 1].reshape(blocks_here, RAND, BLOCK, width_here)
    random_kv = (random_k, random_v)
    near_part = partial_attend(query_view, near_kv[0], near_kv[1], near_valid)
    far_part = partial_attend(
        query_view, random_kv[0], random_kv[1], jnp.ones((blocks_here, RAND, heads_here), dtype=bool)
    )
    attended = merge_attend(near_part, far_part)
    mix_sum = reduced[:, :width_here].reshape(row_total, heads_here, HEAD_DIM)
    total_sum = reduced[:, width_here : width_here + heads_here]
    global_out = (mix_sum / total_sum[..., None]).reshape(row_total, width_here).astype(jnp.bfloat16)
    global_out = global_out.reshape(GLOB, BLOCK, width_here)
    block_index = jnp.arange(blocks_here)
    for global_slot in range(GLOB):
        hit = mine_global[global_slot] & (block_index == local_global[global_slot])
        attended = jnp.where(hit[:, None, None], global_out[global_slot][None], attended)
    mixed = sum_over_head(head_partials(attended.reshape(tok_here, width_here), out_weight))
    return mixed.astype(jnp.bfloat16)


def solution(mesh):
    in_specs = (
        P("seq", "head"),
        P("seq", "head"),
        P("seq", "head"),
        P("head", None),
        P(),
        P(),
        P("head"),
        P(),
        P(),
    )
    out_specs = P("seq", "head")
    return jax.shard_map(
        on_device, mesh=mesh, in_specs=in_specs, out_specs=out_specs, check_vma=False
    )
```

```python
import math

import jax
import jax.numpy as jnp
from jax import lax
from jax.sharding import PartitionSpec as P

HEAD_DIM = 128
BLOCK = 64
GLOB = 2
RAND = 3
WMAX = 2


masked_score = -1e30


def padded_2(cells, sides, width):
    for axis, dim in sides:
        count = lax.axis_size(axis)
        ends = count - 1
        head = lax.slice_in_dim(cells, 0, width, axis=dim)
        tail = lax.slice_in_dim(cells, cells.shape[dim] - width, cells.shape[dim], axis=dim)
        cells = jnp.concatenate(
            [
                lax.ppermute(tail, axis, [(i, (i + 1) % count) for i in range(ends)]),
                cells,
                lax.ppermute(head, axis, [((i + 1) % count, i) for i in range(ends)]),
            ],
            axis=dim,
        )
    return cells


def yarn_tables(yarn_scale, yarn_context):
    half_dim = HEAD_DIM // 2
    pair_index = jnp.arange(half_dim).astype(jnp.float32)
    base_rate = 10000.0 ** (-2.0 * pair_index / HEAD_DIM)
    factor = yarn_scale[0].astype(jnp.float32)
    context = yarn_context[0].astype(jnp.float32)
    turn_ratio = context * base_rate / (2.0 * math.pi)
    ramp_weight = jnp.clip((turn_ratio - 1.0) / 31.0, 0.0, 1.0)
    frequency = base_rate * ((1.0 - ramp_weight) / factor + ramp_weight)
    mscale = 0.1 * jnp.log(factor) + 1.0
    return (frequency, mscale)


def rotate(source, first_row, frequency, mscale):
    row_count, row_width = source.shape
    half_dim = HEAD_DIM // 2
    position = (first_row + jnp.arange(row_count)).astype(jnp.float32)
    angle_table = position[:, None] * frequency[None, :]
    cosine = jnp.cos(angle_table) * mscale
    sine_part = jnp.sin(angle_table) * mscale
    cosine = jnp.concatenate([cosine, cosine], axis=1)[:, None, :]
    sine_part = jnp.concatenate([sine_part, sine_part], axis=1)[:, None, :]
    grid = source.astype(jnp.float32).reshape(row_count, row_width // HEAD_DIM, HEAD_DIM)
    turned_half = jnp.concatenate([-grid[..., half_dim:], grid[..., :half_dim]], axis=2)
    turned = grid * cosine + turned_half * sine_part
    return turned.reshape(row_count, row_width).astype(jnp.bfloat16)


def block_attend(query_blocks, key_blocks, value_blocks, valid_slots):
    count_q, slot_count = (key_blocks.shape[0], key_blocks.shape[1])
    heads_here = query_blocks.shape[-1] // HEAD_DIM
    query_grid = query_blocks.reshape(count_q, BLOCK, heads_here, HEAD_DIM)
    key_grid = key_blocks.reshape(count_q, slot_count * BLOCK, heads_here, HEAD_DIM)
    value_grid = value_blocks.reshape(count_q, slot_count * BLOCK, heads_here, HEAD_DIM)
    scores = jnp.einsum(
        "bqhd,bshd->bhqs", query_grid, key_grid, preferred_element_type=jnp.float32
    ) * (1.0 / math.sqrt(HEAD_DIM))
    present = jnp.repeat(jnp.transpose(valid_slots, (0, 2, 1)), BLOCK, axis=2)[:, :, None, :]
    scores = jnp.where(present, scores, masked_score)
    peak = jnp.max(scores, axis=3, keepdims=True)
    expo = jnp.exp(scores - peak)
    total = jnp.sum(expo, axis=3)
    weights = expo.astype(jnp.bfloat16)
    mixture = jnp.einsum("bhqs,bshd->bqhd", weights, value_grid, preferred_element_type=jnp.float32)
    mixture = mixture / jnp.transpose(total, (0, 2, 1))[..., None]
    return mixture.reshape(count_q, BLOCK, heads_here * HEAD_DIM).astype(jnp.bfloat16)


def xor_perm(count, bit):
    return [(i, i ^ bit) for i in range(count)]


def tree_reduce(parts, merge, axis):
    count = lax.axis_size(axis)
    place = lax.axis_index(axis)
    bits = []
    bit = 1
    while bit < count:
        bits.append(bit)
        bit *= 2
    for bit in bits:
        upper = (place // bit) % 2
        halves = jax.tree.map(lambda x: x.reshape((2, x.shape[0] // 2) + x.shape[1:]), parts)
        keep = jax.tree.map(lambda h: lax.dynamic_index_in_dim(h, upper, 0, keepdims=False), halves)
        send = jax.tree.map(lambda h: lax.dynamic_index_in_dim(h, 1 - upper, 0, keepdims=False), halves)
        got = lax.ppermute(send, axis, xor_perm(count, bit))
        parts = merge(keep, got)
    for bit in reversed(bits):
        upper = (place // bit) % 2
        got = lax.ppermute(parts, axis, xor_perm(count, bit))

        def join(mine, theirs):
            pair = jnp.stack([mine, theirs])
            first = lax.dynamic_index_in_dim(pair, upper, 0, keepdims=False)
            second = lax.dynamic_index_in_dim(pair, 1 - upper, 0, keepdims=False)
            return jnp.concatenate([first, second], axis=0)

        parts = jax.tree.map(join, parts, got)
    return parts


def tree_scatter(parts, merge, axis):
    count = lax.axis_size(axis)
    place = lax.axis_index(axis)
    bit = 1
    while bit < count:
        upper = (place // bit) % 2
        halves = parts.reshape((2, parts.shape[0] // 2) + parts.shape[1:])
        keep = lax.dynamic_index_in_dim(halves, upper, 0, keepdims=False)
        send = lax.dynamic_index_in_dim(halves, 1 - upper, 0, keepdims=False)
        parts = merge(keep, lax.ppermute(send, axis, xor_perm(count, bit)))
        bit *= 2
    return parts


def bit_reversed(count):
    width = count.bit_length() - 1
    return [int(format(i, "0%db" % width)[::-1], 2) if width else 0 for i in range(count)]


def add_merge(a, b):
    return jax.tree.map(jnp.add, a, b)


def softmax_merge(a, b):
    width = a.shape[1] - 128
    heads = width // HEAD_DIM
    peak_a = a[:, width + heads : width + 2 * heads]
    peak_b = b[:, width + heads : width + 2 * heads]
    peak = jnp.maximum(peak_a, peak_b)
    scale_a = jnp.exp(peak_a - peak)
    scale_b = jnp.exp(peak_b - peak)
    rows = a.shape[0]
    mix = (
        a[:, :width].reshape(rows, heads, HEAD_DIM) * scale_a[..., None]
        + b[:, :width].reshape(rows, heads, HEAD_DIM) * scale_b[..., None]
    ).reshape(rows, width)
    total = a[:, width : width + heads] * scale_a + b[:, width : width + heads] * scale_b
    pad = jnp.zeros((rows, 128 - 2 * heads), a.dtype)
    return jnp.concatenate([mix, total, peak, pad], axis=1)


def head_partials(rows, out_weight):
    head_count = lax.axis_size("head")
    partial = lax.dot_general(
        out_weight, rows, (((0,), (1,)), ((), ())), preferred_element_type=jnp.float32
    ).astype(jnp.bfloat16)
    return partial.reshape(head_count, out_weight.shape[1] // head_count, rows.shape[0])


def sum_over_head(partial):
    gathered = lax.all_to_all(partial, "head", 0, 0, tiled=True)
    return jnp.sum(gathered.astype(jnp.float32), axis=0).T


def partial_attend(query_blocks, key_blocks, value_blocks, valid_slots):
    count_q, slot_count = (key_blocks.shape[0], key_blocks.shape[1])
    heads_here = query_blocks.shape[-1] // HEAD_DIM
    query_grid = query_blocks.reshape(count_q, BLOCK, heads_here, HEAD_DIM)
    key_grid = key_blocks.reshape(count_q, slot_count * BLOCK, heads_here, HEAD_DIM)
    value_grid = value_blocks.reshape(count_q, slot_count * BLOCK, heads_here, HEAD_DIM)
    scores = jnp.einsum(
        "bqhd,bshd->bhqs", query_grid, key_grid, preferred_element_type=jnp.float32
    ) * (1.0 / math.sqrt(HEAD_DIM))
    present = jnp.repeat(jnp.transpose(valid_slots, (0, 2, 1)), BLOCK, axis=2)[:, :, None, :]
    scores = jnp.where(present, scores, masked_score)
    peak = jnp.max(scores, axis=3)
    expo = jnp.exp(scores - peak[..., None])
    total = jnp.sum(expo, axis=3)
    mixture = jnp.einsum(
        "bhqs,bshd->bqhd", expo.astype(jnp.bfloat16), value_grid, preferred_element_type=jnp.float32
    )
    return mixture, total, peak


def merge_attend(first, second):
    mix_a, total_a, peak_a = first
    mix_b, total_b, peak_b = second
    peak = jnp.maximum(peak_a, peak_b)
    scale_a = jnp.exp(peak_a - peak)
    scale_b = jnp.exp(peak_b - peak)
    total = total_a * scale_a + total_b * scale_b
    mix = mix_a * jnp.transpose(scale_a, (0, 2, 1))[..., None] + mix_b * jnp.transpose(scale_b, (0, 2, 1))[..., None]
    mix = mix / jnp.transpose(total, (0, 2, 1))[..., None]
    count_q = mix.shape[0]
    return mix.reshape(count_q, BLOCK, -1).astype(jnp.bfloat16)


def on_device(
    queries,
    keys,
    values,
    out_weight,
    global_blocks,
    random_blocks,
    window_blocks,
    yarn_scale,
    yarn_context,
):
    tok_here, width_here = queries.shape
    heads_here = width_here // HEAD_DIM
    blocks_here = tok_here // BLOCK
    seq_count = lax.axis_size("seq")
    seq_place = lax.axis_index("seq")
    block_total = seq_count * blocks_here
    frequency, mscale = yarn_tables(yarn_scale, yarn_context)
    first_row = seq_place * tok_here
    query_rot = rotate(queries, first_row, frequency, mscale)
    key_rot = rotate(keys, first_row, frequency, mscale)
    pair_kv = jnp.stack([key_rot, values])
    local_blocks = pair_kv.reshape(2, blocks_here, BLOCK, width_here)

    def padded_block(index):
        if index < WMAX:
            return from_left[:, index]
        if index < WMAX + blocks_here:
            return local_blocks[:, index - WMAX]
        return from_right[:, index - WMAX - blocks_here]

    offsets = jnp.arange(-WMAX, WMAX + 1)
    window_ids = seq_place * blocks_here + jnp.arange(blocks_here)[:, None] + offsets[None, :]
    inside = (window_ids >= 0) & (window_ids < block_total)
    reach = jnp.abs(offsets)[None, :, None] <= window_blocks[None, None, :]
    window_valid = inside[:, :, None] & reach
    owner_global = global_blocks // blocks_here
    local_global = jnp.clip(global_blocks - seq_place * blocks_here, 0, blocks_here - 1)
    mine_global = owner_global == seq_place
    query_view = query_rot.reshape(blocks_here, BLOCK, width_here)
    key_view = key_rot.reshape(blocks_here, BLOCK, width_here)
    value_view = values.reshape(blocks_here, BLOCK, width_here)
    picked = jnp.stack([query_view[local_global], key_view[local_global], value_view[local_global]])
    masked = jnp.where(mine_global[None, :, None, None], picked, jnp.zeros_like(picked))
    shared = tree_reduce(masked.reshape(3 * GLOB * BLOCK, width_here), add_merge, "seq")
    shared = shared.reshape(3, GLOB, BLOCK, width_here)
    halo = WMAX * BLOCK
    seq_ends = seq_count - 1
    halo_kv, shared = lax.optimization_barrier((pair_kv, shared))
    from_left = lax.ppermute(
        halo_kv[:, tok_here - halo :], "seq", [(i, (i + 1) % seq_count) for i in range(seq_ends)]
    ).reshape(2, WMAX, BLOCK, width_here)
    from_right = lax.ppermute(
        halo_kv[:, :halo], "seq", [((i + 1) % seq_count, i) for i in range(seq_ends)]
    ).reshape(2, WMAX, BLOCK, width_here)
    slot_parts = [
        jnp.stack(
            [padded_block(block + offset_slot) for offset_slot in range(2 * WMAX + 1)], axis=1
        )
        for block in range(blocks_here)
    ]
    global_kv = jnp.broadcast_to(shared[1:3][:, None], (2, blocks_here, GLOB, BLOCK, width_here))
    near_kv = jnp.concatenate([jnp.stack(slot_parts, axis=1), global_kv], axis=2)
    near_valid = jnp.concatenate(
        [window_valid, jnp.ones((blocks_here, GLOB, heads_here), dtype=bool)], axis=1
    )
    global_query = shared[0]
    key_later = key_rot
    value_later = values
    global_query = global_query.reshape(GLOB, BLOCK, heads_here, HEAD_DIM)
    key_grid = key_later.reshape(tok_here, heads_here, HEAD_DIM)
    value_grid = value_later.reshape(tok_here, heads_here, HEAD_DIM)
    global_scores = jnp.einsum(
        "gqhd,khd->gqhk", global_query, key_grid, preferred_element_type=jnp.float32
    ) * (1.0 / math.sqrt(HEAD_DIM))
    local_peak = jnp.max(global_scores, axis=3)
    expo = jnp.exp(global_scores - local_peak[..., None])
    partial_total = jnp.sum(expo, axis=3)
    partial_mix = jnp.einsum(
        "gqhk,khd->gqhd", expo.astype(jnp.bfloat16), value_grid, preferred_element_type=jnp.float32
    )
    row_total = GLOB * BLOCK
    packed = jnp.concatenate(
        [
            partial_mix.reshape(row_total, width_here),
            partial_total.reshape(row_total, heads_here),
            local_peak.reshape(row_total, heads_here),
            jnp.zeros((row_total, 128 - 2 * heads_here), jnp.float32),
        ],
        axis=1,
    )
    slot_total = blocks_here * RAND
    capacity = (slot_total + seq_count - 1) // seq_count
    flat_ids = random_blocks.reshape(seq_count, slot_total)
    owners = flat_ids // blocks_here
    slot_order = jnp.arange(slot_total)
    same_owner = (owners[:, :, None] == owners[:, None, :]) & (
        slot_order[None, None, :] < slot_order[None, :, None]
    )
    ranks = jnp.sum(same_owner.astype(jnp.int32), axis=2)
    local_ids = flat_ids - owners * blocks_here
    wanted = (owners[:, None, :] == seq_place) & (
        ranks[:, None, :] == jnp.arange(capacity)[None, :, None]
    )
    send_local = jnp.sum(jnp.where(wanted, local_ids[:, None, :], 0), axis=2)
    kv_blocks = jnp.transpose(halo_kv.reshape(2, blocks_here, BLOCK, width_here), (1, 0, 2, 3))
    outgoing = kv_blocks[send_local]
    packed, from_left, from_right, outgoing = lax.optimization_barrier(
        (packed, from_left, from_right, outgoing)
    )
    slice_part = tree_scatter(packed, softmax_merge, "seq")
    slice_rows = (
        (slice_part[:, :width_here].reshape(-1, heads_here, HEAD_DIM) / slice_part[:, width_here : width_here + heads_here, None])
        .reshape(-1, width_here)
        .astype(jnp.bfloat16)
    )
    rows_each = slice_rows.shape[0]
    kv_rows = capacity * 2 * BLOCK
    outgoing = jnp.concatenate(
        [
            outgoing.reshape(seq_count, kv_rows, width_here),
            jnp.broadcast_to(slice_rows[None], (seq_count, rows_each, width_here)),
        ],
        axis=1,
    )
    incoming = lax.all_to_all(outgoing, "seq", split_axis=0, concat_axis=0, tiled=True)
    global_rows = incoming[:, kv_rows:][jnp.array(bit_reversed(seq_count))]
    incoming = incoming[:, :kv_rows].reshape(seq_count, capacity, 2, BLOCK, width_here)
    my_owners = owners[seq_place]
    my_ranks = ranks[seq_place]
    random_k = incoming[my_owners, my_ranks, 0].reshape(blocks_here, RAND, BLOCK, width_here)
    random_v = incoming[my_owners, my_ranks, 1].reshape(blocks_here, RAND, BLOCK, width_here)
    random_kv = (random_k, random_v)
    near_part = partial_attend(query_view, near_kv[0], near_kv[1], near_valid)
    far_part = partial_attend(
        query_view, random_kv[0], random_kv[1], jnp.ones((blocks_here, RAND, heads_here), dtype=bool)
    )
    attended = merge_attend(near_part, far_part)
    global_out = global_rows.reshape(row_total, width_here)
    global_out = global_out.reshape(GLOB, BLOCK, width_here)
    block_index = jnp.arange(blocks_here)
    for global_slot in range(GLOB):
        hit = mine_global[global_slot] & (block_index == local_global[global_slot])
        attended = jnp.where(hit[:, None, None], global_out[global_slot][None], attended)
    mixed = sum_over_head(head_partials(attended.reshape(tok_here, width_here), out_weight))
    return mixed.astype(jnp.bfloat16)


def solution(mesh):
    in_specs = (
        P("seq", "head"),
        P("seq", "head"),
        P("seq", "head"),
        P("head", None),
        P(),
        P(),
        P("head"),
        P(),
        P(),
    )
    out_specs = P("seq", "head")
    return jax.shard_map(
        on_device, mesh=mesh, in_specs=in_specs, out_specs=out_specs, check_vma=False
    )
```

```python
import math

import jax
import jax.numpy as jnp
from jax import lax
from jax.sharding import PartitionSpec as P

HEAD_DIM = 128
BLOCK = 64
GLOB = 2
RAND = 3
WMAX = 2


masked_score = -1e30


def padded_2(cells, sides, width):
    for axis, dim in sides:
        count = lax.axis_size(axis)
        ends = count - 1
        head = lax.slice_in_dim(cells, 0, width, axis=dim)
        tail = lax.slice_in_dim(cells, cells.shape[dim] - width, cells.shape[dim], axis=dim)
        cells = jnp.concatenate(
            [
                lax.ppermute(tail, axis, [(i, (i + 1) % count) for i in range(ends)]),
                cells,
                lax.ppermute(head, axis, [((i + 1) % count, i) for i in range(ends)]),
            ],
            axis=dim,
        )
    return cells


def yarn_tables(yarn_scale, yarn_context):
    half_dim = HEAD_DIM // 2
    pair_index = jnp.arange(half_dim).astype(jnp.float32)
    base_rate = 10000.0 ** (-2.0 * pair_index / HEAD_DIM)
    factor = yarn_scale[0].astype(jnp.float32)
    context = yarn_context[0].astype(jnp.float32)
    turn_ratio = context * base_rate / (2.0 * math.pi)
    ramp_weight = jnp.clip((turn_ratio - 1.0) / 31.0, 0.0, 1.0)
    frequency = base_rate * ((1.0 - ramp_weight) / factor + ramp_weight)
    mscale = 0.1 * jnp.log(factor) + 1.0
    return (frequency, mscale)


def rotate(source, first_row, frequency, mscale):
    row_count, row_width = source.shape
    half_dim = HEAD_DIM // 2
    position = (first_row + jnp.arange(row_count)).astype(jnp.float32)
    angle_table = position[:, None] * frequency[None, :]
    cosine = jnp.cos(angle_table) * mscale
    sine_part = jnp.sin(angle_table) * mscale
    cosine = jnp.concatenate([cosine, cosine], axis=1)[:, None, :]
    sine_part = jnp.concatenate([sine_part, sine_part], axis=1)[:, None, :]
    grid = source.astype(jnp.float32).reshape(row_count, row_width // HEAD_DIM, HEAD_DIM)
    turned_half = jnp.concatenate([-grid[..., half_dim:], grid[..., :half_dim]], axis=2)
    turned = grid * cosine + turned_half * sine_part
    return turned.reshape(row_count, row_width).astype(jnp.bfloat16)


def block_attend(query_blocks, key_blocks, value_blocks, valid_slots):
    count_q, slot_count = (key_blocks.shape[0], key_blocks.shape[1])
    heads_here = query_blocks.shape[-1] // HEAD_DIM
    query_grid = query_blocks.reshape(count_q, BLOCK, heads_here, HEAD_DIM)
    key_grid = key_blocks.reshape(count_q, slot_count * BLOCK, heads_here, HEAD_DIM)
    value_grid = value_blocks.reshape(count_q, slot_count * BLOCK, heads_here, HEAD_DIM)
    scores = jnp.einsum(
        "bqhd,bshd->bhqs", query_grid, key_grid, preferred_element_type=jnp.float32
    ) * (1.0 / math.sqrt(HEAD_DIM))
    present = jnp.repeat(jnp.transpose(valid_slots, (0, 2, 1)), BLOCK, axis=2)[:, :, None, :]
    scores = jnp.where(present, scores, masked_score)
    peak = jnp.max(scores, axis=3, keepdims=True)
    expo = jnp.exp(scores - peak)
    total = jnp.sum(expo, axis=3)
    weights = expo.astype(jnp.bfloat16)
    mixture = jnp.einsum("bhqs,bshd->bqhd", weights, value_grid, preferred_element_type=jnp.float32)
    mixture = mixture / jnp.transpose(total, (0, 2, 1))[..., None]
    return mixture.reshape(count_q, BLOCK, heads_here * HEAD_DIM).astype(jnp.bfloat16)


def xor_perm(count, bit):
    return [(i, i ^ bit) for i in range(count)]


def tree_reduce(parts, merge, axis):
    count = lax.axis_size(axis)
    place = lax.axis_index(axis)
    bits = []
    bit = 1
    while bit < count:
        bits.append(bit)
        bit *= 2
    for bit in bits:
        upper = (place // bit) % 2
        halves = jax.tree.map(lambda x: x.reshape((2, x.shape[0] // 2) + x.shape[1:]), parts)
        keep = jax.tree.map(lambda h: lax.dynamic_index_in_dim(h, upper, 0, keepdims=False), halves)
        send = jax.tree.map(lambda h: lax.dynamic_index_in_dim(h, 1 - upper, 0, keepdims=False), halves)
        got = lax.ppermute(send, axis, xor_perm(count, bit))
        parts = merge(keep, got)
    for bit in reversed(bits):
        upper = (place // bit) % 2
        got = lax.ppermute(parts, axis, xor_perm(count, bit))

        def join(mine, theirs):
            pair = jnp.stack([mine, theirs])
            first = lax.dynamic_index_in_dim(pair, upper, 0, keepdims=False)
            second = lax.dynamic_index_in_dim(pair, 1 - upper, 0, keepdims=False)
            return jnp.concatenate([first, second], axis=0)

        parts = jax.tree.map(join, parts, got)
    return parts


def tree_scatter(parts, merge, axis):
    count = lax.axis_size(axis)
    place = lax.axis_index(axis)
    bit = 1
    while bit < count:
        upper = (place // bit) % 2
        halves = parts.reshape((2, parts.shape[0] // 2) + parts.shape[1:])
        keep = lax.dynamic_index_in_dim(halves, upper, 0, keepdims=False)
        send = lax.dynamic_index_in_dim(halves, 1 - upper, 0, keepdims=False)
        parts = merge(keep, lax.ppermute(send, axis, xor_perm(count, bit)))
        bit *= 2
    return parts


def bit_reversed(count):
    width = count.bit_length() - 1
    return [int(format(i, "0%db" % width)[::-1], 2) if width else 0 for i in range(count)]


def add_merge(a, b):
    return jax.tree.map(jnp.add, a, b)


def softmax_merge(a, b):
    width = a.shape[1] - 128
    heads = width // HEAD_DIM
    peak_a = a[:, width + heads : width + 2 * heads]
    peak_b = b[:, width + heads : width + 2 * heads]
    peak = jnp.maximum(peak_a, peak_b)
    scale_a = jnp.exp(peak_a - peak)
    scale_b = jnp.exp(peak_b - peak)
    rows = a.shape[0]
    mix = (
        a[:, :width].reshape(rows, heads, HEAD_DIM) * scale_a[..., None]
        + b[:, :width].reshape(rows, heads, HEAD_DIM) * scale_b[..., None]
    ).reshape(rows, width)
    total = a[:, width : width + heads] * scale_a + b[:, width : width + heads] * scale_b
    pad = jnp.zeros((rows, 128 - 2 * heads), a.dtype)
    return jnp.concatenate([mix, total, peak, pad], axis=1)


def head_partials(rows, out_weight):
    head_count = lax.axis_size("head")
    partial = lax.dot_general(
        out_weight, rows, (((0,), (1,)), ((), ())), preferred_element_type=jnp.float32
    ).astype(jnp.bfloat16)
    return partial.reshape(head_count, out_weight.shape[1] // head_count, rows.shape[0])


def sum_over_head(partial):
    gathered = lax.all_to_all(partial, "head", 0, 0, tiled=True)
    return jnp.sum(gathered.astype(jnp.float32), axis=0).T


def partial_attend(query_blocks, key_blocks, value_blocks, valid_slots):
    count_q, slot_count = (key_blocks.shape[0], key_blocks.shape[1])
    heads_here = query_blocks.shape[-1] // HEAD_DIM
    query_grid = query_blocks.reshape(count_q, BLOCK, heads_here, HEAD_DIM)
    key_grid = key_blocks.reshape(count_q, slot_count * BLOCK, heads_here, HEAD_DIM)
    value_grid = value_blocks.reshape(count_q, slot_count * BLOCK, heads_here, HEAD_DIM)
    scores = jnp.einsum(
        "bqhd,bshd->bhqs", query_grid, key_grid, preferred_element_type=jnp.float32
    ) * (1.0 / math.sqrt(HEAD_DIM))
    present = jnp.repeat(jnp.transpose(valid_slots, (0, 2, 1)), BLOCK, axis=2)[:, :, None, :]
    scores = jnp.where(present, scores, masked_score)
    peak = jnp.max(scores, axis=3)
    expo = jnp.exp(scores - peak[..., None])
    total = jnp.sum(expo, axis=3)
    mixture = jnp.einsum(
        "bhqs,bshd->bqhd", expo.astype(jnp.bfloat16), value_grid, preferred_element_type=jnp.float32
    )
    return mixture, total, peak


def merge_attend(first, second):
    mix_a, total_a, peak_a = first
    mix_b, total_b, peak_b = second
    peak = jnp.maximum(peak_a, peak_b)
    scale_a = jnp.exp(peak_a - peak)
    scale_b = jnp.exp(peak_b - peak)
    total = total_a * scale_a + total_b * scale_b
    mix = mix_a * jnp.transpose(scale_a, (0, 2, 1))[..., None] + mix_b * jnp.transpose(scale_b, (0, 2, 1))[..., None]
    mix = mix / jnp.transpose(total, (0, 2, 1))[..., None]
    count_q = mix.shape[0]
    return mix.reshape(count_q, BLOCK, -1).astype(jnp.bfloat16)


def on_device(
    queries,
    keys,
    values,
    out_weight,
    global_blocks,
    random_blocks,
    window_blocks,
    yarn_scale,
    yarn_context,
):
    tok_here, width_here = queries.shape
    heads_here = width_here // HEAD_DIM
    blocks_here = tok_here // BLOCK
    seq_count = lax.axis_size("seq")
    seq_place = lax.axis_index("seq")
    block_total = seq_count * blocks_here
    frequency, mscale = yarn_tables(yarn_scale, yarn_context)
    first_row = seq_place * tok_here
    query_rot = rotate(queries, first_row, frequency, mscale)
    key_rot = rotate(keys, first_row, frequency, mscale)
    pair_kv = jnp.stack([key_rot, values])
    local_blocks = pair_kv.reshape(2, blocks_here, BLOCK, width_here)

    def padded_block(index):
        if index < WMAX:
            return from_left[:, index]
        if index < WMAX + blocks_here:
            return local_blocks[:, index - WMAX]
        return from_right[:, index - WMAX - blocks_here]

    offsets = jnp.arange(-WMAX, WMAX + 1)
    window_ids = seq_place * blocks_here + jnp.arange(blocks_here)[:, None] + offsets[None, :]
    inside = (window_ids >= 0) & (window_ids < block_total)
    reach = jnp.abs(offsets)[None, :, None] <= window_blocks[None, None, :]
    window_valid = inside[:, :, None] & reach
    owner_global = global_blocks // blocks_here
    local_global = jnp.clip(global_blocks - seq_place * blocks_here, 0, blocks_here - 1)
    mine_global = owner_global == seq_place
    query_view = query_rot.reshape(blocks_here, BLOCK, width_here)
    key_view = key_rot.reshape(blocks_here, BLOCK, width_here)
    value_view = values.reshape(blocks_here, BLOCK, width_here)
    picked = jnp.stack([query_view[local_global], key_view[local_global], value_view[local_global]])
    masked = jnp.where(mine_global[None, :, None, None], picked, jnp.zeros_like(picked))
    shared = tree_reduce(masked.reshape(3 * GLOB * BLOCK, width_here), add_merge, "seq")
    shared = shared.reshape(3, GLOB, BLOCK, width_here)
    halo = WMAX * BLOCK
    seq_ends = seq_count - 1
    halo_kv, shared = lax.optimization_barrier((pair_kv, shared))
    from_left = lax.ppermute(
        halo_kv[:, tok_here - halo :], "seq", [(i, (i + 1) % seq_count) for i in range(seq_ends)]
    ).reshape(2, WMAX, BLOCK, width_here)
    from_right = lax.ppermute(
        halo_kv[:, :halo], "seq", [((i + 1) % seq_count, i) for i in range(seq_ends)]
    ).reshape(2, WMAX, BLOCK, width_here)
    slot_parts = [
        jnp.stack(
            [padded_block(block + offset_slot) for offset_slot in range(2 * WMAX + 1)], axis=1
        )
        for block in range(blocks_here)
    ]
    global_kv = jnp.broadcast_to(shared[1:3][:, None], (2, blocks_here, GLOB, BLOCK, width_here))
    near_kv = jnp.concatenate([jnp.stack(slot_parts, axis=1), global_kv], axis=2)
    near_valid = jnp.concatenate(
        [window_valid, jnp.ones((blocks_here, GLOB, heads_here), dtype=bool)], axis=1
    )
    global_query = shared[0]
    key_later = key_rot
    value_later = values
    global_query = global_query.reshape(GLOB, BLOCK, heads_here, HEAD_DIM)
    key_grid = key_later.reshape(tok_here, heads_here, HEAD_DIM)
    value_grid = value_later.reshape(tok_here, heads_here, HEAD_DIM)
    global_scores = jnp.einsum(
        "gqhd,khd->gqhk", global_query, key_grid, preferred_element_type=jnp.float32
    ) * (1.0 / math.sqrt(HEAD_DIM))
    local_peak = jnp.max(global_scores, axis=3)
    expo = jnp.exp(global_scores - local_peak[..., None])
    partial_total = jnp.sum(expo, axis=3)
    partial_mix = jnp.einsum(
        "gqhk,khd->gqhd", expo.astype(jnp.bfloat16), value_grid, preferred_element_type=jnp.float32
    )
    row_total = GLOB * BLOCK
    packed = jnp.concatenate(
        [
            partial_mix.reshape(row_total, width_here),
            partial_total.reshape(row_total, heads_here),
            local_peak.reshape(row_total, heads_here),
            jnp.zeros((row_total, 128 - 2 * heads_here), jnp.float32),
        ],
        axis=1,
    )
    slot_total = blocks_here * RAND
    capacity = (slot_total + seq_count - 1) // seq_count
    flat_ids = random_blocks.reshape(seq_count, slot_total)
    owners = flat_ids // blocks_here
    slot_order = jnp.arange(slot_total)
    same_owner = (owners[:, :, None] == owners[:, None, :]) & (
        slot_order[None, None, :] < slot_order[None, :, None]
    )
    ranks = jnp.sum(same_owner.astype(jnp.int32), axis=2)
    local_ids = flat_ids - owners * blocks_here
    wanted = (owners[:, None, :] == seq_place) & (
        ranks[:, None, :] == jnp.arange(capacity)[None, :, None]
    )
    send_local = jnp.sum(jnp.where(wanted, local_ids[:, None, :], 0), axis=2)
    kv_blocks = jnp.transpose(halo_kv.reshape(2, blocks_here, BLOCK, width_here), (1, 0, 2, 3))
    outgoing = kv_blocks[send_local]
    kv_rows = capacity * 2 * BLOCK
    rows_each = GLOB * BLOCK // seq_count
    outgoing = jnp.concatenate(
        [
            outgoing.reshape(seq_count, kv_rows, width_here),
            jnp.zeros((seq_count, rows_each, width_here), jnp.bfloat16),
        ],
        axis=1,
    )
    packed, from_left, from_right, outgoing = lax.optimization_barrier(
        (packed, from_left, from_right, outgoing)
    )
    slice_part = tree_scatter(packed, softmax_merge, "seq")
    slice_rows = (
        (slice_part[:, :width_here].reshape(-1, heads_here, HEAD_DIM) / slice_part[:, width_here : width_here + heads_here, None])
        .reshape(-1, width_here)
        .astype(jnp.bfloat16)
    )
    outgoing = lax.dynamic_update_slice(
        outgoing, jnp.broadcast_to(slice_rows[None], (seq_count, rows_each, width_here)), (0, kv_rows, 0)
    )
    incoming = lax.all_to_all(outgoing, "seq", split_axis=0, concat_axis=0, tiled=True)
    global_rows = incoming[:, kv_rows:][jnp.array(bit_reversed(seq_count))]
    my_owners = owners[seq_place]
    my_ranks = ranks[seq_place]
    slot_start = my_ranks * (2 * BLOCK)
    random_k = jnp.stack(
        [lax.dynamic_slice(incoming, (my_owners[j], slot_start[j], 0), (1, BLOCK, width_here))[0] for j in range(blocks_here * RAND)]
    ).reshape(blocks_here, RAND, BLOCK, width_here)
    random_v = jnp.stack(
        [lax.dynamic_slice(incoming, (my_owners[j], slot_start[j] + BLOCK, 0), (1, BLOCK, width_here))[0] for j in range(blocks_here * RAND)]
    ).reshape(blocks_here, RAND, BLOCK, width_here)
    random_kv = (random_k, random_v)
    near_part = partial_attend(query_view, near_kv[0], near_kv[1], near_valid)
    far_part = partial_attend(
        query_view, random_kv[0], random_kv[1], jnp.ones((blocks_here, RAND, heads_here), dtype=bool)
    )
    attended = merge_attend(near_part, far_part)
    global_out = global_rows.reshape(row_total, width_here)
    global_out = global_out.reshape(GLOB, BLOCK, width_here)
    block_index = jnp.arange(blocks_here)
    for global_slot in range(GLOB):
        hit = mine_global[global_slot] & (block_index == local_global[global_slot])
        attended = jnp.where(hit[:, None, None], global_out[global_slot][None], attended)
    mixed = sum_over_head(head_partials(attended.reshape(tok_here, width_here), out_weight))
    return mixed.astype(jnp.bfloat16)


def solution(mesh):
    in_specs = (
        P("seq", "head"),
        P("seq", "head"),
        P("seq", "head"),
        P("head", None),
        P(),
        P(),
        P("head"),
        P(),
        P(),
    )
    out_specs = P("seq", "head")
    return jax.shard_map(
        on_device, mesh=mesh, in_specs=in_specs, out_specs=out_specs, check_vma=False
    )
```

```python
import math

import jax
import jax.numpy as jnp
from jax import lax
from jax.sharding import PartitionSpec as P

HEAD_DIM = 128
BLOCK = 64
GLOB = 2
RAND = 3
WMAX = 2


masked_score = -1e30


def padded_2(cells, sides, width):
    for axis, dim in sides:
        count = lax.axis_size(axis)
        ends = count - 1
        head = lax.slice_in_dim(cells, 0, width, axis=dim)
        tail = lax.slice_in_dim(cells, cells.shape[dim] - width, cells.shape[dim], axis=dim)
        cells = jnp.concatenate(
            [
                lax.ppermute(tail, axis, [(i, (i + 1) % count) for i in range(ends)]),
                cells,
                lax.ppermute(head, axis, [((i + 1) % count, i) for i in range(ends)]),
            ],
            axis=dim,
        )
    return cells


def yarn_tables(yarn_scale, yarn_context):
    half_dim = HEAD_DIM // 2
    pair_index = jnp.arange(half_dim).astype(jnp.float32)
    base_rate = 10000.0 ** (-2.0 * pair_index / HEAD_DIM)
    factor = yarn_scale[0].astype(jnp.float32)
    context = yarn_context[0].astype(jnp.float32)
    turn_ratio = context * base_rate / (2.0 * math.pi)
    ramp_weight = jnp.clip((turn_ratio - 1.0) / 31.0, 0.0, 1.0)
    frequency = base_rate * ((1.0 - ramp_weight) / factor + ramp_weight)
    mscale = 0.1 * jnp.log(factor) + 1.0
    return (frequency, mscale)


def rotate(source, first_row, frequency, mscale):
    row_count, row_width = source.shape
    half_dim = HEAD_DIM // 2
    position = (first_row + jnp.arange(row_count)).astype(jnp.float32)
    angle_table = position[:, None] * frequency[None, :]
    cosine = jnp.cos(angle_table) * mscale
    sine_part = jnp.sin(angle_table) * mscale
    cosine = jnp.concatenate([cosine, cosine], axis=1)[:, None, :]
    sine_part = jnp.concatenate([sine_part, sine_part], axis=1)[:, None, :]
    grid = source.astype(jnp.float32).reshape(row_count, row_width // HEAD_DIM, HEAD_DIM)
    turned_half = jnp.concatenate([-grid[..., half_dim:], grid[..., :half_dim]], axis=2)
    turned = grid * cosine + turned_half * sine_part
    return turned.reshape(row_count, row_width).astype(jnp.bfloat16)


def block_attend(query_blocks, key_blocks, value_blocks, valid_slots):
    count_q, slot_count = (key_blocks.shape[0], key_blocks.shape[1])
    heads_here = query_blocks.shape[-1] // HEAD_DIM
    query_grid = query_blocks.reshape(count_q, BLOCK, heads_here, HEAD_DIM)
    key_grid = key_blocks.reshape(count_q, slot_count * BLOCK, heads_here, HEAD_DIM)
    value_grid = value_blocks.reshape(count_q, slot_count * BLOCK, heads_here, HEAD_DIM)
    scores = jnp.einsum(
        "bqhd,bshd->bhqs", query_grid, key_grid, preferred_element_type=jnp.float32
    ) * (1.0 / math.sqrt(HEAD_DIM))
    present = jnp.repeat(jnp.transpose(valid_slots, (0, 2, 1)), BLOCK, axis=2)[:, :, None, :]
    scores = jnp.where(present, scores, masked_score)
    peak = jnp.max(scores, axis=3, keepdims=True)
    expo = jnp.exp(scores - peak)
    total = jnp.sum(expo, axis=3)
    weights = expo.astype(jnp.bfloat16)
    mixture = jnp.einsum("bhqs,bshd->bqhd", weights, value_grid, preferred_element_type=jnp.float32)
    mixture = mixture / jnp.transpose(total, (0, 2, 1))[..., None]
    return mixture.reshape(count_q, BLOCK, heads_here * HEAD_DIM).astype(jnp.bfloat16)


def xor_perm(count, bit):
    return [(i, i ^ bit) for i in range(count)]


def tree_reduce(parts, merge, axis):
    count = lax.axis_size(axis)
    place = lax.axis_index(axis)
    bits = []
    bit = 1
    while bit < count:
        bits.append(bit)
        bit *= 2
    for bit in bits:
        upper = (place // bit) % 2
        halves = jax.tree.map(lambda x: x.reshape((2, x.shape[0] // 2) + x.shape[1:]), parts)
        keep = jax.tree.map(lambda h: lax.dynamic_index_in_dim(h, upper, 0, keepdims=False), halves)
        send = jax.tree.map(lambda h: lax.dynamic_index_in_dim(h, 1 - upper, 0, keepdims=False), halves)
        got = lax.ppermute(send, axis, xor_perm(count, bit))
        parts = merge(keep, got)
    for bit in reversed(bits):
        upper = (place // bit) % 2
        got = lax.ppermute(parts, axis, xor_perm(count, bit))

        def join(mine, theirs):
            pair = jnp.stack([mine, theirs])
            first = lax.dynamic_index_in_dim(pair, upper, 0, keepdims=False)
            second = lax.dynamic_index_in_dim(pair, 1 - upper, 0, keepdims=False)
            return jnp.concatenate([first, second], axis=0)

        parts = jax.tree.map(join, parts, got)
    return parts


def tree_scatter(parts, merge, axis):
    count = lax.axis_size(axis)
    place = lax.axis_index(axis)
    bit = 1
    while bit < count:
        upper = (place // bit) % 2
        halves = parts.reshape((2, parts.shape[0] // 2) + parts.shape[1:])
        keep = lax.dynamic_index_in_dim(halves, upper, 0, keepdims=False)
        send = lax.dynamic_index_in_dim(halves, 1 - upper, 0, keepdims=False)
        parts = merge(keep, lax.ppermute(send, axis, xor_perm(count, bit)))
        bit *= 2
    return parts


def bit_reversed(count):
    width = count.bit_length() - 1
    return [int(format(i, "0%db" % width)[::-1], 2) if width else 0 for i in range(count)]


def add_merge(a, b):
    return jax.tree.map(jnp.add, a, b)


def softmax_merge(a, b):
    width = a.shape[1] - 128
    heads = width // HEAD_DIM
    peak_a = a[:, width + heads : width + 2 * heads]
    peak_b = b[:, width + heads : width + 2 * heads]
    peak = jnp.maximum(peak_a, peak_b)
    scale_a = jnp.exp(peak_a - peak)
    scale_b = jnp.exp(peak_b - peak)
    rows = a.shape[0]
    mix = (
        a[:, :width].reshape(rows, heads, HEAD_DIM) * scale_a[..., None]
        + b[:, :width].reshape(rows, heads, HEAD_DIM) * scale_b[..., None]
    ).reshape(rows, width)
    total = a[:, width : width + heads] * scale_a + b[:, width : width + heads] * scale_b
    pad = jnp.zeros((rows, 128 - 2 * heads), a.dtype)
    return jnp.concatenate([mix, total, peak, pad], axis=1)


def head_partials(rows, out_weight):
    head_count = lax.axis_size("head")
    partial = lax.dot_general(
        out_weight, rows, (((0,), (1,)), ((), ())), preferred_element_type=jnp.float32
    ).astype(jnp.bfloat16)
    return partial.reshape(head_count, out_weight.shape[1] // head_count, rows.shape[0])


def sum_over_head(partial):
    gathered = lax.all_to_all(partial, "head", 0, 0, tiled=True)
    return jnp.sum(gathered.astype(jnp.float32), axis=0).T


def partial_attend(query_blocks, key_blocks, value_blocks, valid_slots):
    count_q, slot_count = (key_blocks.shape[0], key_blocks.shape[1])
    heads_here = query_blocks.shape[-1] // HEAD_DIM
    query_grid = query_blocks.reshape(count_q, BLOCK, heads_here, HEAD_DIM)
    key_grid = key_blocks.reshape(count_q, slot_count * BLOCK, heads_here, HEAD_DIM)
    value_grid = value_blocks.reshape(count_q, slot_count * BLOCK, heads_here, HEAD_DIM)
    scores = jnp.einsum(
        "bqhd,bshd->bhqs", query_grid, key_grid, preferred_element_type=jnp.float32
    ) * (1.0 / math.sqrt(HEAD_DIM))
    present = jnp.repeat(jnp.transpose(valid_slots, (0, 2, 1)), BLOCK, axis=2)[:, :, None, :]
    scores = jnp.where(present, scores, masked_score)
    peak = jnp.max(scores, axis=3)
    expo = jnp.exp(scores - peak[..., None])
    total = jnp.sum(expo, axis=3)
    mixture = jnp.einsum(
        "bhqs,bshd->bqhd", expo.astype(jnp.bfloat16), value_grid, preferred_element_type=jnp.float32
    )
    return mixture, total, peak


def merge_attend(first, second):
    mix_a, total_a, peak_a = first
    mix_b, total_b, peak_b = second
    peak = jnp.maximum(peak_a, peak_b)
    scale_a = jnp.exp(peak_a - peak)
    scale_b = jnp.exp(peak_b - peak)
    total = total_a * scale_a + total_b * scale_b
    mix = mix_a * jnp.transpose(scale_a, (0, 2, 1))[..., None] + mix_b * jnp.transpose(scale_b, (0, 2, 1))[..., None]
    mix = mix / jnp.transpose(total, (0, 2, 1))[..., None]
    count_q = mix.shape[0]
    return mix.reshape(count_q, BLOCK, -1).astype(jnp.bfloat16)


def on_device(
    queries,
    keys,
    values,
    out_weight,
    global_blocks,
    random_blocks,
    window_blocks,
    yarn_scale,
    yarn_context,
):
    tok_here, width_here = queries.shape
    heads_here = width_here // HEAD_DIM
    blocks_here = tok_here // BLOCK
    seq_count = lax.axis_size("seq")
    seq_place = lax.axis_index("seq")
    block_total = seq_count * blocks_here
    frequency, mscale = yarn_tables(yarn_scale, yarn_context)
    first_row = seq_place * tok_here
    query_rot = rotate(queries, first_row, frequency, mscale)
    key_rot = rotate(keys, first_row, frequency, mscale)
    pair_kv = jnp.stack([key_rot, values])
    local_blocks = pair_kv.reshape(2, blocks_here, BLOCK, width_here)

    def padded_block(index):
        if index < WMAX:
            return from_left[:, index]
        if index < WMAX + blocks_here:
            return local_blocks[:, index - WMAX]
        return from_right[:, index - WMAX - blocks_here]

    offsets = jnp.arange(-WMAX, WMAX + 1)
    window_ids = seq_place * blocks_here + jnp.arange(blocks_here)[:, None] + offsets[None, :]
    inside = (window_ids >= 0) & (window_ids < block_total)
    reach = jnp.abs(offsets)[None, :, None] <= window_blocks[None, None, :]
    window_valid = inside[:, :, None] & reach
    owner_global = global_blocks // blocks_here
    local_global = jnp.clip(global_blocks - seq_place * blocks_here, 0, blocks_here - 1)
    mine_global = owner_global == seq_place
    query_view = query_rot.reshape(blocks_here, BLOCK, width_here)
    key_view = key_rot.reshape(blocks_here, BLOCK, width_here)
    value_view = values.reshape(blocks_here, BLOCK, width_here)
    picked = jnp.stack([query_view[local_global], key_view[local_global], value_view[local_global]])
    masked = jnp.where(mine_global[None, :, None, None], picked, jnp.zeros_like(picked))
    shared = tree_reduce(masked.reshape(3 * GLOB * BLOCK, width_here), add_merge, "seq")
    shared = shared.reshape(3, GLOB, BLOCK, width_here)
    halo = WMAX * BLOCK
    seq_ends = seq_count - 1
    halo_kv, shared = lax.optimization_barrier((pair_kv, shared))
    from_left = lax.ppermute(
        halo_kv[:, tok_here - halo :], "seq", [(i, (i + 1) % seq_count) for i in range(seq_ends)]
    ).reshape(2, WMAX, BLOCK, width_here)
    from_right = lax.ppermute(
        halo_kv[:, :halo], "seq", [((i + 1) % seq_count, i) for i in range(seq_ends)]
    ).reshape(2, WMAX, BLOCK, width_here)
    slot_parts = [
        jnp.stack(
            [padded_block(block + offset_slot) for offset_slot in range(2 * WMAX + 1)], axis=1
        )
        for block in range(blocks_here)
    ]
    global_kv = jnp.broadcast_to(shared[1:3][:, None], (2, blocks_here, GLOB, BLOCK, width_here))
    near_kv = jnp.concatenate([jnp.stack(slot_parts, axis=1), global_kv], axis=2)
    near_valid = jnp.concatenate(
        [window_valid, jnp.ones((blocks_here, GLOB, heads_here), dtype=bool)], axis=1
    )
    global_query = shared[0]
    key_later = key_rot
    value_later = values
    global_query = global_query.reshape(GLOB, BLOCK, heads_here, HEAD_DIM)
    key_grid = key_later.reshape(tok_here, heads_here, HEAD_DIM)
    value_grid = value_later.reshape(tok_here, heads_here, HEAD_DIM)
    global_scores = jnp.einsum(
        "gqhd,khd->gqhk", global_query, key_grid, preferred_element_type=jnp.float32
    ) * (1.0 / math.sqrt(HEAD_DIM))
    local_peak = jnp.max(global_scores, axis=3)
    expo = jnp.exp(global_scores - local_peak[..., None])
    partial_total = jnp.sum(expo, axis=3)
    partial_mix = jnp.einsum(
        "gqhk,khd->gqhd", expo.astype(jnp.bfloat16), value_grid, preferred_element_type=jnp.float32
    )
    row_total = GLOB * BLOCK
    packed = jnp.concatenate(
        [
            partial_mix.reshape(row_total, width_here),
            partial_total.reshape(row_total, heads_here),
            local_peak.reshape(row_total, heads_here),
            jnp.zeros((row_total, 128 - 2 * heads_here), jnp.float32),
        ],
        axis=1,
    )
    slot_total = blocks_here * RAND
    capacity = (slot_total + seq_count - 1) // seq_count
    flat_ids = random_blocks.reshape(seq_count, slot_total)
    owners = flat_ids // blocks_here
    slot_order = jnp.arange(slot_total)
    same_owner = (owners[:, :, None] == owners[:, None, :]) & (
        slot_order[None, None, :] < slot_order[None, :, None]
    )
    ranks = jnp.sum(same_owner.astype(jnp.int32), axis=2)
    local_ids = flat_ids - owners * blocks_here
    wanted = (owners[:, None, :] == seq_place) & (
        ranks[:, None, :] == jnp.arange(capacity)[None, :, None]
    )
    send_local = jnp.sum(jnp.where(wanted, local_ids[:, None, :], 0), axis=2)
    kv_blocks = jnp.transpose(halo_kv.reshape(2, blocks_here, BLOCK, width_here), (1, 0, 2, 3))
    outgoing = kv_blocks[send_local]
    kv_rows = capacity * 2 * BLOCK
    rows_each = GLOB * BLOCK // seq_count
    outgoing = jnp.concatenate(
        [
            outgoing.reshape(seq_count, kv_rows, width_here),
            jnp.zeros((seq_count, rows_each, width_here), jnp.bfloat16),
        ],
        axis=1,
    )
    packed, from_left, from_right, outgoing = lax.optimization_barrier(
        (packed, from_left, from_right, outgoing)
    )
    slice_part = tree_scatter(packed, softmax_merge, "seq")
    slice_rows = (
        (slice_part[:, :width_here].reshape(-1, heads_here, HEAD_DIM) / slice_part[:, width_here : width_here + heads_here, None])
        .reshape(-1, width_here)
        .astype(jnp.bfloat16)
    )
    outgoing = lax.dynamic_update_slice(
        outgoing, jnp.broadcast_to(slice_rows[None], (seq_count, rows_each, width_here)), (0, kv_rows, 0)
    )
    incoming = lax.all_to_all(outgoing, "seq", split_axis=0, concat_axis=0, tiled=True)
    global_rows = incoming[:, kv_rows:][jnp.array(bit_reversed(seq_count))]
    my_owners = owners[seq_place]
    my_ranks = ranks[seq_place]
    incoming = incoming[:, :kv_rows].reshape(seq_count, capacity, 2, BLOCK, width_here)
    random_k = incoming[my_owners, my_ranks, 0].reshape(blocks_here, RAND, BLOCK, width_here)
    random_v = incoming[my_owners, my_ranks, 1].reshape(blocks_here, RAND, BLOCK, width_here)
    random_kv = (random_k, random_v)
    near_part = partial_attend(query_view, near_kv[0], near_kv[1], near_valid)
    far_part = partial_attend(
        query_view, random_kv[0], random_kv[1], jnp.ones((blocks_here, RAND, heads_here), dtype=bool)
    )
    attended = merge_attend(near_part, far_part)
    global_out = global_rows.reshape(row_total, width_here)
    global_out = global_out.reshape(GLOB, BLOCK, width_here)
    block_index = jnp.arange(blocks_here)
    for global_slot in range(GLOB):
        hit = mine_global[global_slot] & (block_index == local_global[global_slot])
        attended = jnp.where(hit[:, None, None], global_out[global_slot][None], attended)
    mixed = sum_over_head(head_partials(attended.reshape(tok_here, width_here), out_weight))
    return mixed.astype(jnp.bfloat16)


def solution(mesh):
    in_specs = (
        P("seq", "head"),
        P("seq", "head"),
        P("seq", "head"),
        P("head", None),
        P(),
        P(),
        P("head"),
        P(),
        P(),
    )
    out_specs = P("seq", "head")
    return jax.shard_map(
        on_device, mesh=mesh, in_specs=in_specs, out_specs=out_specs, check_vma=False
    )
```

```python
import math

import jax
import jax.numpy as jnp
from jax import lax
from jax.sharding import PartitionSpec as P

HEAD_DIM = 128
BLOCK = 64
GLOB = 2
RAND = 3
WMAX = 2


masked_score = -1e30


def padded_2(cells, sides, width):
    for axis, dim in sides:
        count = lax.axis_size(axis)
        ends = count - 1
        head = lax.slice_in_dim(cells, 0, width, axis=dim)
        tail = lax.slice_in_dim(cells, cells.shape[dim] - width, cells.shape[dim], axis=dim)
        cells = jnp.concatenate(
            [
                lax.ppermute(tail, axis, [(i, (i + 1) % count) for i in range(ends)]),
                cells,
                lax.ppermute(head, axis, [((i + 1) % count, i) for i in range(ends)]),
            ],
            axis=dim,
        )
    return cells


def yarn_tables(yarn_scale, yarn_context):
    half_dim = HEAD_DIM // 2
    pair_index = jnp.arange(half_dim).astype(jnp.float32)
    base_rate = 10000.0 ** (-2.0 * pair_index / HEAD_DIM)
    factor = yarn_scale[0].astype(jnp.float32)
    context = yarn_context[0].astype(jnp.float32)
    turn_ratio = context * base_rate / (2.0 * math.pi)
    ramp_weight = jnp.clip((turn_ratio - 1.0) / 31.0, 0.0, 1.0)
    frequency = base_rate * ((1.0 - ramp_weight) / factor + ramp_weight)
    mscale = 0.1 * jnp.log(factor) + 1.0
    return (frequency, mscale)


def rotate(source, first_row, frequency, mscale):
    row_count, row_width = source.shape
    half_dim = HEAD_DIM // 2
    position = (first_row + jnp.arange(row_count)).astype(jnp.float32)
    angle_table = position[:, None] * frequency[None, :]
    cosine = jnp.cos(angle_table) * mscale
    sine_part = jnp.sin(angle_table) * mscale
    cosine = jnp.concatenate([cosine, cosine], axis=1)[:, None, :]
    sine_part = jnp.concatenate([sine_part, sine_part], axis=1)[:, None, :]
    grid = source.astype(jnp.float32).reshape(row_count, row_width // HEAD_DIM, HEAD_DIM)
    turned_half = jnp.concatenate([-grid[..., half_dim:], grid[..., :half_dim]], axis=2)
    turned = grid * cosine + turned_half * sine_part
    return turned.reshape(row_count, row_width).astype(jnp.bfloat16)


def block_attend(query_blocks, key_blocks, value_blocks, valid_slots):
    count_q, slot_count = (key_blocks.shape[0], key_blocks.shape[1])
    heads_here = query_blocks.shape[-1] // HEAD_DIM
    query_grid = query_blocks.reshape(count_q, BLOCK, heads_here, HEAD_DIM)
    key_grid = key_blocks.reshape(count_q, slot_count * BLOCK, heads_here, HEAD_DIM)
    value_grid = value_blocks.reshape(count_q, slot_count * BLOCK, heads_here, HEAD_DIM)
    scores = jnp.einsum(
        "bqhd,bshd->bhqs", query_grid, key_grid, preferred_element_type=jnp.float32
    ) * (1.0 / math.sqrt(HEAD_DIM))
    present = jnp.repeat(jnp.transpose(valid_slots, (0, 2, 1)), BLOCK, axis=2)[:, :, None, :]
    scores = jnp.where(present, scores, masked_score)
    peak = jnp.max(scores, axis=3, keepdims=True)
    expo = jnp.exp(scores - peak)
    total = jnp.sum(expo, axis=3)
    weights = expo.astype(jnp.bfloat16)
    mixture = jnp.einsum("bhqs,bshd->bqhd", weights, value_grid, preferred_element_type=jnp.float32)
    mixture = mixture / jnp.transpose(total, (0, 2, 1))[..., None]
    return mixture.reshape(count_q, BLOCK, heads_here * HEAD_DIM).astype(jnp.bfloat16)


def xor_perm(count, bit):
    return [(i, i ^ bit) for i in range(count)]


def tree_reduce(parts, merge, axis):
    count = lax.axis_size(axis)
    place = lax.axis_index(axis)
    bits = []
    bit = 1
    while bit < count:
        bits.append(bit)
        bit *= 2
    for bit in bits:
        upper = (place // bit) % 2
        halves = jax.tree.map(lambda x: x.reshape((2, x.shape[0] // 2) + x.shape[1:]), parts)
        keep = jax.tree.map(lambda h: lax.dynamic_index_in_dim(h, upper, 0, keepdims=False), halves)
        send = jax.tree.map(lambda h: lax.dynamic_index_in_dim(h, 1 - upper, 0, keepdims=False), halves)
        got = lax.ppermute(send, axis, xor_perm(count, bit))
        parts = merge(keep, got)
    for bit in reversed(bits):
        upper = (place // bit) % 2
        got = lax.ppermute(parts, axis, xor_perm(count, bit))

        def join(mine, theirs):
            pair = jnp.stack([mine, theirs])
            first = lax.dynamic_index_in_dim(pair, upper, 0, keepdims=False)
            second = lax.dynamic_index_in_dim(pair, 1 - upper, 0, keepdims=False)
            return jnp.concatenate([first, second], axis=0)

        parts = jax.tree.map(join, parts, got)
    return parts


def tree_scatter(parts, merge, axis):
    count = lax.axis_size(axis)
    place = lax.axis_index(axis)
    bit = 1
    while bit < count:
        upper = (place // bit) % 2
        halves = parts.reshape((2, parts.shape[0] // 2) + parts.shape[1:])
        keep = lax.dynamic_index_in_dim(halves, upper, 0, keepdims=False)
        send = lax.dynamic_index_in_dim(halves, 1 - upper, 0, keepdims=False)
        parts = merge(keep, lax.ppermute(send, axis, xor_perm(count, bit)))
        bit *= 2
    return parts


def bit_reversed(count):
    width = count.bit_length() - 1
    return [int(format(i, "0%db" % width)[::-1], 2) if width else 0 for i in range(count)]


def add_merge(a, b):
    return jax.tree.map(jnp.add, a, b)


def softmax_merge(a, b):
    width = a.shape[1] - 128
    heads = width // HEAD_DIM
    peak_a = a[:, width + heads : width + 2 * heads]
    peak_b = b[:, width + heads : width + 2 * heads]
    peak = jnp.maximum(peak_a, peak_b)
    scale_a = jnp.exp(peak_a - peak)
    scale_b = jnp.exp(peak_b - peak)
    rows = a.shape[0]
    mix = (
        a[:, :width].reshape(rows, heads, HEAD_DIM) * scale_a[..., None]
        + b[:, :width].reshape(rows, heads, HEAD_DIM) * scale_b[..., None]
    ).reshape(rows, width)
    total = a[:, width : width + heads] * scale_a + b[:, width : width + heads] * scale_b
    pad = jnp.zeros((rows, 128 - 2 * heads), a.dtype)
    return jnp.concatenate([mix, total, peak, pad], axis=1)


def head_partials(rows, out_weight):
    head_count = lax.axis_size("head")
    partial = lax.dot_general(
        out_weight, rows, (((0,), (1,)), ((), ())), preferred_element_type=jnp.float32
    ).astype(jnp.bfloat16)
    return partial.reshape(head_count, out_weight.shape[1] // head_count, rows.shape[0])


def sum_over_head(partial):
    gathered = lax.all_to_all(partial, "head", 0, 0, tiled=True)
    return jnp.sum(gathered.astype(jnp.float32), axis=0).T


def partial_attend(query_blocks, key_blocks, value_blocks, valid_slots):
    count_q, slot_count = (key_blocks.shape[0], key_blocks.shape[1])
    heads_here = query_blocks.shape[-1] // HEAD_DIM
    query_grid = query_blocks.reshape(count_q, BLOCK, heads_here, HEAD_DIM)
    key_grid = key_blocks.reshape(count_q, slot_count * BLOCK, heads_here, HEAD_DIM)
    value_grid = value_blocks.reshape(count_q, slot_count * BLOCK, heads_here, HEAD_DIM)
    scores = jnp.einsum(
        "bqhd,bshd->bhqs", query_grid, key_grid, preferred_element_type=jnp.float32
    ) * (1.0 / math.sqrt(HEAD_DIM))
    present = jnp.repeat(jnp.transpose(valid_slots, (0, 2, 1)), BLOCK, axis=2)[:, :, None, :]
    scores = jnp.where(present, scores, masked_score)
    peak = jnp.max(scores, axis=3)
    expo = jnp.exp(scores - peak[..., None])
    total = jnp.sum(expo, axis=3)
    mixture = jnp.einsum(
        "bhqs,bshd->bqhd", expo.astype(jnp.bfloat16), value_grid, preferred_element_type=jnp.float32
    )
    return mixture, total, peak


def merge_attend(first, second):
    mix_a, total_a, peak_a = first
    mix_b, total_b, peak_b = second
    peak = jnp.maximum(peak_a, peak_b)
    scale_a = jnp.exp(peak_a - peak)
    scale_b = jnp.exp(peak_b - peak)
    total = total_a * scale_a + total_b * scale_b
    mix = mix_a * jnp.transpose(scale_a, (0, 2, 1))[..., None] + mix_b * jnp.transpose(scale_b, (0, 2, 1))[..., None]
    mix = mix / jnp.transpose(total, (0, 2, 1))[..., None]
    count_q = mix.shape[0]
    return mix.reshape(count_q, BLOCK, -1).astype(jnp.bfloat16)


def on_device(
    queries,
    keys,
    values,
    out_weight,
    global_blocks,
    random_blocks,
    window_blocks,
    yarn_scale,
    yarn_context,
):
    tok_here, width_here = queries.shape
    heads_here = width_here // HEAD_DIM
    blocks_here = tok_here // BLOCK
    seq_count = lax.axis_size("seq")
    seq_place = lax.axis_index("seq")
    block_total = seq_count * blocks_here
    frequency, mscale = yarn_tables(yarn_scale, yarn_context)
    first_row = seq_place * tok_here
    query_rot = rotate(queries, first_row, frequency, mscale)
    key_rot = rotate(keys, first_row, frequency, mscale)
    pair_kv = jnp.stack([key_rot, values])
    local_blocks = pair_kv.reshape(2, blocks_here, BLOCK, width_here)

    def padded_block(index):
        if index < WMAX:
            return from_left[:, index]
        if index < WMAX + blocks_here:
            return local_blocks[:, index - WMAX]
        return from_right[:, index - WMAX - blocks_here]

    offsets = jnp.arange(-WMAX, WMAX + 1)
    window_ids = seq_place * blocks_here + jnp.arange(blocks_here)[:, None] + offsets[None, :]
    inside = (window_ids >= 0) & (window_ids < block_total)
    reach = jnp.abs(offsets)[None, :, None] <= window_blocks[None, None, :]
    window_valid = inside[:, :, None] & reach
    owner_global = global_blocks // blocks_here
    local_global = jnp.clip(global_blocks - seq_place * blocks_here, 0, blocks_here - 1)
    mine_global = owner_global == seq_place
    query_view = query_rot.reshape(blocks_here, BLOCK, width_here)
    key_view = key_rot.reshape(blocks_here, BLOCK, width_here)
    value_view = values.reshape(blocks_here, BLOCK, width_here)
    picked = jnp.stack([query_view[local_global], key_view[local_global], value_view[local_global]])
    masked = jnp.where(mine_global[None, :, None, None], picked, jnp.zeros_like(picked))
    shared = tree_reduce(masked.reshape(3 * GLOB * BLOCK, width_here), add_merge, "seq")
    shared = shared.reshape(3, GLOB, BLOCK, width_here)
    halo = WMAX * BLOCK
    seq_ends = seq_count - 1
    halo_kv, shared = lax.optimization_barrier((pair_kv, shared))
    from_left = lax.ppermute(
        halo_kv[:, tok_here - halo :], "seq", [(i, (i + 1) % seq_count) for i in range(seq_ends)]
    ).reshape(2, WMAX, BLOCK, width_here)
    from_right = lax.ppermute(
        halo_kv[:, :halo], "seq", [((i + 1) % seq_count, i) for i in range(seq_ends)]
    ).reshape(2, WMAX, BLOCK, width_here)
    slot_parts = [
        jnp.stack(
            [padded_block(block + offset_slot) for offset_slot in range(2 * WMAX + 1)], axis=1
        )
        for block in range(blocks_here)
    ]
    global_kv = jnp.broadcast_to(shared[1:3][:, None], (2, blocks_here, GLOB, BLOCK, width_here))
    near_kv = jnp.concatenate([jnp.stack(slot_parts, axis=1), global_kv], axis=2)
    near_valid = jnp.concatenate(
        [window_valid, jnp.ones((blocks_here, GLOB, heads_here), dtype=bool)], axis=1
    )
    global_query = shared[0]
    key_later = key_rot
    value_later = values
    global_query = global_query.reshape(GLOB, BLOCK, heads_here, HEAD_DIM)
    key_grid = key_later.reshape(tok_here, heads_here, HEAD_DIM)
    value_grid = value_later.reshape(tok_here, heads_here, HEAD_DIM)
    global_scores = jnp.einsum(
        "gqhd,khd->gqhk", global_query, key_grid, preferred_element_type=jnp.float32
    ) * (1.0 / math.sqrt(HEAD_DIM))
    local_peak = jnp.max(global_scores, axis=3)
    expo = jnp.exp(global_scores - local_peak[..., None])
    partial_total = jnp.sum(expo, axis=3)
    partial_mix = jnp.einsum(
        "gqhk,khd->gqhd", expo.astype(jnp.bfloat16), value_grid, preferred_element_type=jnp.float32
    )
    row_total = GLOB * BLOCK
    packed = jnp.concatenate(
        [
            partial_mix.reshape(row_total, width_here),
            partial_total.reshape(row_total, heads_here),
            local_peak.reshape(row_total, heads_here),
            jnp.zeros((row_total, 128 - 2 * heads_here), jnp.float32),
        ],
        axis=1,
    )
    slot_total = blocks_here * RAND
    capacity = (slot_total + seq_count - 1) // seq_count
    flat_ids = random_blocks.reshape(seq_count, slot_total)
    owners = flat_ids // blocks_here
    slot_order = jnp.arange(slot_total)
    same_owner = (owners[:, :, None] == owners[:, None, :]) & (
        slot_order[None, None, :] < slot_order[None, :, None]
    )
    ranks = jnp.sum(same_owner.astype(jnp.int32), axis=2)
    local_ids = flat_ids - owners * blocks_here
    wanted = (owners[:, None, :] == seq_place) & (
        ranks[:, None, :] == jnp.arange(capacity)[None, :, None]
    )
    send_local = jnp.sum(jnp.where(wanted, local_ids[:, None, :], 0), axis=2)
    kv_blocks = jnp.transpose(halo_kv.reshape(2, blocks_here, BLOCK, width_here), (1, 0, 2, 3))
    outgoing = kv_blocks[send_local]
    kv_rows = capacity * 2 * BLOCK
    rows_each = GLOB * BLOCK // seq_count
    outgoing = jnp.concatenate(
        [
            outgoing.reshape(seq_count, kv_rows, width_here),
            jnp.zeros((seq_count, rows_each, width_here), jnp.bfloat16),
        ],
        axis=1,
    )
    packed, from_left, from_right, outgoing = lax.optimization_barrier(
        (packed, from_left, from_right, outgoing)
    )
    slice_part = tree_scatter(packed, softmax_merge, "seq")
    slice_rows = (
        (slice_part[:, :width_here].reshape(-1, heads_here, HEAD_DIM) / slice_part[:, width_here : width_here + heads_here, None])
        .reshape(-1, width_here)
        .astype(jnp.bfloat16)
    )
    outgoing = lax.dynamic_update_slice(
        outgoing, jnp.broadcast_to(slice_rows[None], (seq_count, rows_each, width_here)), (0, kv_rows, 0)
    )
    incoming = lax.all_to_all(outgoing, "seq", split_axis=0, concat_axis=0, tiled=True)
    global_rows = incoming[:, kv_rows:][jnp.array(bit_reversed(seq_count))]
    my_owners = owners[seq_place]
    my_ranks = ranks[seq_place]
    sub = math.gcd(BLOCK, rows_each)
    pieces = incoming.reshape(seq_count, (kv_rows + rows_each) // sub, sub, width_here)
    first_piece = (my_ranks * (2 * BLOCK) // sub)[:, None] + jnp.arange(BLOCK // sub)[None, :]
    random_k = pieces[my_owners[:, None], first_piece].reshape(blocks_here, RAND, BLOCK, width_here)
    random_v = pieces[my_owners[:, None], first_piece + BLOCK // sub].reshape(
        blocks_here, RAND, BLOCK, width_here
    )
    random_kv = (random_k, random_v)
    near_part = partial_attend(query_view, near_kv[0], near_kv[1], near_valid)
    far_part = partial_attend(
        query_view, random_kv[0], random_kv[1], jnp.ones((blocks_here, RAND, heads_here), dtype=bool)
    )
    attended = merge_attend(near_part, far_part)
    global_out = global_rows.reshape(row_total, width_here)
    global_out = global_out.reshape(GLOB, BLOCK, width_here)
    block_index = jnp.arange(blocks_here)
    for global_slot in range(GLOB):
        hit = mine_global[global_slot] & (block_index == local_global[global_slot])
        attended = jnp.where(hit[:, None, None], global_out[global_slot][None], attended)
    mixed = sum_over_head(head_partials(attended.reshape(tok_here, width_here), out_weight))
    return mixed.astype(jnp.bfloat16)


def solution(mesh):
    in_specs = (
        P("seq", "head"),
        P("seq", "head"),
        P("seq", "head"),
        P("head", None),
        P(),
        P(),
        P("head"),
        P(),
        P(),
    )
    out_specs = P("seq", "head")
    return jax.shard_map(
        on_device, mesh=mesh, in_specs=in_specs, out_specs=out_specs, check_vma=False
    )
```

```python
import math

import jax
import jax.numpy as jnp
from jax import lax
from jax.sharding import PartitionSpec as P

HEAD_DIM = 128
BLOCK = 64
GLOB = 2
RAND = 3
WMAX = 2


masked_score = -1e30


def padded_2(cells, sides, width):
    for axis, dim in sides:
        count = lax.axis_size(axis)
        ends = count - 1
        head = lax.slice_in_dim(cells, 0, width, axis=dim)
        tail = lax.slice_in_dim(cells, cells.shape[dim] - width, cells.shape[dim], axis=dim)
        cells = jnp.concatenate(
            [
                lax.ppermute(tail, axis, [(i, (i + 1) % count) for i in range(ends)]),
                cells,
                lax.ppermute(head, axis, [((i + 1) % count, i) for i in range(ends)]),
            ],
            axis=dim,
        )
    return cells


def yarn_tables(yarn_scale, yarn_context):
    half_dim = HEAD_DIM // 2
    pair_index = jnp.arange(half_dim).astype(jnp.float32)
    base_rate = 10000.0 ** (-2.0 * pair_index / HEAD_DIM)
    factor = yarn_scale[0].astype(jnp.float32)
    context = yarn_context[0].astype(jnp.float32)
    turn_ratio = context * base_rate / (2.0 * math.pi)
    ramp_weight = jnp.clip((turn_ratio - 1.0) / 31.0, 0.0, 1.0)
    frequency = base_rate * ((1.0 - ramp_weight) / factor + ramp_weight)
    mscale = 0.1 * jnp.log(factor) + 1.0
    return (frequency, mscale)


def rotate(source, first_row, frequency, mscale):
    row_count, row_width = source.shape
    half_dim = HEAD_DIM // 2
    position = (first_row + jnp.arange(row_count)).astype(jnp.float32)
    angle_table = position[:, None] * frequency[None, :]
    cosine = jnp.cos(angle_table) * mscale
    sine_part = jnp.sin(angle_table) * mscale
    cosine = jnp.concatenate([cosine, cosine], axis=1)[:, None, :]
    sine_part = jnp.concatenate([sine_part, sine_part], axis=1)[:, None, :]
    grid = source.astype(jnp.float32).reshape(row_count, row_width // HEAD_DIM, HEAD_DIM)
    turned_half = jnp.concatenate([-grid[..., half_dim:], grid[..., :half_dim]], axis=2)
    turned = grid * cosine + turned_half * sine_part
    return turned.reshape(row_count, row_width).astype(jnp.bfloat16)


def block_attend(query_blocks, key_blocks, value_blocks, valid_slots):
    count_q, slot_count = (key_blocks.shape[0], key_blocks.shape[1])
    heads_here = query_blocks.shape[-1] // HEAD_DIM
    query_grid = query_blocks.reshape(count_q, BLOCK, heads_here, HEAD_DIM)
    key_grid = key_blocks.reshape(count_q, slot_count * BLOCK, heads_here, HEAD_DIM)
    value_grid = value_blocks.reshape(count_q, slot_count * BLOCK, heads_here, HEAD_DIM)
    scores = jnp.einsum(
        "bqhd,bshd->bhqs", query_grid, key_grid, preferred_element_type=jnp.float32
    ) * (1.0 / math.sqrt(HEAD_DIM))
    present = jnp.repeat(jnp.transpose(valid_slots, (0, 2, 1)), BLOCK, axis=2)[:, :, None, :]
    scores = jnp.where(present, scores, masked_score)
    peak = jnp.max(scores, axis=3, keepdims=True)
    expo = jnp.exp(scores - peak)
    total = jnp.sum(expo, axis=3)
    weights = expo.astype(jnp.bfloat16)
    mixture = jnp.einsum("bhqs,bshd->bqhd", weights, value_grid, preferred_element_type=jnp.float32)
    mixture = mixture / jnp.transpose(total, (0, 2, 1))[..., None]
    return mixture.reshape(count_q, BLOCK, heads_here * HEAD_DIM).astype(jnp.bfloat16)


def xor_perm(count, bit):
    return [(i, i ^ bit) for i in range(count)]


def tree_reduce(parts, merge, axis):
    count = lax.axis_size(axis)
    place = lax.axis_index(axis)
    bits = []
    bit = 1
    while bit < count:
        bits.append(bit)
        bit *= 2
    for bit in bits:
        upper = (place // bit) % 2
        halves = jax.tree.map(lambda x: x.reshape((2, x.shape[0] // 2) + x.shape[1:]), parts)
        keep = jax.tree.map(lambda h: lax.dynamic_index_in_dim(h, upper, 0, keepdims=False), halves)
        send = jax.tree.map(lambda h: lax.dynamic_index_in_dim(h, 1 - upper, 0, keepdims=False), halves)
        got = lax.ppermute(send, axis, xor_perm(count, bit))
        parts = merge(keep, got)
    for bit in reversed(bits):
        upper = (place // bit) % 2
        got = lax.ppermute(parts, axis, xor_perm(count, bit))

        def join(mine, theirs):
            pair = jnp.stack([mine, theirs])
            first = lax.dynamic_index_in_dim(pair, upper, 0, keepdims=False)
            second = lax.dynamic_index_in_dim(pair, 1 - upper, 0, keepdims=False)
            return jnp.concatenate([first, second], axis=0)

        parts = jax.tree.map(join, parts, got)
    return parts


def tree_scatter(parts, merge, axis):
    count = lax.axis_size(axis)
    place = lax.axis_index(axis)
    bit = 1
    while bit < count:
        upper = (place // bit) % 2
        halves = parts.reshape((2, parts.shape[0] // 2) + parts.shape[1:])
        keep = lax.dynamic_index_in_dim(halves, upper, 0, keepdims=False)
        send = lax.dynamic_index_in_dim(halves, 1 - upper, 0, keepdims=False)
        parts = merge(keep, lax.ppermute(send, axis, xor_perm(count, bit)))
        bit *= 2
    return parts


def bit_reversed(count):
    width = count.bit_length() - 1
    return [int(format(i, "0%db" % width)[::-1], 2) if width else 0 for i in range(count)]


def add_merge(a, b):
    return jax.tree.map(jnp.add, a, b)


def softmax_merge(a, b):
    width = a.shape[1] - 128
    heads = width // HEAD_DIM
    peak_a = a[:, width + heads : width + 2 * heads]
    peak_b = b[:, width + heads : width + 2 * heads]
    peak = jnp.maximum(peak_a, peak_b)
    scale_a = jnp.exp(peak_a - peak)
    scale_b = jnp.exp(peak_b - peak)
    rows = a.shape[0]
    mix = (
        a[:, :width].reshape(rows, heads, HEAD_DIM) * scale_a[..., None]
        + b[:, :width].reshape(rows, heads, HEAD_DIM) * scale_b[..., None]
    ).reshape(rows, width)
    total = a[:, width : width + heads] * scale_a + b[:, width : width + heads] * scale_b
    pad = jnp.zeros((rows, 128 - 2 * heads), a.dtype)
    return jnp.concatenate([mix, total, peak, pad], axis=1)


def head_partials(rows, out_weight):
    head_count = lax.axis_size("head")
    partial = lax.dot_general(
        out_weight, rows, (((0,), (1,)), ((), ())), preferred_element_type=jnp.float32
    ).astype(jnp.bfloat16)
    return partial.reshape(head_count, out_weight.shape[1] // head_count, rows.shape[0])


def sum_over_head(partial):
    gathered = lax.all_to_all(partial, "head", 0, 0, tiled=True)
    return jnp.sum(gathered.astype(jnp.float32), axis=0).T


def partial_attend(query_blocks, key_blocks, value_blocks, valid_slots):
    count_q, slot_count = (key_blocks.shape[0], key_blocks.shape[1])
    heads_here = query_blocks.shape[-1] // HEAD_DIM
    query_grid = query_blocks.reshape(count_q, BLOCK, heads_here, HEAD_DIM)
    key_grid = key_blocks.reshape(count_q, slot_count * BLOCK, heads_here, HEAD_DIM)
    value_grid = value_blocks.reshape(count_q, slot_count * BLOCK, heads_here, HEAD_DIM)
    scores = jnp.einsum(
        "bqhd,bshd->bhqs", query_grid, key_grid, preferred_element_type=jnp.float32
    ) * (1.0 / math.sqrt(HEAD_DIM))
    present = jnp.repeat(jnp.transpose(valid_slots, (0, 2, 1)), BLOCK, axis=2)[:, :, None, :]
    scores = jnp.where(present, scores, masked_score)
    peak = jnp.max(scores, axis=3)
    expo = jnp.exp(scores - peak[..., None])
    total = jnp.sum(expo, axis=3)
    mixture = jnp.einsum(
        "bhqs,bshd->bqhd", expo.astype(jnp.bfloat16), value_grid, preferred_element_type=jnp.float32
    )
    return mixture, total, peak


def merge_attend(first, second):
    mix_a, total_a, peak_a = first
    mix_b, total_b, peak_b = second
    peak = jnp.maximum(peak_a, peak_b)
    scale_a = jnp.exp(peak_a - peak)
    scale_b = jnp.exp(peak_b - peak)
    total = total_a * scale_a + total_b * scale_b
    mix = mix_a * jnp.transpose(scale_a, (0, 2, 1))[..., None] + mix_b * jnp.transpose(scale_b, (0, 2, 1))[..., None]
    mix = mix / jnp.transpose(total, (0, 2, 1))[..., None]
    count_q = mix.shape[0]
    return mix.reshape(count_q, BLOCK, -1).astype(jnp.bfloat16)


def on_device(
    queries,
    keys,
    values,
    out_weight,
    global_blocks,
    random_blocks,
    window_blocks,
    yarn_scale,
    yarn_context,
):
    tok_here, width_here = queries.shape
    heads_here = width_here // HEAD_DIM
    blocks_here = tok_here // BLOCK
    seq_count = lax.axis_size("seq")
    seq_place = lax.axis_index("seq")
    block_total = seq_count * blocks_here
    frequency, mscale = yarn_tables(yarn_scale, yarn_context)
    first_row = seq_place * tok_here
    query_rot = rotate(queries, first_row, frequency, mscale)
    key_rot = rotate(keys, first_row, frequency, mscale)
    pair_kv = jnp.stack([key_rot, values])
    local_blocks = pair_kv.reshape(2, blocks_here, BLOCK, width_here)

    def padded_block(index):
        if index < WMAX:
            return from_left[:, index]
        if index < WMAX + blocks_here:
            return local_blocks[:, index - WMAX]
        return from_right[:, index - WMAX - blocks_here]

    offsets = jnp.arange(-WMAX, WMAX + 1)
    window_ids = seq_place * blocks_here + jnp.arange(blocks_here)[:, None] + offsets[None, :]
    inside = (window_ids >= 0) & (window_ids < block_total)
    reach = jnp.abs(offsets)[None, :, None] <= window_blocks[None, None, :]
    window_valid = inside[:, :, None] & reach
    owner_global = global_blocks // blocks_here
    local_global = jnp.clip(global_blocks - seq_place * blocks_here, 0, blocks_here - 1)
    mine_global = owner_global == seq_place
    query_view = query_rot.reshape(blocks_here, BLOCK, width_here)
    key_view = key_rot.reshape(blocks_here, BLOCK, width_here)
    value_view = values.reshape(blocks_here, BLOCK, width_here)
    picked = jnp.stack([query_view[local_global], key_view[local_global], value_view[local_global]])
    masked = jnp.where(mine_global[None, :, None, None], picked, jnp.zeros_like(picked))
    shared = tree_reduce(masked.reshape(3 * GLOB * BLOCK, width_here), add_merge, "seq")
    shared = shared.reshape(3, GLOB, BLOCK, width_here)
    halo = WMAX * BLOCK
    seq_ends = seq_count - 1
    halo_kv, shared = lax.optimization_barrier((pair_kv, shared))
    from_left = lax.ppermute(
        halo_kv[:, tok_here - halo :], "seq", [(i, (i + 1) % seq_count) for i in range(seq_ends)]
    ).reshape(2, WMAX, BLOCK, width_here)
    from_right = lax.ppermute(
        halo_kv[:, :halo], "seq", [((i + 1) % seq_count, i) for i in range(seq_ends)]
    ).reshape(2, WMAX, BLOCK, width_here)
    slot_parts = [
        jnp.stack(
            [padded_block(block + offset_slot) for offset_slot in range(2 * WMAX + 1)], axis=1
        )
        for block in range(blocks_here)
    ]
    global_kv = jnp.broadcast_to(shared[1:3][:, None], (2, blocks_here, GLOB, BLOCK, width_here))
    near_kv = jnp.concatenate([jnp.stack(slot_parts, axis=1), global_kv], axis=2)
    near_valid = jnp.concatenate(
        [window_valid, jnp.ones((blocks_here, GLOB, heads_here), dtype=bool)], axis=1
    )
    global_query = shared[0]
    key_later = key_rot
    value_later = values
    global_query = global_query.reshape(GLOB, BLOCK, heads_here, HEAD_DIM)
    key_grid = key_later.reshape(tok_here, heads_here, HEAD_DIM)
    value_grid = value_later.reshape(tok_here, heads_here, HEAD_DIM)
    global_scores = jnp.einsum(
        "gqhd,khd->gqhk", global_query, key_grid, preferred_element_type=jnp.float32
    ) * (1.0 / math.sqrt(HEAD_DIM))
    local_peak = jnp.max(global_scores, axis=3)
    expo = jnp.exp(global_scores - local_peak[..., None])
    partial_total = jnp.sum(expo, axis=3)
    partial_mix = jnp.einsum(
        "gqhk,khd->gqhd", expo.astype(jnp.bfloat16), value_grid, preferred_element_type=jnp.float32
    )
    row_total = GLOB * BLOCK
    packed = jnp.concatenate(
        [
            partial_mix.reshape(row_total, width_here),
            partial_total.reshape(row_total, heads_here),
            local_peak.reshape(row_total, heads_here),
            jnp.zeros((row_total, 128 - 2 * heads_here), jnp.float32),
        ],
        axis=1,
    )
    slot_total = blocks_here * RAND
    capacity = (slot_total + seq_count - 1) // seq_count
    flat_ids = random_blocks.reshape(seq_count, slot_total)
    owners = flat_ids // blocks_here
    slot_order = jnp.arange(slot_total)
    same_owner = (owners[:, :, None] == owners[:, None, :]) & (
        slot_order[None, None, :] < slot_order[None, :, None]
    )
    ranks = jnp.sum(same_owner.astype(jnp.int32), axis=2)
    local_ids = flat_ids - owners * blocks_here
    wanted = (owners[:, None, :] == seq_place) & (
        ranks[:, None, :] == jnp.arange(capacity)[None, :, None]
    )
    send_local = jnp.sum(jnp.where(wanted, local_ids[:, None, :], 0), axis=2)
    kv_blocks = jnp.transpose(halo_kv.reshape(2, blocks_here, BLOCK, width_here), (1, 0, 2, 3))
    outgoing = kv_blocks[send_local]
    kv_rows = capacity * 2 * BLOCK
    rows_each = GLOB * BLOCK // seq_count
    outgoing = jnp.concatenate(
        [
            outgoing.reshape(seq_count, kv_rows, width_here),
            jnp.zeros((seq_count, rows_each, width_here), jnp.bfloat16),
        ],
        axis=1,
    )
    packed, from_left, from_right, outgoing = lax.optimization_barrier(
        (packed, from_left, from_right, outgoing)
    )
    slice_part = tree_scatter(packed, softmax_merge, "seq")
    slice_rows = (
        (slice_part[:, :width_here].reshape(-1, heads_here, HEAD_DIM) / slice_part[:, width_here : width_here + heads_here, None])
        .reshape(-1, width_here)
        .astype(jnp.bfloat16)
    )
    outgoing = lax.dynamic_update_slice(
        outgoing, jnp.broadcast_to(slice_rows[None], (seq_count, rows_each, width_here)), (0, kv_rows, 0)
    )
    incoming = lax.all_to_all(outgoing, "seq", split_axis=0, concat_axis=0, tiled=True)
    global_rows = incoming[:, kv_rows:][jnp.array(bit_reversed(seq_count))]
    my_owners = owners[seq_place]
    my_ranks = ranks[seq_place]
    sub = math.gcd(BLOCK, rows_each)
    pieces = incoming.reshape(seq_count, (kv_rows + rows_each) // sub, sub, width_here)
    both_pieces = (my_ranks * (2 * BLOCK) // sub)[:, None] + jnp.arange(2 * BLOCK // sub)[None, :]
    random_both = pieces[my_owners[:, None], both_pieces].reshape(blocks_here, RAND, 2, BLOCK, width_here)
    random_k = random_both[:, :, 0]
    random_v = random_both[:, :, 1]
    random_kv = (random_k, random_v)
    near_part = partial_attend(query_view, near_kv[0], near_kv[1], near_valid)
    far_part = partial_attend(
        query_view, random_kv[0], random_kv[1], jnp.ones((blocks_here, RAND, heads_here), dtype=bool)
    )
    attended = merge_attend(near_part, far_part)
    global_out = global_rows.reshape(row_total, width_here)
    global_out = global_out.reshape(GLOB, BLOCK, width_here)
    block_index = jnp.arange(blocks_here)
    for global_slot in range(GLOB):
        hit = mine_global[global_slot] & (block_index == local_global[global_slot])
        attended = jnp.where(hit[:, None, None], global_out[global_slot][None], attended)
    mixed = sum_over_head(head_partials(attended.reshape(tok_here, width_here), out_weight))
    return mixed.astype(jnp.bfloat16)


def solution(mesh):
    in_specs = (
        P("seq", "head"),
        P("seq", "head"),
        P("seq", "head"),
        P("head", None),
        P(),
        P(),
        P("head"),
        P(),
        P(),
    )
    out_specs = P("seq", "head")
    return jax.shard_map(
        on_device, mesh=mesh, in_specs=in_specs, out_specs=out_specs, check_vma=False
    )
```
